32 devices in a mesh: ctx: 32 (over z, y, x, core), tp: 1.
Axes of the slice: x: 2, y: 2, z: 4, core: 2. Of those that a mesh axis runs over, the one named last changes fastest.
Arguments:
- x_in: bfloat16 [8192, 8192], P('ctx', 'tp'), may hold values from -6 to 6
- gate_z: bfloat16 [8192, 8192], P('ctx', 'tp'), may hold values from -6 to 6
- bc_in: bfloat16 [8192, 256], P('ctx'), may hold values from -6 to 6
- dt_raw: float32 [128, 8192], P('tp', 'ctx'), may hold values from -2.5 to 2.5
- dt_bias: float32 [128], P('tp')
- a_rate: float32 [128], P('tp')
- skip_d: float32 [128], P('tp'), may hold values from 0.5 to 1.5
- conv_x_w: bfloat16 [4, 8192], P(None, 'tp'), may hold values from -3 to 3
- conv_x_b: bfloat16 [8192], P('tp'), may hold values from -3 to 3
- conv_bc_w: bfloat16 [4, 256], replicated, may hold values from -3 to 3
- conv_bc_b: bfloat16 [256], replicated, may hold values from -3 to 3
- norm_gain: bfloat16 [8192], P('tp'), may hold values from 0.5 to 1.5
- segment_ids: int32 [8192], P('ctx'), may hold values from 0 to 7, never falling along the last dimension, each value on 1 to 2048 neighbouring positions
Outputs:
- y_out: bfloat16 [8192, 8192], P('ctx', 'tp')
The draws below stay inside these ranges and needn't reach their ends.
Inputs may be any that keep to these rules, and one draw needn't show every extreme that they name: `segment_ids`: segment numbers never fall along the tokens and every number is used; a file holds at most a quarter of 8192 tokens, and one holds exactly that many.
All inputs are finite; a program needn't handle non-finite values.
Results may differ from the reference program's by a relative error of at most 0.0034.
Values may be sent and summed in bfloat16 or wider, within the bound.
No kernel may reach another device: no remote copies, remote signals or barrier semaphores. Data moves between devices by JAX's collectives and lax.ppermute only.
A program may use at most 256 MiB of HBM per device.

```python
import math
import jax
import jax.numpy as jnp
import numpy as np
from jax import lax

HEADS = 128
HEAD_DIM = 64
STATE = 128
GROUP = 256
CONV = 4
TOKENS = 8192
INNER = 8192
N_CTX = 32


def head_kinds(key):
    share = 0.5
    return jax.random.bernoulli(jax.random.fold_in(key, 7), share, (HEADS,))


def draw_dt_bias(key, part):
    quick = head_kinds(key)
    quick_step = jax.random.uniform(jax.random.fold_in(key, 11), (HEADS,), jnp.float32, 0.3, 0.7)
    jitter = jax.random.uniform(jax.random.fold_in(key, 13), (HEADS,), jnp.float32, -0.35, 0.35)
    slow_step = 2.0 / math.sqrt(TOKENS) * jnp.exp(jitter)
    target = jnp.where(quick, quick_step, slow_step)
    return jnp.log(jnp.expm1(target)).astype(jnp.float32)


def draw_a_rate(key, part):
    quick = head_kinds(key)
    quick_rate = jnp.exp(jax.random.uniform(jax.random.fold_in(key, 17), (HEADS,), jnp.float32, math.log(0.04), math.log(0.1)))
    jitter = jax.random.uniform(jax.random.fold_in(key, 19), (HEADS,), jnp.float32, -0.7, 0.7)
    slow_rate = 0.15 / math.sqrt(TOKENS) * jnp.exp(jitter)
    return jnp.where(quick, quick_rate, slow_rate).astype(jnp.float32)


def steps_of(own_key, dims, shards, smallest, top_value):
    def one(position, shards_of):
        steps = jax.random.uniform(jax.random.fold_in(jax.random.fold_in(own_key, 6), position), (shards_of,), jnp.float32, smallest / len(shards), top_value / len(shards))
        return jnp.repeat(jnp.exp(steps), dims[position] // shards_of).reshape((-1,) + (1,) * (len(dims) - position - 1))

    gain = one(*shards[0])
    for cut in shards[1:]:
        gain = gain * one(*cut)
    return gain


def profile(count, total, bound, slope):
    weights = [(1 << 20) // math.isqrt(grade ** slope) + 1 for grade in range(2, count + 1)]
    rest, counts = total - bound - (count - 1), [1] * (count - 1)
    while rest > 0:
        candidates = [i for i in range(count - 1) if counts[i] < bound]
        pool, remaining = sum([weights[i] for i in candidates]), rest
        for i in candidates:
            extra = min(bound - counts[i], max(1, remaining * weights[i] // pool), rest)
            counts[i] = counts[i] + extra
            rest = rest - extra
    return np.array([bound] + counts)


def uneven(own_key, number_of, total, limit, lean):
    if number_of == 2:
        one = jax.random.randint(own_key, (), max(1, total - limit), min(limit, total - 1) + 1)
        return jnp.stack([one, total - one])
    sizes = jnp.asarray(profile(number_of, total, limit, lean), jnp.int32)
    pairs = (number_of - 1) // 2
    giver, taker = sizes[1:1 + 2 * pairs:2], sizes[2:2 + 2 * pairs:2]
    slack = jnp.minimum(giver - 1, limit - taker)
    shifted = jax.random.randint(jax.random.fold_in(own_key, 1), (pairs,), 0, 1 << 20) % (slack + 1)
    sizes = sizes.at[1:1 + 2 * pairs:2].set(giver - shifted).at[2:2 + 2 * pairs:2].set(taker + shifted)
    return sizes[jax.random.permutation(jax.random.fold_in(own_key, 2), number_of)]


def noise(stream_key, dims, width, most, cuts=(), dtype=jnp.bfloat16):
    factor_of = steps_of(stream_key, dims, cuts, -0.22, 0.18) if cuts else 1.0
    result = jax.random.normal(stream_key, dims, jnp.float32) * width * factor_of
    return jnp.minimum(jnp.maximum(result, -most), most).astype(dtype)


def setup_inputs(seed: int = 0) -> dict:
    keys = jax.random.split(jax.random.key(seed), 14)
    return {
        "x_in": noise(keys[0], (TOKENS, INNER), 1.0, 6.0, ((0, 32),)),
        "gate_z": noise(keys[1], (TOKENS, INNER), 1.0, 6.0, ((0, 32),)),
        "bc_in": noise(keys[2], (TOKENS, 2 * STATE), 1.0, 6.0, ((0, 32),)),
        "dt_raw": noise(keys[3], (HEADS, TOKENS), 0.5, 2.5, ((1, 32),), jnp.float32),
        "dt_bias": draw_dt_bias(jax.random.fold_in(keys[13], 71), 0),
        "a_rate": draw_a_rate(jax.random.fold_in(keys[13], 71), 0),
        "skip_d": jnp.clip(jax.random.uniform(keys[6], (HEADS,), jnp.float32, 0.5, 1.5), 0.5, 1.5),
        "conv_x_w": noise(keys[7], (CONV, INNER), CONV ** -0.5, 3.0),
        "conv_x_b": noise(keys[8], (INNER,), 0.5, 3.0),
        "conv_bc_w": noise(keys[9], (CONV, 2 * STATE), CONV ** -0.5, 3.0),
        "conv_bc_b": noise(keys[10], (2 * STATE,), 0.5, 3.0),
        "norm_gain": jnp.clip(1.0 + 0.1 * jax.random.normal(keys[11], (INNER,), jnp.float32), 0.5, 1.5).astype(jnp.bfloat16),
        "segment_ids": jnp.searchsorted(jnp.cumsum(uneven(keys[12], max(4, N_CTX // 4), TOKENS, TOKENS // 4, 2)), jnp.arange(TOKENS), side="right").astype(jnp.int32),
    }


epsilon = 1e-05

def causal_conv(rim_vals, values, rim_segment, segment, weight, offset_bias):
    extended = jnp.concatenate([rim_vals, values], axis=0)
    ext_segment = jnp.concatenate([rim_segment, segment], axis=0)
    length = values.shape[0]
    summed = jnp.zeros(values.shape, jnp.float32) + offset_bias.astype(jnp.float32)
    for offset in range(CONV):
        visible = (ext_segment[offset:offset + length] == segment).astype(jnp.float32)
        summed = summed + weight[offset].astype(jnp.float32) * extended[offset:offset + length].astype(jnp.float32) * visible[:, None]
    return jax.nn.silu(summed).astype(jnp.bfloat16)

def mixing_part(x_group, b_group, c_group, step_size, cum_decay, segment):
    places = jnp.arange(segment.shape[0])
    visible = jnp.logical_and(places[:, None] >= places[None, :], segment[:, None] == segment[None, :])
    scores = jnp.einsum('in,jn->ij', c_group.astype(jnp.float32), b_group.astype(jnp.float32))
    exponent = jnp.where(visible[None], cum_decay[:, :, None] - cum_decay[:, None, :], -jnp.inf)
    mixing = (scores[None] * jnp.exp(exponent) * step_size[:, None, :]).astype(jnp.bfloat16)
    mixing = lax.optimization_barrier(mixing)
    return jnp.einsum('hij,jhp->ihp', mixing.astype(jnp.float32), x_group.astype(jnp.float32))

def state_part(x_group, b_group, step_size, cum_decay, segment, seg_before):
    closing = cum_decay[:, -1:]
    tail_mask = (segment == segment[-1]).astype(jnp.float32)
    factor = jnp.exp(closing - cum_decay) * step_size * tail_mask[None]
    weighted = (b_group.astype(jnp.float32)[None] * factor[:, :, None]).astype(jnp.bfloat16)
    weighted = lax.optimization_barrier(weighted)
    block_state = jnp.einsum('hjn,jhp->hpn', weighted.astype(jnp.float32), x_group.astype(jnp.float32))
    transmit = jnp.exp(cum_decay[:, -1]) * (segment[-1] == seg_before).astype(jnp.float32)
    return (block_state, transmit)

def entry_part(c_group, entering, cum_decay, segment, seg_before):
    packed = lax.optimization_barrier(entering.astype(jnp.bfloat16))
    reach = jnp.exp(cum_decay) * (segment == seg_before).astype(jnp.float32)[None]
    product = jnp.einsum('in,hpn->ihp', c_group.astype(jnp.float32), packed.astype(jnp.float32))
    return product * jnp.transpose(reach)[:, :, None]

def finish(y_total, gate_rows, norm_gain):
    gated = y_total * jax.nn.silu(gate_rows.astype(jnp.float32))
    mean_sq = lax.optimization_barrier(jnp.sum(gated * gated, axis=1, keepdims=True)) / INNER
    return (gated * lax.rsqrt(mean_sq + epsilon) * norm_gain.astype(jnp.float32)).astype(jnp.bfloat16)

def reference(x_in, gate_z, bc_in, dt_raw, dt_bias, a_rate, skip_d, conv_x_w, conv_x_b, conv_bc_w, conv_bc_b, norm_gain, segment_ids):
    block_count = TOKENS // GROUP
    step_size = jax.nn.softplus(dt_raw + dt_bias[:, None])
    log_decay = -step_size * a_rate[:, None]
    step_blocks = jnp.transpose(step_size.reshape(HEADS, block_count, GROUP), (1, 0, 2))
    decay_blocks = jnp.transpose(log_decay.reshape(HEADS, block_count, GROUP), (1, 0, 2))
    inputs = (x_in.reshape(block_count, GROUP, INNER), gate_z.reshape(block_count, GROUP, INNER), bc_in.reshape(block_count, GROUP, 2 * STATE), step_blocks, decay_blocks, segment_ids.reshape(block_count, GROUP))
    start = (jnp.zeros((HEADS, HEAD_DIM, STATE), jnp.float32), jnp.zeros((CONV - 1, INNER), jnp.bfloat16), jnp.zeros((CONV - 1, 2 * STATE), jnp.bfloat16), jnp.full((CONV - 1,), -1, jnp.int32))

    def advance(carried, block_data):
        state_now, rim_x, rim_bc, rim_segment = carried
        x_block, gate_block, bc_block, step_here, decay_here, segment = block_data
        x_conv = causal_conv(rim_x, x_block, rim_segment, segment, conv_x_w, conv_x_b)
        bc_conv = causal_conv(rim_bc, bc_block, rim_segment, segment, conv_bc_w, conv_bc_b)
        b_group = bc_conv[:, :STATE]
        c_group = bc_conv[:, STATE:]
        cum_decay = jnp.cumsum(decay_here, axis=1)
        x_group = x_conv.reshape(GROUP, HEADS, HEAD_DIM)
        seg_before = rim_segment[CONV - 2]
        y_intra = mixing_part(x_group, b_group, c_group, step_here, cum_decay, segment)
        y_state = entry_part(c_group, state_now, cum_decay, segment, seg_before)
        y_total = y_intra + y_state + skip_d[None, :, None] * x_group.astype(jnp.float32)
        normed = finish(y_total.reshape(GROUP, INNER), gate_block, norm_gain)
        block_state, transmit = state_part(x_group, b_group, step_here, cum_decay, segment, seg_before)
        state_next = transmit[:, None, None] * state_now + block_state
        tail = GROUP - (CONV - 1)
        return ((state_next, x_block[tail:], bc_block[tail:], segment[tail:]), normed)
    finals, outputs = lax.scan(advance, start, inputs)
    return outputs.reshape(TOKENS, INNER)
```

```python
import functools

import jax
import jax.numpy as jnp
from jax import lax
from jax.sharding import PartitionSpec as P

HEAD_DIM = 64
STATE = 128
GROUP = 256
CONV = 4
INNER = 8192


epsilon = 1e-05


def passed_along(value, axis, steps):
    count = lax.axis_size(axis)
    leading, last = (max(0, -steps), min(count, count - steps))
    return lax.ppermute(value, axis, [(source, source + steps) for source in range(leading, last)])


def causal_conv(rim_vals, values, rim_segment, segment, weight, offset_bias):
    extended = jnp.concatenate([rim_vals, values], axis=0)
    ext_segment = jnp.concatenate([rim_segment, segment], axis=0)
    length = values.shape[0]
    summed = jnp.zeros(values.shape, jnp.float32) + offset_bias.astype(jnp.float32)
    for offset in range(CONV):
        visible = (ext_segment[offset : offset + length] == segment).astype(jnp.float32)
        summed = (
            summed
            + weight[offset].astype(jnp.float32)
            * extended[offset : offset + length].astype(jnp.float32)
            * visible[:, None]
        )
    return jax.nn.silu(summed).astype(jnp.bfloat16)


def mixing_part(x_group, b_group, c_group, step_size, cum_decay, segment):
    places = jnp.arange(segment.shape[0])
    visible = jnp.logical_and(
        places[:, None] >= places[None, :], segment[:, None] == segment[None, :]
    )
    scores = jnp.einsum("in,jn->ij", c_group, b_group, preferred_element_type=jnp.float32)
    exponent = jnp.where(visible[None], cum_decay[:, :, None] - cum_decay[:, None, :], -jnp.inf)
    mixing = (scores[None] * jnp.exp(exponent) * step_size[:, None, :]).astype(jnp.bfloat16)
    return jnp.einsum("hij,jhp->ihp", mixing, x_group, preferred_element_type=jnp.float32)


def state_part(x_group, b_group, step_size, cum_decay, segment, seg_before):
    closing = cum_decay[:, -1:]
    tail_mask = (segment == segment[-1]).astype(jnp.float32)
    factor = jnp.exp(closing - cum_decay) * step_size * tail_mask[None]
    weighted = (b_group.astype(jnp.float32)[None] * factor[:, :, None]).astype(jnp.bfloat16)
    block_state = jnp.einsum("hjn,jhp->hpn", weighted, x_group, preferred_element_type=jnp.float32)
    transmit = jnp.exp(cum_decay[:, -1]) * (segment[-1] == seg_before).astype(jnp.float32)
    return (block_state, transmit)


def entry_part(c_group, entering, cum_decay, segment, seg_before):
    packed = entering.astype(jnp.bfloat16)
    reach = jnp.exp(cum_decay) * (segment == seg_before).astype(jnp.float32)[None]
    product = jnp.einsum("in,hpn->ihp", c_group, packed, preferred_element_type=jnp.float32)
    return product * jnp.transpose(reach)[:, :, None]


def shifted(value, axis, steps, count):
    return lax.ppermute(value, axis, [(s, s + steps) for s in range(count - steps)])


def scan_rounds(carry, axis, stride, span, count):
    transmit, state = shifted(carry, axis, stride, count)
    covered = 1
    while covered < span - 1:
        far_t, far_s = shifted((transmit, state), axis, stride * covered, count)
        state = transmit[:, None, None] * far_s + state
        transmit = transmit * far_t
        covered *= 2
    return state


def device_entry(dev_transmit, dev_state, paired):
    count = lax.axis_size("ctx")
    if not paired:
        return scan_rounds((dev_transmit, dev_state), "ctx", 1, count, count)
    heads = dev_state.shape[0]
    half = heads // 2
    core = lax.axis_index("ctx") % 2
    swap = [(s, s ^ 1) for s in range(count)]
    own_lo = core * half
    give = lax.dynamic_slice_in_dim(dev_state, half - own_lo, half, 0)
    other_t, other_s = lax.ppermute((dev_transmit, give), "ctx", swap)
    mine_s = lax.dynamic_slice_in_dim(dev_state, own_lo, half, 0)
    mine_t = lax.dynamic_slice_in_dim(dev_transmit, own_lo, half, 0)
    peer_t = lax.dynamic_slice_in_dim(other_t, own_lo, half, 0)
    first = core == 0
    chip_s = jnp.where(first, peer_t[:, None, None] * mine_s + other_s, mine_t[:, None, None] * other_s + mine_s)
    chip_t = mine_t * peer_t
    entering = scan_rounds((chip_t, chip_s), "ctx", 2, count // 2, count)
    lead_t = jnp.where(first, mine_t, peer_t)
    lead_s = jnp.where(first, mine_s, other_s)
    second = lead_t[:, None, None] * entering + lead_s
    back = lax.ppermute(jnp.where(first, second, entering), "ctx", swap)
    mine = jnp.where(first, entering, second)
    low = jnp.where(first, mine, back)
    high = jnp.where(first, back, mine)
    return jnp.concatenate([low, high], axis=0)


def chain_states(block_states, transmits, paired):

    def advance(carried, item):
        passing, state_now = carried
        transmit, block_state = item
        return (
            (passing * transmit, transmit[:, None, None] * state_now + block_state),
            (passing, state_now),
        )

    start = (jnp.ones_like(transmits[0]), jnp.zeros_like(block_states[0]))
    finals, befores = lax.scan(advance, start, (transmits, block_states))
    entering_dev = device_entry(finals[0], finals[1], paired)
    return befores[0][:, :, None, None] * entering_dev[None] + befores[1]


def local(
    paired,
    x_in,
    gate_z,
    bc_in,
    dt_raw,
    dt_bias,
    a_rate,
    skip_d,
    conv_x_w,
    conv_x_b,
    conv_bc_w,
    conv_bc_b,
    norm_gain,
    segment_ids,
):
    tok_rows = x_in.shape[0]
    channels = x_in.shape[1]
    head_count = dt_raw.shape[0]
    block_count = tok_rows // GROUP
    rim_rows = CONV - 1
    rim_x, rim_bc, rim_mark = passed_along(
        (
            x_in[tok_rows - rim_rows :],
            bc_in[tok_rows - rim_rows :],
            segment_ids[tok_rows - rim_rows :].astype(jnp.bfloat16),
        ),
        "ctx",
        1,
    )
    rim_segment = rim_mark.astype(jnp.int32)
    x_conv = causal_conv(rim_x, x_in, rim_segment, segment_ids, conv_x_w, conv_x_b)
    bc_conv = causal_conv(rim_bc, bc_in, rim_segment, segment_ids, conv_bc_w, conv_bc_b)
    step_size = jax.nn.softplus(dt_raw + dt_bias[:, None])
    log_decay = -step_size * a_rate[:, None]
    cum_decay = jnp.transpose(
        jnp.cumsum(log_decay.reshape(head_count, block_count, GROUP), axis=2), (1, 0, 2)
    )
    step_blocks = jnp.transpose(step_size.reshape(head_count, block_count, GROUP), (1, 0, 2))
    seg_blocks = segment_ids.reshape(block_count, GROUP)
    seg_before = jnp.concatenate([rim_segment[rim_rows - 1 :], seg_blocks[:-1, -1]])
    x_blocks = x_conv.reshape(block_count, GROUP, head_count, HEAD_DIM)
    b_blocks = bc_conv[:, :STATE].reshape(block_count, GROUP, STATE)
    c_blocks = bc_conv[:, STATE:].reshape(block_count, GROUP, STATE)
    everything = (x_blocks, b_blocks, c_blocks, step_blocks, cum_decay, seg_blocks, seg_before)

    def both_of(item):
        x_group, b_group, c_group, steps_here, decay_here, segment, before = item
        block_state, transmit = state_part(
            x_group, b_group, steps_here, decay_here, segment, before
        )
        return (
            mixing_part(x_group, b_group, c_group, steps_here, decay_here, segment),
            block_state,
            transmit,
        )

    y_intra, block_states, transmits = lax.map(both_of, everything)
    entering = chain_states(block_states, transmits, paired)

    def enter_of(item):
        c_group, decay_here, segment, before, entering_here = item
        return entry_part(c_group, entering_here, decay_here, segment, before)

    y_state = lax.map(enter_of, (c_blocks, cum_decay, seg_blocks, seg_before, entering))
    y_blocks = y_intra + y_state
    x_heads = x_conv.reshape(tok_rows, head_count, HEAD_DIM).astype(jnp.float32)
    y_total = y_blocks.reshape(tok_rows, head_count, HEAD_DIM) + skip_d[None, :, None] * x_heads
    gated = y_total.reshape(tok_rows, channels) * jax.nn.silu(gate_z.astype(jnp.float32))
    local_sq = jnp.sum(gated * gated, axis=1)
    total_sq = lax.psum(local_sq, "tp")
    scale = lax.rsqrt(total_sq / INNER + epsilon)
    return (gated * scale[:, None] * norm_gain.astype(jnp.float32)).astype(jnp.bfloat16)


def cores_paired(mesh):
    row = mesh.devices[:, 0] if mesh.devices.ndim == 2 else mesh.devices.reshape(-1)
    if len(row) % 2:
        return False
    try:
        for lo, hi in zip(row[0::2], row[1::2]):
            if tuple(lo.coords) != tuple(hi.coords) or lo.core_on_chip == hi.core_on_chip:
                return False
    except AttributeError:
        return False
    return True


def solution(mesh):
    in_specs = (
        P("ctx", "tp"),
        P("ctx", "tp"),
        P("ctx", None),
        P("tp", "ctx"),
        P("tp"),
        P("tp"),
        P("tp"),
        P(None, "tp"),
        P("tp"),
        P(),
        P(),
        P("tp"),
        P("ctx"),
    )
    out_specs = P("ctx", "tp")
    paired = cores_paired(mesh)
    return jax.shard_map(functools.partial(local, paired), mesh=mesh, in_specs=in_specs, out_specs=out_specs, check_vma=False)
```

```python
import functools

import jax
import jax.numpy as jnp
from jax import lax
from jax.sharding import PartitionSpec as P

HEAD_DIM = 64
STATE = 128
GROUP = 256
CONV = 4
INNER = 8192


epsilon = 1e-05


def passed_along(value, axis, steps):
    count = lax.axis_size(axis)
    leading, last = (max(0, -steps), min(count, count - steps))
    return lax.ppermute(value, axis, [(source, source + steps) for source in range(leading, last)])


def causal_conv(rim_vals, values, rim_segment, segment, weight, offset_bias):
    extended = jnp.concatenate([rim_vals, values], axis=0)
    ext_segment = jnp.concatenate([rim_segment, segment], axis=0)
    length = values.shape[0]
    summed = jnp.zeros(values.shape, jnp.float32) + offset_bias.astype(jnp.float32)
    for offset in range(CONV):
        visible = (ext_segment[offset : offset + length] == segment).astype(jnp.float32)
        summed = (
            summed
            + weight[offset].astype(jnp.float32)
            * extended[offset : offset + length].astype(jnp.float32)
            * visible[:, None]
        )
    return jax.nn.silu(summed).astype(jnp.bfloat16)


def mixing_part(x_group, b_group, c_group, step_size, cum_decay, segment):
    places = jnp.arange(segment.shape[0])
    visible = jnp.logical_and(
        places[:, None] >= places[None, :], segment[:, None] == segment[None, :]
    )
    scores = jnp.einsum("in,jn->ij", c_group, b_group, preferred_element_type=jnp.float32)
    exponent = jnp.where(visible[None], cum_decay[:, :, None] - cum_decay[:, None, :], -jnp.inf)
    mixing = (scores[None] * jnp.exp(exponent) * step_size[:, None, :]).astype(jnp.bfloat16)
    return jnp.einsum("hij,jhp->ihp", mixing, x_group, preferred_element_type=jnp.float32)


def state_part(x_group, b_group, step_size, cum_decay, segment, seg_before):
    closing = cum_decay[:, -1:]
    tail_mask = (segment == segment[-1]).astype(jnp.float32)
    factor = jnp.exp(closing - cum_decay) * step_size * tail_mask[None]
    weighted = (b_group.astype(jnp.float32)[None] * factor[:, :, None]).astype(jnp.bfloat16)
    block_state = jnp.einsum("hjn,jhp->hpn", weighted, x_group, preferred_element_type=jnp.float32)
    transmit = jnp.exp(cum_decay[:, -1]) * (segment[-1] == seg_before).astype(jnp.float32)
    return (block_state, transmit)


def entry_part(c_group, entering, cum_decay, segment, seg_before):
    packed = entering.astype(jnp.bfloat16)
    reach = jnp.exp(cum_decay) * (segment == seg_before).astype(jnp.float32)[None]
    product = jnp.einsum("in,hpn->ihp", c_group, packed, preferred_element_type=jnp.float32)
    return product * jnp.transpose(reach)[:, :, None]


def shifted(value, axis, steps, count):
    return lax.ppermute(value, axis, [(s, s + steps) for s in range(count - steps)])


def scan_round(transmit, state, axis, shift, count):
    far_t, far_s = shifted((transmit, state), axis, shift, count)
    return transmit * far_t, transmit[:, None, None] * far_s + state


def scan_rounds(carry, axis, stride, span, count, far):
    near, needed, rider = far
    carry, rider = lax.optimization_barrier((carry, rider))
    far[2] = rider
    transmit, state = shifted(carry, axis, stride, count)
    covered = 1
    while covered < min(span - 1, near):
        transmit, state = scan_round(transmit, state, axis, stride * covered, count)
        covered *= 2
    if covered < span - 1:

        def rest(carried):
            t, s = carried
            reach = covered
            while reach < span - 1:
                t, s = scan_round(t, s, axis, stride * reach, count)
                reach *= 2
            return t, s

        transmit, state = lax.cond(needed, rest, lambda carried: carried, (transmit, state))
    return state


def gather_small(value, axis):
    count = lax.axis_size(axis)
    if count & (count - 1):
        return lax.all_gather(value, axis, tiled=True)
    place = lax.axis_index(axis)
    size = 1
    while size < count:
        other = lax.ppermute(value, axis, [(s, s ^ size) for s in range(count)])
        value = jnp.where(
            (place & size) == 0,
            jnp.concatenate([value, other]),
            jnp.concatenate([other, value]),
        )
        size *= 2
    return value


def long_runs(last_id, paired, tok_rows):
    count = lax.axis_size("ctx")
    longest = (count * tok_rows // 4 - 1) // tok_rows
    group = 2 if paired else 1
    near = 1
    while near * group <= longest:
        near *= 2
    window = near * group
    ids = gather_small(last_id, "ctx")
    joined = jnp.concatenate([jnp.zeros((1,), jnp.int32), (ids[1:] == ids[:-1]).astype(jnp.int32)])
    if window > count:
        return near, jnp.zeros((), jnp.bool_)
    breaks = jnp.cumsum(1 - joined)
    ahead = jnp.concatenate([jnp.zeros((1,), jnp.int32), breaks[:-window]])
    return near, jnp.any(breaks[window - 1 :] - ahead == 0)


def blockwise(f, items):
    if jax.tree.leaves(items)[0].shape[0] == 1:
        out = f(jax.tree.map(lambda a: a[0], items))
        return jax.tree.map(lambda a: a[None], out)
    return lax.map(f, items)


def device_entry(dev_transmit, dev_state, paired, far):
    count = lax.axis_size("ctx")
    if not paired:
        return scan_rounds((dev_transmit, dev_state), "ctx", 1, count, count, far)
    heads = dev_state.shape[0]
    half = heads // 2
    core = lax.axis_index("ctx") % 2
    swap = [(s, s ^ 1) for s in range(count)]
    own_lo = core * half
    give = lax.dynamic_slice_in_dim(dev_state, half - own_lo, half, 0)
    other_t, other_s = lax.ppermute((dev_transmit, give), "ctx", swap)
    mine_s = lax.dynamic_slice_in_dim(dev_state, own_lo, half, 0)
    mine_t = lax.dynamic_slice_in_dim(dev_transmit, own_lo, half, 0)
    peer_t = lax.dynamic_slice_in_dim(other_t, own_lo, half, 0)
    first = core == 0
    chip_s = jnp.where(first, peer_t[:, None, None] * mine_s + other_s, mine_t[:, None, None] * other_s + mine_s)
    chip_t = mine_t * peer_t
    entering = scan_rounds((chip_t, chip_s), "ctx", 2, count // 2, count, far)
    lead_t = jnp.where(first, mine_t, peer_t)
    lead_s = jnp.where(first, mine_s, other_s)
    second = lead_t[:, None, None] * entering + lead_s
    back = lax.ppermute(jnp.where(first, second, entering), "ctx", swap)
    mine = jnp.where(first, entering, second)
    low = jnp.where(first, mine, back)
    high = jnp.where(first, back, mine)
    return jnp.concatenate([low, high], axis=0)


def chain_states(block_states, transmits, paired, far):

    def advance(carried, item):
        passing, state_now = carried
        transmit, block_state = item
        return (
            (passing * transmit, transmit[:, None, None] * state_now + block_state),
            (passing, state_now),
        )

    start = (jnp.ones_like(transmits[0]), jnp.zeros_like(block_states[0]))
    finals, befores = lax.scan(advance, start, (transmits, block_states))
    entering_dev = device_entry(finals[0], finals[1], paired, far)
    return befores[0][:, :, None, None] * entering_dev[None] + befores[1]


def local(
    paired,
    x_in,
    gate_z,
    bc_in,
    dt_raw,
    dt_bias,
    a_rate,
    skip_d,
    conv_x_w,
    conv_x_b,
    conv_bc_w,
    conv_bc_b,
    norm_gain,
    segment_ids,
):
    tok_rows = x_in.shape[0]
    channels = x_in.shape[1]
    head_count = dt_raw.shape[0]
    block_count = tok_rows // GROUP
    rim_rows = CONV - 1
    rim_x, rim_bc, rim_mark = passed_along(
        (
            x_in[tok_rows - rim_rows :],
            bc_in[tok_rows - rim_rows :],
            segment_ids[tok_rows - rim_rows :].astype(jnp.bfloat16),
        ),
        "ctx",
        1,
    )
    rim_segment = rim_mark.astype(jnp.int32)
    x_conv = causal_conv(rim_x, x_in, rim_segment, segment_ids, conv_x_w, conv_x_b)
    bc_conv = causal_conv(rim_bc, bc_in, rim_segment, segment_ids, conv_bc_w, conv_bc_b)
    step_size = jax.nn.softplus(dt_raw + dt_bias[:, None])
    log_decay = -step_size * a_rate[:, None]
    cum_decay = jnp.transpose(
        jnp.cumsum(log_decay.reshape(head_count, block_count, GROUP), axis=2), (1, 0, 2)
    )
    step_blocks = jnp.transpose(step_size.reshape(head_count, block_count, GROUP), (1, 0, 2))
    seg_blocks = segment_ids.reshape(block_count, GROUP)
    seg_before = jnp.concatenate([rim_segment[rim_rows - 1 :], seg_blocks[:-1, -1]])
    x_blocks = x_conv.reshape(block_count, GROUP, head_count, HEAD_DIM)
    b_blocks = bc_conv[:, :STATE].reshape(block_count, GROUP, STATE)
    c_blocks = bc_conv[:, STATE:].reshape(block_count, GROUP, STATE)

    def state_of(item):
        x_group, b_group, steps_here, decay_here, segment, before = item
        return state_part(x_group, b_group, steps_here, decay_here, segment, before)

    def intra_of(item):
        x_group, b_group, c_group, steps_here, decay_here, segment = item
        return mixing_part(x_group, b_group, c_group, steps_here, decay_here, segment)

    block_states, transmits = blockwise(
        state_of, (x_blocks, b_blocks, step_blocks, cum_decay, seg_blocks, seg_before)
    )
    intra_items = (x_blocks, b_blocks, c_blocks, step_blocks, cum_decay, seg_blocks)
    far = [*long_runs(segment_ids[tok_rows - 1 :], paired, tok_rows), intra_items]
    entering = chain_states(block_states, transmits, paired, far)
    y_intra = blockwise(intra_of, far[2])

    def enter_of(item):
        c_group, decay_here, segment, before, entering_here = item
        return entry_part(c_group, entering_here, decay_here, segment, before)

    y_state = blockwise(enter_of, (c_blocks, cum_decay, seg_blocks, seg_before, entering))
    y_blocks = y_intra + y_state
    x_heads = x_conv.reshape(tok_rows, head_count, HEAD_DIM).astype(jnp.float32)
    y_total = y_blocks.reshape(tok_rows, head_count, HEAD_DIM) + skip_d[None, :, None] * x_heads
    gated = y_total.reshape(tok_rows, channels) * jax.nn.silu(gate_z.astype(jnp.float32))
    local_sq = jnp.sum(gated * gated, axis=1)
    total_sq = lax.psum(local_sq, "tp")
    scale = lax.rsqrt(total_sq / INNER + epsilon)
    return (gated * scale[:, None] * norm_gain.astype(jnp.float32)).astype(jnp.bfloat16)


def cores_paired(mesh):
    row = mesh.devices[:, 0] if mesh.devices.ndim == 2 else mesh.devices.reshape(-1)
    if len(row) % 2:
        return False
    try:
        for lo, hi in zip(row[0::2], row[1::2]):
            if tuple(lo.coords) != tuple(hi.coords) or lo.core_on_chip == hi.core_on_chip:
                return False
    except AttributeError:
        return False
    return True


def solution(mesh):
    in_specs = (
        P("ctx", "tp"),
        P("ctx", "tp"),
        P("ctx", None),
        P("tp", "ctx"),
        P("tp"),
        P("tp"),
        P("tp"),
        P(None, "tp"),
        P("tp"),
        P(),
        P(),
        P("tp"),
        P("ctx"),
    )
    out_specs = P("ctx", "tp")
    paired = cores_paired(mesh)
    return jax.shard_map(functools.partial(local, paired), mesh=mesh, in_specs=in_specs, out_specs=out_specs, check_vma=False)
```

```python
import functools

import jax
import jax.numpy as jnp
from jax import lax
from jax.sharding import PartitionSpec as P

HEAD_DIM = 64
STATE = 128
GROUP = 256
CONV = 4
INNER = 8192


epsilon = 1e-05


def passed_along(value, axis, steps):
    count = lax.axis_size(axis)
    leading, last = (max(0, -steps), min(count, count - steps))
    return lax.ppermute(value, axis, [(source, source + steps) for source in range(leading, last)])


def causal_conv(rim_vals, values, rim_segment, segment, weight, offset_bias):
    extended = jnp.concatenate([rim_vals, values], axis=0)
    ext_segment = jnp.concatenate([rim_segment, segment], axis=0)
    length = values.shape[0]
    summed = jnp.zeros(values.shape, jnp.float32) + offset_bias.astype(jnp.float32)
    for offset in range(CONV):
        visible = (ext_segment[offset : offset + length] == segment).astype(jnp.float32)
        summed = (
            summed
            + weight[offset].astype(jnp.float32)
            * extended[offset : offset + length].astype(jnp.float32)
            * visible[:, None]
        )
    return jax.nn.silu(summed).astype(jnp.bfloat16)


def mixing_part(x_group, b_group, c_group, step_size, cum_decay, segment):
    places = jnp.arange(segment.shape[0])
    visible = jnp.logical_and(
        places[:, None] >= places[None, :], segment[:, None] == segment[None, :]
    )
    scores = jnp.einsum("in,jn->ij", c_group, b_group, preferred_element_type=jnp.float32)
    exponent = jnp.where(visible[None], cum_decay[:, :, None] - cum_decay[:, None, :], -jnp.inf)
    mixing = (scores[None] * jnp.exp(exponent) * step_size[:, None, :]).astype(jnp.bfloat16)
    return jnp.einsum("hij,jhp->ihp", mixing, x_group, preferred_element_type=jnp.float32)


def state_part(x_group, b_group, step_size, cum_decay, segment, seg_before):
    closing = cum_decay[:, -1:]
    tail_mask = (segment == segment[-1]).astype(jnp.float32)
    factor = jnp.exp(closing - cum_decay) * step_size * tail_mask[None]
    weighted = (b_group.astype(jnp.float32)[None] * factor[:, :, None]).astype(jnp.bfloat16)
    block_state = jnp.einsum("hjn,jhp->hpn", weighted, x_group, preferred_element_type=jnp.float32)
    transmit = jnp.exp(cum_decay[:, -1]) * (segment[-1] == seg_before).astype(jnp.float32)
    return (block_state, transmit)


def entry_part(c_group, entering, cum_decay, segment, seg_before):
    packed = entering.astype(jnp.bfloat16)
    reach = jnp.exp(cum_decay) * (segment == seg_before).astype(jnp.float32)[None]
    product = jnp.einsum("in,hpn->ihp", c_group, packed, preferred_element_type=jnp.float32)
    return product * jnp.transpose(reach)[:, :, None]


def shifted(value, axis, steps, count):
    return lax.ppermute(value, axis, [(s, s + steps) for s in range(count - steps)])


def scan_round(transmit, state, axis, shift, count):
    far_t, far_s = shifted((transmit, state), axis, shift, count)
    return transmit * far_t, transmit[:, None, None] * far_s + state


def scan_rounds(carry, axis, stride, span, count, far):
    near, needed, rider, work = far
    carry, rider, needed = lax.optimization_barrier((carry, rider, needed))
    transmit, state = shifted(carry, axis, stride, count)
    (transmit, state), far[2] = lax.optimization_barrier(((transmit, state), work(rider)))
    covered = 1
    while covered < min(span - 1, near):
        transmit, state = scan_round(transmit, state, axis, stride * covered, count)
        covered *= 2
    if covered < span - 1:

        def rest(carried):
            t, s = carried
            reach = covered
            while reach < span - 1:
                t, s = scan_round(t, s, axis, stride * reach, count)
                reach *= 2
            return t, s

        transmit, state = lax.cond(needed, rest, lambda carried: carried, (transmit, state))
    return state


def gather_small(value, axis):
    count = lax.axis_size(axis)
    if count & (count - 1):
        return lax.all_gather(value, axis, tiled=True)
    place = lax.axis_index(axis)
    size = 1
    while size < count:
        other = lax.ppermute(value, axis, [(s, s ^ size) for s in range(count)])
        value = jnp.where(
            (place & size) == 0,
            jnp.concatenate([value, other]),
            jnp.concatenate([other, value]),
        )
        size *= 2
    return value


def long_runs(last_id, paired, tok_rows):
    count = lax.axis_size("ctx")
    longest = (count * tok_rows // 4 - 1) // tok_rows
    group = 2 if paired else 1
    near = 1
    while near * group <= longest:
        near *= 2
    window = near * group
    ids = gather_small(last_id, "ctx")
    joined = jnp.concatenate([jnp.zeros((1,), jnp.int32), (ids[1:] == ids[:-1]).astype(jnp.int32)])
    if window > count:
        return near, jnp.zeros((), jnp.bool_)
    breaks = jnp.cumsum(1 - joined)
    ahead = jnp.concatenate([jnp.zeros((1,), jnp.int32), breaks[:-window]])
    return near, jnp.any(breaks[window - 1 :] - ahead == 0)


def blockwise(f, items):
    if jax.tree.leaves(items)[0].shape[0] == 1:
        out = f(jax.tree.map(lambda a: a[0], items))
        return jax.tree.map(lambda a: a[None], out)
    return lax.map(f, items)


def device_entry(dev_transmit, dev_state, paired, far):
    count = lax.axis_size("ctx")
    if not paired:
        return scan_rounds((dev_transmit, dev_state), "ctx", 1, count, count, far)
    heads = dev_state.shape[0]
    half = heads // 2
    core = lax.axis_index("ctx") % 2
    swap = [(s, s ^ 1) for s in range(count)]
    own_lo = core * half
    give = lax.dynamic_slice_in_dim(dev_state, half - own_lo, half, 0)
    other_t, other_s = lax.ppermute((dev_transmit, give), "ctx", swap)
    mine_s = lax.dynamic_slice_in_dim(dev_state, own_lo, half, 0)
    mine_t = lax.dynamic_slice_in_dim(dev_transmit, own_lo, half, 0)
    peer_t = lax.dynamic_slice_in_dim(other_t, own_lo, half, 0)
    first = core == 0
    chip_s = jnp.where(first, peer_t[:, None, None] * mine_s + other_s, mine_t[:, None, None] * other_s + mine_s)
    chip_t = mine_t * peer_t
    entering = scan_rounds((chip_t, chip_s), "ctx", 2, count // 2, count, far)
    lead_t = jnp.where(first, mine_t, peer_t)
    lead_s = jnp.where(first, mine_s, other_s)
    second = lead_t[:, None, None] * entering + lead_s
    back = lax.ppermute(jnp.where(first, second, entering), "ctx", swap)
    mine = jnp.where(first, entering, second)
    low = jnp.where(first, mine, back)
    high = jnp.where(first, back, mine)
    return jnp.concatenate([low, high], axis=0)


def chain_states(block_states, transmits, paired, far):

    def advance(carried, item):
        passing, state_now = carried
        transmit, block_state = item
        return (
            (passing * transmit, transmit[:, None, None] * state_now + block_state),
            (passing, state_now),
        )

    start = (jnp.ones_like(transmits[0]), jnp.zeros_like(block_states[0]))
    finals, befores = lax.scan(advance, start, (transmits, block_states))
    entering_dev = device_entry(finals[0], finals[1], paired, far)
    return befores[0][:, :, None, None] * entering_dev[None] + befores[1]


def local(
    paired,
    x_in,
    gate_z,
    bc_in,
    dt_raw,
    dt_bias,
    a_rate,
    skip_d,
    conv_x_w,
    conv_x_b,
    conv_bc_w,
    conv_bc_b,
    norm_gain,
    segment_ids,
):
    tok_rows = x_in.shape[0]
    channels = x_in.shape[1]
    head_count = dt_raw.shape[0]
    block_count = tok_rows // GROUP
    rim_rows = CONV - 1
    rim_x, rim_bc, rim_mark = passed_along(
        (
            x_in[tok_rows - rim_rows :],
            bc_in[tok_rows - rim_rows :],
            segment_ids[tok_rows - rim_rows :].astype(jnp.bfloat16),
        ),
        "ctx",
        1,
    )
    rim_segment = rim_mark.astype(jnp.int32)
    x_conv = causal_conv(rim_x, x_in, rim_segment, segment_ids, conv_x_w, conv_x_b)
    bc_conv = causal_conv(rim_bc, bc_in, rim_segment, segment_ids, conv_bc_w, conv_bc_b)
    step_size = jax.nn.softplus(dt_raw + dt_bias[:, None])
    log_decay = -step_size * a_rate[:, None]
    cum_decay = jnp.transpose(
        jnp.cumsum(log_decay.reshape(head_count, block_count, GROUP), axis=2), (1, 0, 2)
    )
    step_blocks = jnp.transpose(step_size.reshape(head_count, block_count, GROUP), (1, 0, 2))
    seg_blocks = segment_ids.reshape(block_count, GROUP)
    seg_before = jnp.concatenate([rim_segment[rim_rows - 1 :], seg_blocks[:-1, -1]])
    x_blocks = x_conv.reshape(block_count, GROUP, head_count, HEAD_DIM)
    b_blocks = bc_conv[:, :STATE].reshape(block_count, GROUP, STATE)
    c_blocks = bc_conv[:, STATE:].reshape(block_count, GROUP, STATE)

    def state_of(item):
        x_group, b_group, steps_here, decay_here, segment, before = item
        return state_part(x_group, b_group, steps_here, decay_here, segment, before)

    def intra_of(item):
        x_group, b_group, c_group, steps_here, decay_here, segment = item
        return mixing_part(x_group, b_group, c_group, steps_here, decay_here, segment)

    block_states, transmits = blockwise(
        state_of, (x_blocks, b_blocks, step_blocks, cum_decay, seg_blocks, seg_before)
    )
    intra_items = (x_blocks, b_blocks, c_blocks, step_blocks, cum_decay, seg_blocks)
    far = [
        *long_runs(segment_ids[tok_rows - 1 :], paired, tok_rows),
        intra_items,
        functools.partial(blockwise, intra_of),
    ]
    entering = chain_states(block_states, transmits, paired, far)
    y_intra = far[2]

    def enter_of(item):
        c_group, decay_here, segment, before, entering_here = item
        return entry_part(c_group, entering_here, decay_here, segment, before)

    y_state = blockwise(enter_of, (c_blocks, cum_decay, seg_blocks, seg_before, entering))
    y_blocks = y_intra + y_state
    x_heads = x_conv.reshape(tok_rows, head_count, HEAD_DIM).astype(jnp.float32)
    y_total = y_blocks.reshape(tok_rows, head_count, HEAD_DIM) + skip_d[None, :, None] * x_heads
    gated = y_total.reshape(tok_rows, channels) * jax.nn.silu(gate_z.astype(jnp.float32))
    local_sq = jnp.sum(gated * gated, axis=1)
    total_sq = lax.psum(local_sq, "tp")
    scale = lax.rsqrt(total_sq / INNER + epsilon)
    return (gated * scale[:, None] * norm_gain.astype(jnp.float32)).astype(jnp.bfloat16)


def cores_paired(mesh):
    row = mesh.devices[:, 0] if mesh.devices.ndim == 2 else mesh.devices.reshape(-1)
    if len(row) % 2:
        return False
    try:
        for lo, hi in zip(row[0::2], row[1::2]):
            if tuple(lo.coords) != tuple(hi.coords) or lo.core_on_chip == hi.core_on_chip:
                return False
    except AttributeError:
        return False
    return True


def solution(mesh):
    in_specs = (
        P("ctx", "tp"),
        P("ctx", "tp"),
        P("ctx", None),
        P("tp", "ctx"),
        P("tp"),
        P("tp"),
        P("tp"),
        P(None, "tp"),
        P("tp"),
        P(),
        P(),
        P("tp"),
        P("ctx"),
    )
    out_specs = P("ctx", "tp")
    paired = cores_paired(mesh)
    return jax.shard_map(functools.partial(local, paired), mesh=mesh, in_specs=in_specs, out_specs=out_specs, check_vma=False)
```

```python
import functools

import jax
import jax.numpy as jnp
from jax import lax
from jax.sharding import PartitionSpec as P

HEAD_DIM = 64
STATE = 128
GROUP = 256
CONV = 4
INNER = 8192


epsilon = 1e-05


def passed_along(value, axis, steps):
    count = lax.axis_size(axis)
    leading, last = (max(0, -steps), min(count, count - steps))
    return lax.ppermute(value, axis, [(source, source + steps) for source in range(leading, last)])


def causal_conv(rim_vals, values, rim_segment, segment, weight, offset_bias):
    extended = jnp.concatenate([rim_vals, values], axis=0)
    ext_segment = jnp.concatenate([rim_segment, segment], axis=0)
    length = values.shape[0]
    summed = jnp.zeros(values.shape, jnp.float32) + offset_bias.astype(jnp.float32)
    for offset in range(CONV):
        visible = (ext_segment[offset : offset + length] == segment).astype(jnp.float32)
        summed = (
            summed
            + weight[offset].astype(jnp.float32)
            * extended[offset : offset + length].astype(jnp.float32)
            * visible[:, None]
        )
    return jax.nn.silu(summed).astype(jnp.bfloat16)


def mixing_part(x_group, b_group, c_group, step_size, cum_decay, segment):
    places = jnp.arange(segment.shape[0])
    visible = jnp.logical_and(
        places[:, None] >= places[None, :], segment[:, None] == segment[None, :]
    )
    scores = jnp.einsum("in,jn->ij", c_group, b_group, preferred_element_type=jnp.float32)
    exponent = jnp.where(visible[None], cum_decay[:, :, None] - cum_decay[:, None, :], -jnp.inf)
    mixing = (scores[None] * jnp.exp(exponent) * step_size[:, None, :]).astype(jnp.bfloat16)
    return jnp.einsum("hij,jhp->ihp", mixing, x_group, preferred_element_type=jnp.float32)


def state_part(x_group, b_group, step_size, cum_decay, segment, seg_before):
    closing = cum_decay[:, -1:]
    tail_mask = (segment == segment[-1]).astype(jnp.float32)
    factor = jnp.exp(closing - cum_decay) * step_size * tail_mask[None]
    weighted = (b_group.astype(jnp.float32)[None] * factor[:, :, None]).astype(jnp.bfloat16)
    block_state = jnp.einsum("hjn,jhp->hpn", weighted, x_group, preferred_element_type=jnp.float32)
    transmit = jnp.exp(cum_decay[:, -1]) * (segment[-1] == seg_before).astype(jnp.float32)
    return (block_state, transmit)


def entry_part(c_group, entering, cum_decay, segment, seg_before):
    packed = entering.astype(jnp.bfloat16)
    reach = jnp.exp(cum_decay) * (segment == seg_before).astype(jnp.float32)[None]
    product = jnp.einsum("in,hpn->ihp", c_group, packed, preferred_element_type=jnp.float32)
    return product * jnp.transpose(reach)[:, :, None]


def shifted(value, axis, steps, count):
    return lax.ppermute(value, axis, [(s, s + steps) for s in range(count - steps)])


def scan_round(transmit, state, axis, shift, count):
    far_t, far_s = shifted((transmit, state), axis, shift, count)
    return transmit * far_t, transmit[:, None, None] * far_s + state


def scan_rounds(carry, axis, stride, span, count, far):
    near, needed, rider = far
    carry, rider = lax.optimization_barrier((carry, rider))
    far[2] = rider
    transmit, state = shifted(carry, axis, stride, count)
    covered = 1
    while covered < min(span - 1, near):
        transmit, state = scan_round(transmit, state, axis, stride * covered, count)
        covered *= 2
    if covered < span - 1:

        def rest(carried):
            t, s = carried
            reach = covered
            while reach < span - 1:
                t, s = scan_round(t, s, axis, stride * reach, count)
                reach *= 2
            return t, s

        transmit, state = lax.cond(needed, rest, lambda carried: carried, (transmit, state))
    return state


def gather_round(value, axis, size):
    count = lax.axis_size(axis)
    if count & (count - 1):
        return lax.all_gather(value, axis, tiled=True) if size == 1 else value
    if size >= count:
        return value
    place = lax.axis_index(axis)
    other = lax.ppermute(value, axis, [(s, s ^ size) for s in range(count)])
    return jnp.where(
        (place & size) == 0,
        jnp.concatenate([value, other]),
        jnp.concatenate([other, value]),
    )


def gather_rounds(value, axis, first, last):
    size = 1 << first
    while size < (1 << last):
        value = gather_round(value, axis, size)
        size *= 2
    return value


def long_runs(ids, paired, tok_rows):
    count = lax.axis_size("ctx")
    longest = (count * tok_rows // 4 - 1) // tok_rows
    group = 2 if paired else 1
    near = 1
    while near * group <= longest:
        near *= 2
    window = near * group
    joined = jnp.concatenate([jnp.zeros((1,), jnp.int32), (ids[1:] == ids[:-1]).astype(jnp.int32)])
    if window > count:
        return near, jnp.zeros((), jnp.bool_)
    breaks = jnp.cumsum(1 - joined)
    ahead = jnp.concatenate([jnp.zeros((1,), jnp.int32), breaks[:-window]])
    return near, jnp.any(breaks[window - 1 :] - ahead == 0)


def blockwise(f, items):
    if jax.tree.leaves(items)[0].shape[0] == 1:
        out = f(jax.tree.map(lambda a: a[0], items))
        return jax.tree.map(lambda a: a[None], out)
    return lax.map(f, items)


def device_entry(dev_transmit, dev_state, paired, far):
    count = lax.axis_size("ctx")
    if not paired:
        return scan_rounds((dev_transmit, dev_state), "ctx", 1, count, count, far)
    heads = dev_state.shape[0]
    half = heads // 2
    core = lax.axis_index("ctx") % 2
    swap = [(s, s ^ 1) for s in range(count)]
    own_lo = core * half
    give = lax.dynamic_slice_in_dim(dev_state, half - own_lo, half, 0)
    other_t, other_s = lax.ppermute((dev_transmit, give), "ctx", swap)
    mine_s = lax.dynamic_slice_in_dim(dev_state, own_lo, half, 0)
    mine_t = lax.dynamic_slice_in_dim(dev_transmit, own_lo, half, 0)
    peer_t = lax.dynamic_slice_in_dim(other_t, own_lo, half, 0)
    first = core == 0
    chip_s = jnp.where(first, peer_t[:, None, None] * mine_s + other_s, mine_t[:, None, None] * other_s + mine_s)
    chip_t = mine_t * peer_t
    entering = scan_rounds((chip_t, chip_s), "ctx", 2, count // 2, count, far)
    lead_t = jnp.where(first, mine_t, peer_t)
    lead_s = jnp.where(first, mine_s, other_s)
    second = lead_t[:, None, None] * entering + lead_s
    back = lax.ppermute(jnp.where(first, second, entering), "ctx", swap)
    mine = jnp.where(first, entering, second)
    low = jnp.where(first, mine, back)
    high = jnp.where(first, back, mine)
    return jnp.concatenate([low, high], axis=0)


def chain_states(block_states, transmits, paired, far):

    def advance(carried, item):
        passing, state_now = carried
        transmit, block_state = item
        return (
            (passing * transmit, transmit[:, None, None] * state_now + block_state),
            (passing, state_now),
        )

    start = (jnp.ones_like(transmits[0]), jnp.zeros_like(block_states[0]))
    finals, befores = lax.scan(advance, start, (transmits, block_states))
    entering_dev = device_entry(finals[0], finals[1], paired, far)
    return befores[0][:, :, None, None] * entering_dev[None] + befores[1]


def local(
    paired,
    x_in,
    gate_z,
    bc_in,
    dt_raw,
    dt_bias,
    a_rate,
    skip_d,
    conv_x_w,
    conv_x_b,
    conv_bc_w,
    conv_bc_b,
    norm_gain,
    segment_ids,
):
    tok_rows = x_in.shape[0]
    channels = x_in.shape[1]
    head_count = dt_raw.shape[0]
    block_count = tok_rows // GROUP
    rim_rows = CONV - 1
    bc_width = bc_in.shape[1]
    rims = passed_along(
        jnp.concatenate(
            [
                x_in[tok_rows - rim_rows :],
                bc_in[tok_rows - rim_rows :],
                segment_ids[tok_rows - rim_rows :, None].astype(jnp.bfloat16),
            ],
            axis=1,
        ),
        "ctx",
        1,
    )
    rim_x = rims[:, :channels]
    rim_bc = rims[:, channels : channels + bc_width]
    rim_segment = rims[:, channels + bc_width].astype(jnp.int32)
    ids = gather_rounds(segment_ids[tok_rows - 1 :], "ctx", 0, 2)
    ids, rim_x = lax.optimization_barrier((ids, rim_x))
    x_conv = causal_conv(rim_x, x_in, rim_segment, segment_ids, conv_x_w, conv_x_b)
    ids = gather_rounds(ids, "ctx", 2, 4)
    ids, x_conv = lax.optimization_barrier((ids, x_conv))
    bc_conv = causal_conv(rim_bc, bc_in, rim_segment, segment_ids, conv_bc_w, conv_bc_b)
    step_size = jax.nn.softplus(dt_raw + dt_bias[:, None])
    log_decay = -step_size * a_rate[:, None]
    cum_decay = jnp.transpose(
        jnp.cumsum(log_decay.reshape(head_count, block_count, GROUP), axis=2), (1, 0, 2)
    )
    step_blocks = jnp.transpose(step_size.reshape(head_count, block_count, GROUP), (1, 0, 2))
    seg_blocks = segment_ids.reshape(block_count, GROUP)
    seg_before = jnp.concatenate([rim_segment[rim_rows - 1 :], seg_blocks[:-1, -1]])
    x_blocks = x_conv.reshape(block_count, GROUP, head_count, HEAD_DIM)
    b_blocks = bc_conv[:, :STATE].reshape(block_count, GROUP, STATE)
    c_blocks = bc_conv[:, STATE:].reshape(block_count, GROUP, STATE)

    def state_of(item):
        x_group, b_group, steps_here, decay_here, segment, before = item
        return state_part(x_group, b_group, steps_here, decay_here, segment, before)

    def intra_of(item):
        x_group, b_group, c_group, steps_here, decay_here, segment = item
        return mixing_part(x_group, b_group, c_group, steps_here, decay_here, segment)

    block_states, transmits = blockwise(
        state_of, (x_blocks, b_blocks, step_blocks, cum_decay, seg_blocks, seg_before)
    )
    intra_items = (x_blocks, b_blocks, c_blocks, step_blocks, cum_decay, seg_blocks)
    ids = gather_rounds(ids, "ctx", 4, lax.axis_size("ctx").bit_length())
    ids, block_states = lax.optimization_barrier((ids, block_states))
    far = [*long_runs(ids, paired, tok_rows), intra_items]
    entering = chain_states(block_states, transmits, paired, far)
    y_intra = blockwise(intra_of, far[2])

    def enter_of(item):
        c_group, decay_here, segment, before, entering_here = item
        return entry_part(c_group, entering_here, decay_here, segment, before)

    y_state = blockwise(enter_of, (c_blocks, cum_decay, seg_blocks, seg_before, entering))
    y_blocks = y_intra + y_state
    x_heads = x_conv.reshape(tok_rows, head_count, HEAD_DIM).astype(jnp.float32)
    y_total = y_blocks.reshape(tok_rows, head_count, HEAD_DIM) + skip_d[None, :, None] * x_heads
    gated = y_total.reshape(tok_rows, channels) * jax.nn.silu(gate_z.astype(jnp.float32))
    local_sq = jnp.sum(gated * gated, axis=1)
    total_sq = lax.psum(local_sq, "tp")
    scale = lax.rsqrt(total_sq / INNER + epsilon)
    return (gated * scale[:, None] * norm_gain.astype(jnp.float32)).astype(jnp.bfloat16)


def cores_paired(mesh):
    row = mesh.devices[:, 0] if mesh.devices.ndim == 2 else mesh.devices.reshape(-1)
    if len(row) % 2:
        return False
    try:
        for lo, hi in zip(row[0::2], row[1::2]):
            if tuple(lo.coords) != tuple(hi.coords) or lo.core_on_chip == hi.core_on_chip:
                return False
    except AttributeError:
        return False
    return True


def solution(mesh):
    in_specs = (
        P("ctx", "tp"),
        P("ctx", "tp"),
        P("ctx", None),
        P("tp", "ctx"),
        P("tp"),
        P("tp"),
        P("tp"),
        P(None, "tp"),
        P("tp"),
        P(),
        P(),
        P("tp"),
        P("ctx"),
    )
    out_specs = P("ctx", "tp")
    paired = cores_paired(mesh)
    return jax.shard_map(functools.partial(local, paired), mesh=mesh, in_specs=in_specs, out_specs=out_specs, check_vma=False)
```

```python
import functools

import jax
import jax.numpy as jnp
from jax import lax
from jax.sharding import PartitionSpec as P

HEAD_DIM = 64
STATE = 128
GROUP = 256
CONV = 4
INNER = 8192


epsilon = 1e-05


def passed_along(value, axis, steps):
    count = lax.axis_size(axis)
    leading, last = (max(0, -steps), min(count, count - steps))
    return lax.ppermute(value, axis, [(source, source + steps) for source in range(leading, last)])


def causal_conv(rim_vals, values, rim_segment, segment, weight, offset_bias):
    extended = jnp.concatenate([rim_vals, values], axis=0)
    ext_segment = jnp.concatenate([rim_segment, segment], axis=0)
    length = values.shape[0]
    summed = jnp.zeros(values.shape, jnp.float32) + offset_bias.astype(jnp.float32)
    for offset in range(CONV):
        visible = (ext_segment[offset : offset + length] == segment).astype(jnp.float32)
        summed = (
            summed
            + weight[offset].astype(jnp.float32)
            * extended[offset : offset + length].astype(jnp.float32)
            * visible[:, None]
        )
    return jax.nn.silu(summed).astype(jnp.bfloat16)


def mixing_part(x_group, b_group, c_group, step_size, cum_decay, segment):
    places = jnp.arange(segment.shape[0])
    visible = jnp.logical_and(
        places[:, None] >= places[None, :], segment[:, None] == segment[None, :]
    )
    scores = jnp.einsum("in,jn->ij", c_group, b_group, preferred_element_type=jnp.float32)
    exponent = jnp.where(visible[None], cum_decay[:, :, None] - cum_decay[:, None, :], -jnp.inf)
    mixing = (scores[None] * jnp.exp(exponent) * step_size[:, None, :]).astype(jnp.bfloat16)
    return jnp.einsum("hij,jhp->ihp", mixing, x_group, preferred_element_type=jnp.float32)


def state_part(x_group, b_group, step_size, cum_decay, segment, seg_before):
    closing = cum_decay[:, -1:]
    tail_mask = (segment == segment[-1]).astype(jnp.float32)
    factor = jnp.exp(closing - cum_decay) * step_size * tail_mask[None]
    weighted = (b_group.astype(jnp.float32)[None] * factor[:, :, None]).astype(jnp.bfloat16)
    block_state = jnp.einsum("hjn,jhp->hpn", weighted, x_group, preferred_element_type=jnp.float32)
    transmit = jnp.exp(cum_decay[:, -1]) * (segment[-1] == seg_before).astype(jnp.float32)
    return (block_state, transmit)


def entry_part(c_group, entering, cum_decay, segment, seg_before):
    packed = entering.astype(jnp.bfloat16)
    reach = jnp.exp(cum_decay) * (segment == seg_before).astype(jnp.float32)[None]
    product = jnp.einsum("in,hpn->ihp", c_group, packed, preferred_element_type=jnp.float32)
    return product * jnp.transpose(reach)[:, :, None]


def shifted(value, axis, steps, count):
    return lax.ppermute(value, axis, [(s, s + steps) for s in range(count - steps)])


def scan_round(transmit, state, axis, shift, count):
    far_t, far_s = shifted((transmit, state), axis, shift, count)
    return transmit * far_t, transmit[:, None, None] * far_s + state


def scan_rounds(carry, axis, stride, span, count, far):
    near, needed, rider = far
    carry, rider = lax.optimization_barrier((carry, rider))
    far[2] = rider
    transmit, state = shifted(carry, axis, stride, count)
    covered = 1
    while covered < min(span - 1, near):
        transmit, state = scan_round(transmit, state, axis, stride * covered, count)
        covered *= 2
    if covered < span - 1:

        def rest(carried):
            t, s = carried
            reach = covered
            while reach < span - 1:
                t, s = scan_round(t, s, axis, stride * reach, count)
                reach *= 2
            return t, s

        transmit, state = lax.cond(needed, rest, lambda carried: carried, (transmit, state))
    return state


def gather_round(value, axis, size):
    count = lax.axis_size(axis)
    if count & (count - 1):
        return lax.all_gather(value, axis, tiled=True) if size == 1 else value
    if size >= count:
        return value
    place = lax.axis_index(axis)
    other = lax.ppermute(value, axis, [(s, s ^ size) for s in range(count)])
    return jnp.where(
        (place & size) == 0,
        jnp.concatenate([value, other]),
        jnp.concatenate([other, value]),
    )


def gather_rounds(value, axis, first, last):
    size = 1 << first
    while size < (1 << last):
        value = gather_round(value, axis, size)
        size *= 2
    return value


def long_runs(ids, paired, tok_rows):
    count = lax.axis_size("ctx")
    longest = (count * tok_rows // 4 - 1) // tok_rows
    group = 2 if paired else 1
    near = 1
    while near * group <= longest:
        near *= 2
    window = near * group
    joined = jnp.concatenate([jnp.zeros((1,), jnp.int32), (ids[1:] == ids[:-1]).astype(jnp.int32)])
    if window > count:
        return near, jnp.zeros((), jnp.bool_)
    breaks = jnp.cumsum(1 - joined)
    ahead = jnp.concatenate([jnp.zeros((1,), jnp.int32), breaks[:-window]])
    return near, jnp.any(breaks[window - 1 :] - ahead == 0)


def blockwise(f, items):
    if jax.tree.leaves(items)[0].shape[0] == 1:
        out = f(jax.tree.map(lambda a: a[0], items))
        return jax.tree.map(lambda a: a[None], out)
    return lax.map(f, items)


def device_entry(dev_transmit, dev_state, paired, far):
    count = lax.axis_size("ctx")
    if not paired:
        return scan_rounds((dev_transmit, dev_state), "ctx", 1, count, count, far)
    heads = dev_state.shape[0]
    half = heads // 2
    core = lax.axis_index("ctx") % 2
    swap = [(s, s ^ 1) for s in range(count)]
    own_lo = core * half
    give = lax.dynamic_slice_in_dim(dev_state, half - own_lo, half, 0)
    other_t, other_s = lax.ppermute((dev_transmit, give), "ctx", swap)
    mine_s = lax.dynamic_slice_in_dim(dev_state, own_lo, half, 0)
    mine_t = lax.dynamic_slice_in_dim(dev_transmit, own_lo, half, 0)
    peer_t = lax.dynamic_slice_in_dim(other_t, own_lo, half, 0)
    first = core == 0
    chip_s = jnp.where(first, peer_t[:, None, None] * mine_s + other_s, mine_t[:, None, None] * other_s + mine_s)
    chip_t = mine_t * peer_t
    entering = scan_rounds((chip_t, chip_s), "ctx", 2, count // 2, count, far)
    lead_t = jnp.where(first, mine_t, peer_t)
    lead_s = jnp.where(first, mine_s, other_s)
    second = lead_t[:, None, None] * entering + lead_s
    back = lax.ppermute(jnp.where(first, second, entering), "ctx", swap)
    mine = jnp.where(first, entering, second)
    low = jnp.where(first, mine, back)
    high = jnp.where(first, back, mine)
    return jnp.concatenate([low, high], axis=0)


def chain_states(block_states, transmits, paired, far):

    def advance(carried, item):
        passing, state_now = carried
        transmit, block_state = item
        return (
            (passing * transmit, transmit[:, None, None] * state_now + block_state),
            (passing, state_now),
        )

    start = (jnp.ones_like(transmits[0]), jnp.zeros_like(block_states[0]))
    finals, befores = lax.scan(advance, start, (transmits, block_states))
    entering_dev = device_entry(finals[0], finals[1], paired, far)
    return befores[0][:, :, None, None] * entering_dev[None] + befores[1]


def local(
    paired,
    x_in,
    gate_z,
    bc_in,
    dt_raw,
    dt_bias,
    a_rate,
    skip_d,
    conv_x_w,
    conv_x_b,
    conv_bc_w,
    conv_bc_b,
    norm_gain,
    segment_ids,
):
    tok_rows = x_in.shape[0]
    channels = x_in.shape[1]
    head_count = dt_raw.shape[0]
    block_count = tok_rows // GROUP
    rim_rows = CONV - 1
    bc_width = bc_in.shape[1]
    rims = passed_along(
        jnp.concatenate(
            [
                x_in[tok_rows - rim_rows :],
                bc_in[tok_rows - rim_rows :],
                segment_ids[tok_rows - rim_rows :, None].astype(jnp.bfloat16),
            ],
            axis=1,
        ),
        "ctx",
        1,
    )
    rim_x = rims[:, :channels]
    rim_bc = rims[:, channels : channels + bc_width]
    rim_segment = rims[:, channels + bc_width].astype(jnp.int32)
    ids = gather_rounds(segment_ids[tok_rows - 1 :], "ctx", 0, 2)
    ids, rim_x = lax.optimization_barrier((ids, rim_x))
    pieces = 2 if head_count % 4 == 0 else 1

    def pick(a, axis, piece):
        if pieces == 1:
            return a
        lead, rest = a.shape[:axis], a.shape[axis + 1 :]
        split = a.reshape(lead + (2, pieces, a.shape[axis] // (2 * pieces)) + rest)
        taken = lax.index_in_dim(split, piece, axis + 1, keepdims=False)
        return taken.reshape(lead + (a.shape[axis] // pieces,) + rest)

    bc_conv = causal_conv(rim_bc, bc_in, rim_segment, segment_ids, conv_bc_w, conv_bc_b)
    step_size = jax.nn.softplus(dt_raw + dt_bias[:, None])
    log_decay = -step_size * a_rate[:, None]
    seg_blocks = segment_ids.reshape(block_count, GROUP)
    seg_before = jnp.concatenate([rim_segment[rim_rows - 1 :], seg_blocks[:-1, -1]])
    b_blocks = bc_conv[:, :STATE].reshape(block_count, GROUP, STATE)
    c_blocks = bc_conv[:, STATE:].reshape(block_count, GROUP, STATE)
    part_heads = head_count // pieces
    part_channels = channels // pieces

    def state_of(item):
        x_group, b_group, steps_here, decay_here, segment, before = item
        return state_part(x_group, b_group, steps_here, decay_here, segment, before)

    def intra_of(item):
        x_group, b_group, c_group, steps_here, decay_here, segment = item
        return mixing_part(x_group, b_group, c_group, steps_here, decay_here, segment)

    def enter_of(item):
        c_group, decay_here, segment, before, entering_here = item
        return entry_part(c_group, entering_here, decay_here, segment, before)

    gated_parts = []
    square_parts = []
    for piece in range(pieces):
        x_conv = causal_conv(
            pick(rim_x, 1, piece),
            pick(x_in, 1, piece),
            rim_segment,
            segment_ids,
            pick(conv_x_w, 1, piece),
            pick(conv_x_b, 0, piece),
        )
        if piece == 0:
            ids = gather_rounds(ids, "ctx", 2, 4)
            ids, x_conv = lax.optimization_barrier((ids, x_conv))
        steps = pick(step_size, 0, piece)
        decays = pick(log_decay, 0, piece)
        cum_decay = jnp.transpose(
            jnp.cumsum(decays.reshape(part_heads, block_count, GROUP), axis=2), (1, 0, 2)
        )
        step_blocks = jnp.transpose(steps.reshape(part_heads, block_count, GROUP), (1, 0, 2))
        x_blocks = x_conv.reshape(block_count, GROUP, part_heads, HEAD_DIM)
        block_states, transmits = blockwise(
            state_of, (x_blocks, b_blocks, step_blocks, cum_decay, seg_blocks, seg_before)
        )
        if piece == 0:
            ids = gather_rounds(ids, "ctx", 4, lax.axis_size("ctx").bit_length())
            ids, block_states = lax.optimization_barrier((ids, block_states))
            near, needed = long_runs(ids, paired, tok_rows)
        intra_items = (x_blocks, b_blocks, c_blocks, step_blocks, cum_decay, seg_blocks)
        far = [near, needed, intra_items]
        entering = chain_states(block_states, transmits, paired, far)
        y_intra = blockwise(intra_of, far[2])
        y_state = blockwise(enter_of, (c_blocks, cum_decay, seg_blocks, seg_before, entering))
        y_blocks = y_intra + y_state
        x_heads = x_conv.reshape(tok_rows, part_heads, HEAD_DIM).astype(jnp.float32)
        skip = pick(skip_d, 0, piece)
        y_total = y_blocks.reshape(tok_rows, part_heads, HEAD_DIM) + skip[None, :, None] * x_heads
        gate = pick(gate_z, 1, piece).astype(jnp.float32)
        gated = y_total.reshape(tok_rows, part_channels) * jax.nn.silu(gate)
        gated_parts.append(gated)
        square_parts.append(jnp.sum(gated * gated, axis=1))
    local_sq = square_parts[0]
    for more in square_parts[1:]:
        local_sq = local_sq + more
    total_sq = lax.psum(local_sq, "tp")
    scale = lax.rsqrt(total_sq / INNER + epsilon)
    outs = [
        (gated * scale[:, None] * pick(norm_gain, 0, piece).astype(jnp.float32)).astype(jnp.bfloat16)
        for piece, gated in enumerate(gated_parts)
    ]
    if pieces == 1:
        return outs[0]
    joined = jnp.stack([o.reshape(tok_rows, 2, part_channels // 2) for o in outs], axis=2)
    return joined.reshape(tok_rows, channels)


def cores_paired(mesh):
    row = mesh.devices[:, 0] if mesh.devices.ndim == 2 else mesh.devices.reshape(-1)
    if len(row) % 2:
        return False
    try:
        for lo, hi in zip(row[0::2], row[1::2]):
            if tuple(lo.coords) != tuple(hi.coords) or lo.core_on_chip == hi.core_on_chip:
                return False
    except AttributeError:
        return False
    return True


def solution(mesh):
    in_specs = (
        P("ctx", "tp"),
        P("ctx", "tp"),
        P("ctx", None),
        P("tp", "ctx"),
        P("tp"),
        P("tp"),
        P("tp"),
        P(None, "tp"),
        P("tp"),
        P(),
        P(),
        P("tp"),
        P("ctx"),
    )
    out_specs = P("ctx", "tp")
    paired = cores_paired(mesh)
    return jax.shard_map(functools.partial(local, paired), mesh=mesh, in_specs=in_specs, out_specs=out_specs, check_vma=False)
```

```python
import functools

import jax
import jax.numpy as jnp
from jax import lax
from jax.sharding import PartitionSpec as P

HEAD_DIM = 64
STATE = 128
GROUP = 256
CONV = 4
INNER = 8192


epsilon = 1e-05


def passed_along(value, axis, steps):
    count = lax.axis_size(axis)
    leading, last = (max(0, -steps), min(count, count - steps))
    return lax.ppermute(value, axis, [(source, source + steps) for source in range(leading, last)])


def causal_conv(rim_vals, values, rim_segment, segment, weight, offset_bias):
    extended = jnp.concatenate([rim_vals, values], axis=0)
    ext_segment = jnp.concatenate([rim_segment, segment], axis=0)
    length = values.shape[0]
    summed = jnp.zeros(values.shape, jnp.float32) + offset_bias.astype(jnp.float32)
    for offset in range(CONV):
        visible = (ext_segment[offset : offset + length] == segment).astype(jnp.float32)
        summed = (
            summed
            + weight[offset].astype(jnp.float32)
            * extended[offset : offset + length].astype(jnp.float32)
            * visible[:, None]
        )
    return jax.nn.silu(summed).astype(jnp.bfloat16)


def mixing_part(x_group, b_group, c_group, step_size, cum_decay, segment):
    places = jnp.arange(segment.shape[0])
    visible = jnp.logical_and(
        places[:, None] >= places[None, :], segment[:, None] == segment[None, :]
    )
    scores = jnp.einsum("in,jn->ij", c_group, b_group, preferred_element_type=jnp.float32)
    exponent = jnp.where(visible[None], cum_decay[:, :, None] - cum_decay[:, None, :], -jnp.inf)
    mixing = (scores[None] * jnp.exp(exponent) * step_size[:, None, :]).astype(jnp.bfloat16)
    return jnp.einsum("hij,jhp->ihp", mixing, x_group, preferred_element_type=jnp.float32)


def state_part(x_group, b_group, step_size, cum_decay, segment, seg_before):
    closing = cum_decay[:, -1:]
    tail_mask = (segment == segment[-1]).astype(jnp.float32)
    factor = jnp.exp(closing - cum_decay) * step_size * tail_mask[None]
    weighted = (b_group.astype(jnp.float32)[None] * factor[:, :, None]).astype(jnp.bfloat16)
    block_state = jnp.einsum("hjn,jhp->hpn", weighted, x_group, preferred_element_type=jnp.float32)
    transmit = jnp.exp(cum_decay[:, -1]) * (segment[-1] == seg_before).astype(jnp.float32)
    return (block_state, transmit)


def entry_part(c_group, entering, cum_decay, segment, seg_before):
    packed = entering.astype(jnp.bfloat16)
    reach = jnp.exp(cum_decay) * (segment == seg_before).astype(jnp.float32)[None]
    product = jnp.einsum("in,hpn->ihp", c_group, packed, preferred_element_type=jnp.float32)
    return product * jnp.transpose(reach)[:, :, None]


def shifted(value, axis, steps, count):
    return lax.ppermute(value, axis, [(s, s + steps) for s in range(count - steps)])


def scan_round(transmit, state, axis, shift, count):
    far_t, far_s = shifted((transmit, state), axis, shift, count)
    return transmit * far_t, transmit[:, None, None] * far_s + state


def scan_rounds(carry, axis, stride, span, count, far):
    near, needed, rider = far
    carry, rider = lax.optimization_barrier((carry, rider))
    far[2] = rider
    transmit, state = shifted(carry, axis, stride, count)
    covered = 1
    while covered < min(span - 1, near):
        transmit, state = scan_round(transmit, state, axis, stride * covered, count)
        covered *= 2
    if covered < span - 1:

        def rest(carried):
            t, s = carried
            reach = covered
            while reach < span - 1:
                t, s = scan_round(t, s, axis, stride * reach, count)
                reach *= 2
            return t, s

        transmit, state = lax.cond(needed, rest, lambda carried: carried, (transmit, state))
    return state


def gather_round(value, axis, size):
    count = lax.axis_size(axis)
    if count & (count - 1):
        return lax.all_gather(value, axis, tiled=True) if size == 1 else value
    if size >= count:
        return value
    place = lax.axis_index(axis)
    other = lax.ppermute(value, axis, [(s, s ^ size) for s in range(count)])
    return jnp.where(
        (place & size) == 0,
        jnp.concatenate([value, other]),
        jnp.concatenate([other, value]),
    )


def gather_rounds(value, axis, first, last):
    size = 1 << first
    while size < (1 << last):
        value = gather_round(value, axis, size)
        size *= 2
    return value


def long_runs(ids, paired, tok_rows):
    count = lax.axis_size("ctx")
    longest = (count * tok_rows // 4 - 1) // tok_rows
    group = 2 if paired else 1
    near = 1
    while near * group <= longest:
        near *= 2
    window = near * group
    joined = jnp.concatenate([jnp.zeros((1,), jnp.int32), (ids[1:] == ids[:-1]).astype(jnp.int32)])
    if window > count:
        return near, jnp.zeros((), jnp.bool_)
    breaks = jnp.cumsum(1 - joined)
    ahead = jnp.concatenate([jnp.zeros((1,), jnp.int32), breaks[:-window]])
    return near, jnp.any(breaks[window - 1 :] - ahead == 0)


def blockwise(f, items):
    if jax.tree.leaves(items)[0].shape[0] == 1:
        out = f(jax.tree.map(lambda a: a[0], items))
        return jax.tree.map(lambda a: a[None], out)
    return lax.map(f, items)


def device_entry(dev_transmit, dev_state, paired, far):
    count = lax.axis_size("ctx")
    if not paired:
        return scan_rounds((dev_transmit, dev_state), "ctx", 1, count, count, far)
    heads = dev_state.shape[0]
    half = heads // 2
    core = lax.axis_index("ctx") % 2
    swap = [(s, s ^ 1) for s in range(count)]
    own_lo = core * half
    give = lax.dynamic_slice_in_dim(dev_state, half - own_lo, half, 0)
    other_t, other_s = lax.ppermute((dev_transmit, give), "ctx", swap)
    mine_s = lax.dynamic_slice_in_dim(dev_state, own_lo, half, 0)
    mine_t = lax.dynamic_slice_in_dim(dev_transmit, own_lo, half, 0)
    peer_t = lax.dynamic_slice_in_dim(other_t, own_lo, half, 0)
    first = core == 0
    chip_s = jnp.where(first, peer_t[:, None, None] * mine_s + other_s, mine_t[:, None, None] * other_s + mine_s)
    chip_t = mine_t * peer_t
    entering = scan_rounds((chip_t, chip_s), "ctx", 2, count // 2, count, far)
    lead_t = jnp.where(first, mine_t, peer_t)
    lead_s = jnp.where(first, mine_s, other_s)
    second = lead_t[:, None, None] * entering + lead_s
    back = lax.ppermute(jnp.where(first, second, entering), "ctx", swap)
    mine = jnp.where(first, entering, second)
    low = jnp.where(first, mine, back)
    high = jnp.where(first, back, mine)
    return jnp.concatenate([low, high], axis=0)


def chain_states(block_states, transmits, paired, far):

    def advance(carried, item):
        passing, state_now = carried
        transmit, block_state = item
        return (
            (passing * transmit, transmit[:, None, None] * state_now + block_state),
            (passing, state_now),
        )

    start = (jnp.ones_like(transmits[0]), jnp.zeros_like(block_states[0]))
    finals, befores = lax.scan(advance, start, (transmits, block_states))
    entering_dev = device_entry(finals[0], finals[1], paired, far)
    return befores[0][:, :, None, None] * entering_dev[None] + befores[1]


def local(
    paired,
    x_in,
    gate_z,
    bc_in,
    dt_raw,
    dt_bias,
    a_rate,
    skip_d,
    conv_x_w,
    conv_x_b,
    conv_bc_w,
    conv_bc_b,
    norm_gain,
    segment_ids,
):
    tok_rows = x_in.shape[0]
    channels = x_in.shape[1]
    head_count = dt_raw.shape[0]
    block_count = tok_rows // GROUP
    rim_rows = CONV - 1
    bc_width = bc_in.shape[1]
    rims = passed_along(
        jnp.concatenate(
            [
                x_in[tok_rows - rim_rows :],
                bc_in[tok_rows - rim_rows :],
                segment_ids[tok_rows - rim_rows :, None].astype(jnp.bfloat16),
            ],
            axis=1,
        ),
        "ctx",
        1,
    )
    rim_x = rims[:, :channels]
    rim_bc = rims[:, channels : channels + bc_width]
    rim_segment = rims[:, channels + bc_width].astype(jnp.int32)
    ids = gather_rounds(segment_ids[tok_rows - 1 :], "ctx", 0, 2)
    ids, rim_x = lax.optimization_barrier((ids, rim_x))
    pieces = 2 if head_count % 4 == 0 else 1

    def pick(a, axis, piece):
        if pieces == 1:
            return a
        size = a.shape[axis] // pieces
        return lax.slice_in_dim(a, piece * size, (piece + 1) * size, axis=axis)

    bc_conv = causal_conv(rim_bc, bc_in, rim_segment, segment_ids, conv_bc_w, conv_bc_b)
    step_size = jax.nn.softplus(dt_raw + dt_bias[:, None])
    log_decay = -step_size * a_rate[:, None]
    seg_blocks = segment_ids.reshape(block_count, GROUP)
    seg_before = jnp.concatenate([rim_segment[rim_rows - 1 :], seg_blocks[:-1, -1]])
    b_blocks = bc_conv[:, :STATE].reshape(block_count, GROUP, STATE)
    c_blocks = bc_conv[:, STATE:].reshape(block_count, GROUP, STATE)
    part_heads = head_count // pieces
    part_channels = channels // pieces

    def state_of(item):
        x_group, b_group, steps_here, decay_here, segment, before = item
        return state_part(x_group, b_group, steps_here, decay_here, segment, before)

    def intra_of(item):
        x_group, b_group, c_group, steps_here, decay_here, segment = item
        return mixing_part(x_group, b_group, c_group, steps_here, decay_here, segment)

    def enter_of(item):
        c_group, decay_here, segment, before, entering_here = item
        return entry_part(c_group, entering_here, decay_here, segment, before)

    gated_parts = []
    square_parts = []
    for piece in range(pieces):
        x_conv = causal_conv(
            pick(rim_x, 1, piece),
            pick(x_in, 1, piece),
            rim_segment,
            segment_ids,
            pick(conv_x_w, 1, piece),
            pick(conv_x_b, 0, piece),
        )
        if piece == 0:
            ids = gather_rounds(ids, "ctx", 2, 4)
            ids, x_conv = lax.optimization_barrier((ids, x_conv))
        steps = pick(step_size, 0, piece)
        decays = pick(log_decay, 0, piece)
        cum_decay = jnp.transpose(
            jnp.cumsum(decays.reshape(part_heads, block_count, GROUP), axis=2), (1, 0, 2)
        )
        step_blocks = jnp.transpose(steps.reshape(part_heads, block_count, GROUP), (1, 0, 2))
        x_blocks = x_conv.reshape(block_count, GROUP, part_heads, HEAD_DIM)
        block_states, transmits = blockwise(
            state_of, (x_blocks, b_blocks, step_blocks, cum_decay, seg_blocks, seg_before)
        )
        if piece == 0:
            ids = gather_rounds(ids, "ctx", 4, lax.axis_size("ctx").bit_length())
            ids, block_states = lax.optimization_barrier((ids, block_states))
            near, needed = long_runs(ids, paired, tok_rows)
        intra_items = (x_blocks, b_blocks, c_blocks, step_blocks, cum_decay, seg_blocks)
        far = [near, needed, intra_items]
        entering = chain_states(block_states, transmits, paired, far)
        y_intra = blockwise(intra_of, far[2])
        y_state = blockwise(enter_of, (c_blocks, cum_decay, seg_blocks, seg_before, entering))
        y_blocks = y_intra + y_state
        x_heads = x_conv.reshape(tok_rows, part_heads, HEAD_DIM).astype(jnp.float32)
        skip = pick(skip_d, 0, piece)
        y_total = y_blocks.reshape(tok_rows, part_heads, HEAD_DIM) + skip[None, :, None] * x_heads
        gate = pick(gate_z, 1, piece).astype(jnp.float32)
        gated = y_total.reshape(tok_rows, part_channels) * jax.nn.silu(gate)
        gated_parts.append(gated)
        square_parts.append(jnp.sum(gated * gated, axis=1))
    local_sq = square_parts[0]
    for more in square_parts[1:]:
        local_sq = local_sq + more
    total_sq = lax.psum(local_sq, "tp")
    scale = lax.rsqrt(total_sq / INNER + epsilon)
    outs = [
        (gated * scale[:, None] * pick(norm_gain, 0, piece).astype(jnp.float32)).astype(jnp.bfloat16)
        for piece, gated in enumerate(gated_parts)
    ]
    if pieces == 1:
        return outs[0]
    return jnp.concatenate(outs, axis=1)


def cores_paired(mesh):
    row = mesh.devices[:, 0] if mesh.devices.ndim == 2 else mesh.devices.reshape(-1)
    if len(row) % 2:
        return False
    try:
        for lo, hi in zip(row[0::2], row[1::2]):
            if tuple(lo.coords) != tuple(hi.coords) or lo.core_on_chip == hi.core_on_chip:
                return False
    except AttributeError:
        return False
    return True


def solution(mesh):
    in_specs = (
        P("ctx", "tp"),
        P("ctx", "tp"),
        P("ctx", None),
        P("tp", "ctx"),
        P("tp"),
        P("tp"),
        P("tp"),
        P(None, "tp"),
        P("tp"),
        P(),
        P(),
        P("tp"),
        P("ctx"),
    )
    out_specs = P("ctx", "tp")
    paired = cores_paired(mesh)
    return jax.shard_map(functools.partial(local, paired), mesh=mesh, in_specs=in_specs, out_specs=out_specs, check_vma=False)
```

```python
import functools

import jax
import jax.numpy as jnp
from jax import lax
from jax.experimental import pallas as pl
from jax.experimental.pallas import tpu as pltpu
from jax.sharding import PartitionSpec as P

HEAD_DIM = 64
STATE = 128
GROUP = 256
CONV = 4
INNER = 8192


epsilon = 1e-05


def passed_along(value, axis, steps):
    count = lax.axis_size(axis)
    leading, last = (max(0, -steps), min(count, count - steps))
    return lax.ppermute(value, axis, [(source, source + steps) for source in range(leading, last)])


def causal_conv(rim_vals, values, rim_segment, segment, weight, offset_bias):
    extended = jnp.concatenate([rim_vals, values], axis=0)
    ext_segment = jnp.concatenate([rim_segment, segment], axis=0)
    length = values.shape[0]
    summed = jnp.zeros(values.shape, jnp.float32) + offset_bias.astype(jnp.float32)
    for offset in range(CONV):
        visible = (ext_segment[offset : offset + length] == segment).astype(jnp.float32)
        summed = (
            summed
            + weight[offset].astype(jnp.float32)
            * extended[offset : offset + length].astype(jnp.float32)
            * visible[:, None]
        )
    return jax.nn.silu(summed).astype(jnp.bfloat16)


def conv_rows_kernel(rim_ref, x_ref, w_ref, b_ref, vis_ref, o_ref):
    rows = x_ref.shape[0]
    here = x_ref[...].astype(jnp.float32)
    rim = jnp.concatenate(
        [rim_ref[...].astype(jnp.float32), jnp.zeros((rows - rim_ref.shape[0],) + here.shape[1:], jnp.float32)]
    )
    row = lax.broadcasted_iota(jnp.int32, here.shape, 0)
    summed = b_ref[...].astype(jnp.float32) + w_ref[CONV - 1 : CONV, :].astype(jnp.float32) * here
    for offset in range(CONV - 1):
        lag = CONV - 1 - offset
        early = pltpu.roll(rim, rows - offset, 0) if offset else rim
        seen = jnp.where(row < lag, early, pltpu.roll(here, lag, 0))
        summed = summed + w_ref[offset : offset + 1, :].astype(jnp.float32) * seen * vis_ref[offset]
    o_ref[...] = jax.nn.silu(summed).astype(o_ref.dtype)


def conv_rows(rim_vals, values, rim_segment, segment, weight, offset_bias):
    rows, width = values.shape
    ext_segment = jnp.concatenate([rim_segment, segment], axis=0)
    vis = jnp.stack(
        [(ext_segment[k : k + rows] == segment).astype(jnp.float32) for k in range(CONV - 1)]
    )[:, :, None]
    rim8 = jnp.concatenate([rim_vals, jnp.zeros((8 - rim_vals.shape[0], width), rim_vals.dtype)])
    tile = min(width, 1024)
    return pl.pallas_call(
        conv_rows_kernel,
        out_shape=jax.ShapeDtypeStruct((rows, width), jnp.bfloat16),
        grid=(width // tile,),
        in_specs=[
            pl.BlockSpec((8, tile), lambda j: (0, j)),
            pl.BlockSpec((rows, tile), lambda j: (0, j)),
            pl.BlockSpec((CONV, tile), lambda j: (0, j)),
            pl.BlockSpec((1, tile), lambda j: (0, j)),
            pl.BlockSpec((CONV - 1, rows, 1), lambda j: (0, 0, 0)),
        ],
        out_specs=pl.BlockSpec((rows, tile), lambda j: (0, j)),
        cost_estimate=pl.CostEstimate(
            flops=20 * rows * width, transcendentals=rows * width, bytes_accessed=4 * rows * width
        ),
    )(rim8, values, weight, offset_bias.reshape(1, width), vis)


def mixing_part(x_group, b_group, c_group, step_size, cum_decay, segment):
    places = jnp.arange(segment.shape[0])
    visible = jnp.logical_and(
        places[:, None] >= places[None, :], segment[:, None] == segment[None, :]
    )
    scores = jnp.einsum("in,jn->ij", c_group, b_group, preferred_element_type=jnp.float32)
    exponent = jnp.where(visible[None], cum_decay[:, :, None] - cum_decay[:, None, :], -jnp.inf)
    mixing = (scores[None] * jnp.exp(exponent) * step_size[:, None, :]).astype(jnp.bfloat16)
    return jnp.einsum("hij,jhp->ihp", mixing, x_group, preferred_element_type=jnp.float32)


def state_part(x_group, b_group, step_size, cum_decay, segment, seg_before):
    closing = cum_decay[:, -1:]
    tail_mask = (segment == segment[-1]).astype(jnp.float32)
    factor = jnp.exp(closing - cum_decay) * step_size * tail_mask[None]
    weighted = (b_group.astype(jnp.float32)[None] * factor[:, :, None]).astype(jnp.bfloat16)
    block_state = jnp.einsum("hjn,jhp->hpn", weighted, x_group, preferred_element_type=jnp.float32)
    transmit = jnp.exp(cum_decay[:, -1]) * (segment[-1] == seg_before).astype(jnp.float32)
    return (block_state, transmit)


def entry_part(c_group, entering, cum_decay, segment, seg_before):
    packed = entering.astype(jnp.bfloat16)
    reach = jnp.exp(cum_decay) * (segment == seg_before).astype(jnp.float32)[None]
    product = jnp.einsum("in,hpn->ihp", c_group, packed, preferred_element_type=jnp.float32)
    return product * jnp.transpose(reach)[:, :, None]


def shifted(value, axis, steps, count):
    return lax.ppermute(value, axis, [(s, s + steps) for s in range(count - steps)])


def scan_round(transmit, state, axis, shift, count):
    far_t, far_s = shifted((transmit, state), axis, shift, count)
    return transmit * far_t, transmit[:, None, None] * far_s + state


def scan_rounds(carry, axis, stride, span, count, far):
    near, needed, rider = far
    carry, rider = lax.optimization_barrier((carry, rider))
    far[2] = rider
    transmit, state = shifted(carry, axis, stride, count)
    covered = 1
    while covered < min(span - 1, near):
        transmit, state = scan_round(transmit, state, axis, stride * covered, count)
        covered *= 2
    if covered < span - 1:

        def rest(carried):
            t, s = carried
            reach = covered
            while reach < span - 1:
                t, s = scan_round(t, s, axis, stride * reach, count)
                reach *= 2
            return t, s

        transmit, state = lax.cond(needed, rest, lambda carried: carried, (transmit, state))
    return state


def gather_round(value, axis, size):
    count = lax.axis_size(axis)
    if count & (count - 1):
        return lax.all_gather(value, axis, tiled=True) if size == 1 else value
    if size >= count:
        return value
    place = lax.axis_index(axis)
    other = lax.ppermute(value, axis, [(s, s ^ size) for s in range(count)])
    return jnp.where(
        (place & size) == 0,
        jnp.concatenate([value, other]),
        jnp.concatenate([other, value]),
    )


def gather_rounds(value, axis, first, last):
    size = 1 << first
    while size < (1 << last):
        value = gather_round(value, axis, size)
        size *= 2
    return value


def long_runs(ids, paired, tok_rows):
    count = lax.axis_size("ctx")
    longest = (count * tok_rows // 4 - 1) // tok_rows
    group = 2 if paired else 1
    near = 1
    while near * group <= longest:
        near *= 2
    window = near * group
    joined = jnp.concatenate([jnp.zeros((1,), jnp.int32), (ids[1:] == ids[:-1]).astype(jnp.int32)])
    if window > count:
        return near, jnp.zeros((), jnp.bool_)
    breaks = jnp.cumsum(1 - joined)
    ahead = jnp.concatenate([jnp.zeros((1,), jnp.int32), breaks[:-window]])
    return near, jnp.any(breaks[window - 1 :] - ahead == 0)


def blockwise(f, items):
    if jax.tree.leaves(items)[0].shape[0] == 1:
        out = f(jax.tree.map(lambda a: a[0], items))
        return jax.tree.map(lambda a: a[None], out)
    return lax.map(f, items)


def device_entry(dev_transmit, dev_state, paired, far):
    count = lax.axis_size("ctx")
    if not paired:
        return scan_rounds((dev_transmit, dev_state), "ctx", 1, count, count, far)
    heads = dev_state.shape[0]
    half = heads // 2
    core = lax.axis_index("ctx") % 2
    swap = [(s, s ^ 1) for s in range(count)]
    own_lo = core * half
    give = lax.dynamic_slice_in_dim(dev_state, half - own_lo, half, 0)
    other_t, other_s = lax.ppermute((dev_transmit, give), "ctx", swap)
    mine_s = lax.dynamic_slice_in_dim(dev_state, own_lo, half, 0)
    mine_t = lax.dynamic_slice_in_dim(dev_transmit, own_lo, half, 0)
    peer_t = lax.dynamic_slice_in_dim(other_t, own_lo, half, 0)
    first = core == 0
    chip_s = jnp.where(first, peer_t[:, None, None] * mine_s + other_s, mine_t[:, None, None] * other_s + mine_s)
    chip_t = mine_t * peer_t
    entering = scan_rounds((chip_t, chip_s), "ctx", 2, count // 2, count, far)
    lead_t = jnp.where(first, mine_t, peer_t)
    lead_s = jnp.where(first, mine_s, other_s)
    second = lead_t[:, None, None] * entering + lead_s
    back = lax.ppermute(jnp.where(first, second, entering), "ctx", swap)
    mine = jnp.where(first, entering, second)
    low = jnp.where(first, mine, back)
    high = jnp.where(first, back, mine)
    return jnp.concatenate([low, high], axis=0)


def chain_states(block_states, transmits, paired, far):

    def advance(carried, item):
        passing, state_now = carried
        transmit, block_state = item
        return (
            (passing * transmit, transmit[:, None, None] * state_now + block_state),
            (passing, state_now),
        )

    start = (jnp.ones_like(transmits[0]), jnp.zeros_like(block_states[0]))
    finals, befores = lax.scan(advance, start, (transmits, block_states))
    entering_dev = device_entry(finals[0], finals[1], paired, far)
    return befores[0][:, :, None, None] * entering_dev[None] + befores[1]


def local(
    paired,
    x_in,
    gate_z,
    bc_in,
    dt_raw,
    dt_bias,
    a_rate,
    skip_d,
    conv_x_w,
    conv_x_b,
    conv_bc_w,
    conv_bc_b,
    norm_gain,
    segment_ids,
):
    tok_rows = x_in.shape[0]
    channels = x_in.shape[1]
    head_count = dt_raw.shape[0]
    block_count = tok_rows // GROUP
    rim_rows = CONV - 1
    bc_width = bc_in.shape[1]
    rims = passed_along(
        jnp.concatenate(
            [
                x_in[tok_rows - rim_rows :],
                bc_in[tok_rows - rim_rows :],
                segment_ids[tok_rows - rim_rows :, None].astype(jnp.bfloat16),
            ],
            axis=1,
        ),
        "ctx",
        1,
    )
    rim_x = rims[:, :channels]
    rim_bc = rims[:, channels : channels + bc_width]
    rim_segment = rims[:, channels + bc_width].astype(jnp.int32)
    ids = gather_rounds(segment_ids[tok_rows - 1 :], "ctx", 0, 2)
    ids, rim_x = lax.optimization_barrier((ids, rim_x))
    x_conv = conv_rows(rim_x, x_in, rim_segment, segment_ids, conv_x_w, conv_x_b)
    ids = gather_rounds(ids, "ctx", 2, 4)
    ids, x_conv = lax.optimization_barrier((ids, x_conv))
    bc_conv = causal_conv(rim_bc, bc_in, rim_segment, segment_ids, conv_bc_w, conv_bc_b)
    step_size = jax.nn.softplus(dt_raw + dt_bias[:, None])
    log_decay = -step_size * a_rate[:, None]
    cum_decay = jnp.transpose(
        jnp.cumsum(log_decay.reshape(head_count, block_count, GROUP), axis=2), (1, 0, 2)
    )
    step_blocks = jnp.transpose(step_size.reshape(head_count, block_count, GROUP), (1, 0, 2))
    seg_blocks = segment_ids.reshape(block_count, GROUP)
    seg_before = jnp.concatenate([rim_segment[rim_rows - 1 :], seg_blocks[:-1, -1]])
    x_blocks = x_conv.reshape(block_count, GROUP, head_count, HEAD_DIM)
    b_blocks = bc_conv[:, :STATE].reshape(block_count, GROUP, STATE)
    c_blocks = bc_conv[:, STATE:].reshape(block_count, GROUP, STATE)

    def state_of(item):
        x_group, b_group, steps_here, decay_here, segment, before = item
        return state_part(x_group, b_group, steps_here, decay_here, segment, before)

    def intra_of(item):
        x_group, b_group, c_group, steps_here, decay_here, segment = item
        return mixing_part(x_group, b_group, c_group, steps_here, decay_here, segment)

    block_states, transmits = blockwise(
        state_of, (x_blocks, b_blocks, step_blocks, cum_decay, seg_blocks, seg_before)
    )
    intra_items = (x_blocks, b_blocks, c_blocks, step_blocks, cum_decay, seg_blocks)
    ids = gather_rounds(ids, "ctx", 4, lax.axis_size("ctx").bit_length())
    ids, block_states = lax.optimization_barrier((ids, block_states))
    far = [*long_runs(ids, paired, tok_rows), intra_items]
    entering = chain_states(block_states, transmits, paired, far)
    y_intra = blockwise(intra_of, far[2])

    def enter_of(item):
        c_group, decay_here, segment, before, entering_here = item
        return entry_part(c_group, entering_here, decay_here, segment, before)

    y_state = blockwise(enter_of, (c_blocks, cum_decay, seg_blocks, seg_before, entering))
    y_blocks = y_intra + y_state
    x_heads = x_conv.reshape(tok_rows, head_count, HEAD_DIM).astype(jnp.float32)
    y_total = y_blocks.reshape(tok_rows, head_count, HEAD_DIM) + skip_d[None, :, None] * x_heads
    gated = y_total.reshape(tok_rows, channels) * jax.nn.silu(gate_z.astype(jnp.float32))
    local_sq = jnp.sum(gated * gated, axis=1)
    total_sq = lax.psum(local_sq, "tp")
    scale = lax.rsqrt(total_sq / INNER + epsilon)
    return (gated * scale[:, None] * norm_gain.astype(jnp.float32)).astype(jnp.bfloat16)


def cores_paired(mesh):
    row = mesh.devices[:, 0] if mesh.devices.ndim == 2 else mesh.devices.reshape(-1)
    if len(row) % 2:
        return False
    try:
        for lo, hi in zip(row[0::2], row[1::2]):
            if tuple(lo.coords) != tuple(hi.coords) or lo.core_on_chip == hi.core_on_chip:
                return False
    except AttributeError:
        return False
    return True


def solution(mesh):
    in_specs = (
        P("ctx", "tp"),
        P("ctx", "tp"),
        P("ctx", None),
        P("tp", "ctx"),
        P("tp"),
        P("tp"),
        P("tp"),
        P(None, "tp"),
        P("tp"),
        P(),
        P(),
        P("tp"),
        P("ctx"),
    )
    out_specs = P("ctx", "tp")
    paired = cores_paired(mesh)
    return jax.shard_map(functools.partial(local, paired), mesh=mesh, in_specs=in_specs, out_specs=out_specs, check_vma=False)
```

```python
import functools

import jax
import jax.numpy as jnp
from jax import lax
from jax.experimental import pallas as pl
from jax.experimental.pallas import tpu as pltpu
from jax.sharding import PartitionSpec as P

HEAD_DIM = 64
STATE = 128
GROUP = 256
CONV = 4
INNER = 8192


epsilon = 1e-05


def passed_along(value, axis, steps):
    count = lax.axis_size(axis)
    leading, last = (max(0, -steps), min(count, count - steps))
    return lax.ppermute(value, axis, [(source, source + steps) for source in range(leading, last)])


def causal_conv(rim_vals, values, rim_segment, segment, weight, offset_bias):
    extended = jnp.concatenate([rim_vals, values], axis=0)
    ext_segment = jnp.concatenate([rim_segment, segment], axis=0)
    length = values.shape[0]
    summed = jnp.zeros(values.shape, jnp.float32) + offset_bias.astype(jnp.float32)
    for offset in range(CONV):
        visible = (ext_segment[offset : offset + length] == segment).astype(jnp.float32)
        summed = (
            summed
            + weight[offset].astype(jnp.float32)
            * extended[offset : offset + length].astype(jnp.float32)
            * visible[:, None]
        )
    return jax.nn.silu(summed).astype(jnp.bfloat16)


def conv_rows_kernel(rim_ref, x_ref, w_ref, b_ref, vis_ref, o_ref):
    rows = x_ref.shape[0]
    here = x_ref[...].astype(jnp.float32)
    rim = jnp.concatenate(
        [rim_ref[...].astype(jnp.float32), jnp.zeros((rows - rim_ref.shape[0],) + here.shape[1:], jnp.float32)]
    )
    row = lax.broadcasted_iota(jnp.int32, here.shape, 0)
    summed = b_ref[...].astype(jnp.float32) + w_ref[CONV - 1 : CONV, :].astype(jnp.float32) * here
    for offset in range(CONV - 1):
        lag = CONV - 1 - offset
        early = pltpu.roll(rim, rows - offset, 0) if offset else rim
        seen = jnp.where(row < lag, early, pltpu.roll(here, lag, 0))
        summed = summed + w_ref[offset : offset + 1, :].astype(jnp.float32) * seen * vis_ref[offset]
    o_ref[...] = jnp.transpose(jax.nn.silu(summed)).astype(o_ref.dtype)


def conv_rows(rim_vals, values, rim_segment, segment, weight, offset_bias):
    rows, width = values.shape
    ext_segment = jnp.concatenate([rim_segment, segment], axis=0)
    vis = jnp.stack(
        [(ext_segment[k : k + rows] == segment).astype(jnp.float32) for k in range(CONV - 1)]
    )[:, :, None]
    rim8 = jnp.concatenate([rim_vals, jnp.zeros((8 - rim_vals.shape[0], width), rim_vals.dtype)])
    tile = min(width, 1024)
    return pl.pallas_call(
        conv_rows_kernel,
        out_shape=jax.ShapeDtypeStruct((width, rows), jnp.bfloat16),
        grid=(width // tile,),
        in_specs=[
            pl.BlockSpec((8, tile), lambda j: (0, j)),
            pl.BlockSpec((rows, tile), lambda j: (0, j)),
            pl.BlockSpec((CONV, tile), lambda j: (0, j)),
            pl.BlockSpec((1, tile), lambda j: (0, j)),
            pl.BlockSpec((CONV - 1, rows, 1), lambda j: (0, 0, 0)),
        ],
        out_specs=pl.BlockSpec((tile, rows), lambda j: (j, 0)),
        cost_estimate=pl.CostEstimate(
            flops=20 * rows * width, transcendentals=rows * width, bytes_accessed=4 * rows * width
        ),
    )(rim8, values, weight, offset_bias.reshape(1, width), vis).T


def mixing_part(x_group, b_group, c_group, step_size, cum_decay, segment):
    places = jnp.arange(segment.shape[0])
    visible = jnp.logical_and(
        places[:, None] >= places[None, :], segment[:, None] == segment[None, :]
    )
    scores = jnp.einsum("in,jn->ij", c_group, b_group, preferred_element_type=jnp.float32)
    exponent = jnp.where(visible[None], cum_decay[:, :, None] - cum_decay[:, None, :], -jnp.inf)
    mixing = (scores[None] * jnp.exp(exponent) * step_size[:, None, :]).astype(jnp.bfloat16)
    return jnp.einsum("hij,jhp->ihp", mixing, x_group, preferred_element_type=jnp.float32)


def state_part(x_group, b_group, step_size, cum_decay, segment, seg_before):
    closing = cum_decay[:, -1:]
    tail_mask = (segment == segment[-1]).astype(jnp.float32)
    factor = jnp.exp(closing - cum_decay) * step_size * tail_mask[None]
    weighted = (b_group.astype(jnp.float32)[None] * factor[:, :, None]).astype(jnp.bfloat16)
    block_state = jnp.einsum("hjn,jhp->hpn", weighted, x_group, preferred_element_type=jnp.float32)
    transmit = jnp.exp(cum_decay[:, -1]) * (segment[-1] == seg_before).astype(jnp.float32)
    return (block_state, transmit)


def entry_part(c_group, entering, cum_decay, segment, seg_before):
    packed = entering.astype(jnp.bfloat16)
    reach = jnp.exp(cum_decay) * (segment == seg_before).astype(jnp.float32)[None]
    product = jnp.einsum("in,hpn->ihp", c_group, packed, preferred_element_type=jnp.float32)
    return product * jnp.transpose(reach)[:, :, None]


def shifted(value, axis, steps, count):
    return lax.ppermute(value, axis, [(s, s + steps) for s in range(count - steps)])


def scan_round(transmit, state, axis, shift, count):
    far_t, far_s = shifted((transmit, state), axis, shift, count)
    return transmit * far_t, transmit[:, None, None] * far_s + state


def scan_rounds(carry, axis, stride, span, count, far):
    near, needed, rider = far
    carry, rider = lax.optimization_barrier((carry, rider))
    far[2] = rider
    transmit, state = shifted(carry, axis, stride, count)
    covered = 1
    while covered < min(span - 1, near):
        transmit, state = scan_round(transmit, state, axis, stride * covered, count)
        covered *= 2
    if covered < span - 1:

        def rest(carried):
            t, s = carried
            reach = covered
            while reach < span - 1:
                t, s = scan_round(t, s, axis, stride * reach, count)
                reach *= 2
            return t, s

        transmit, state = lax.cond(needed, rest, lambda carried: carried, (transmit, state))
    return state


def gather_round(value, axis, size):
    count = lax.axis_size(axis)
    if count & (count - 1):
        return lax.all_gather(value, axis, tiled=True) if size == 1 else value
    if size >= count:
        return value
    place = lax.axis_index(axis)
    other = lax.ppermute(value, axis, [(s, s ^ size) for s in range(count)])
    return jnp.where(
        (place & size) == 0,
        jnp.concatenate([value, other]),
        jnp.concatenate([other, value]),
    )


def gather_rounds(value, axis, first, last):
    size = 1 << first
    while size < (1 << last):
        value = gather_round(value, axis, size)
        size *= 2
    return value


def long_runs(ids, paired, tok_rows):
    count = lax.axis_size("ctx")
    longest = (count * tok_rows // 4 - 1) // tok_rows
    group = 2 if paired else 1
    near = 1
    while near * group <= longest:
        near *= 2
    window = near * group
    joined = jnp.concatenate([jnp.zeros((1,), jnp.int32), (ids[1:] == ids[:-1]).astype(jnp.int32)])
    if window > count:
        return near, jnp.zeros((), jnp.bool_)
    breaks = jnp.cumsum(1 - joined)
    ahead = jnp.concatenate([jnp.zeros((1,), jnp.int32), breaks[:-window]])
    return near, jnp.any(breaks[window - 1 :] - ahead == 0)


def blockwise(f, items):
    if jax.tree.leaves(items)[0].shape[0] == 1:
        out = f(jax.tree.map(lambda a: a[0], items))
        return jax.tree.map(lambda a: a[None], out)
    return lax.map(f, items)


def device_entry(dev_transmit, dev_state, paired, far):
    count = lax.axis_size("ctx")
    if not paired:
        return scan_rounds((dev_transmit, dev_state), "ctx", 1, count, count, far)
    heads = dev_state.shape[0]
    half = heads // 2
    core = lax.axis_index("ctx") % 2
    swap = [(s, s ^ 1) for s in range(count)]
    own_lo = core * half
    give = lax.dynamic_slice_in_dim(dev_state, half - own_lo, half, 0)
    other_t, other_s = lax.ppermute((dev_transmit, give), "ctx", swap)
    mine_s = lax.dynamic_slice_in_dim(dev_state, own_lo, half, 0)
    mine_t = lax.dynamic_slice_in_dim(dev_transmit, own_lo, half, 0)
    peer_t = lax.dynamic_slice_in_dim(other_t, own_lo, half, 0)
    first = core == 0
    chip_s = jnp.where(first, peer_t[:, None, None] * mine_s + other_s, mine_t[:, None, None] * other_s + mine_s)
    chip_t = mine_t * peer_t
    entering = scan_rounds((chip_t, chip_s), "ctx", 2, count // 2, count, far)
    lead_t = jnp.where(first, mine_t, peer_t)
    lead_s = jnp.where(first, mine_s, other_s)
    second = lead_t[:, None, None] * entering + lead_s
    back = lax.ppermute(jnp.where(first, second, entering), "ctx", swap)
    mine = jnp.where(first, entering, second)
    low = jnp.where(first, mine, back)
    high = jnp.where(first, back, mine)
    return jnp.concatenate([low, high], axis=0)


def chain_states(block_states, transmits, paired, far):

    def advance(carried, item):
        passing, state_now = carried
        transmit, block_state = item
        return (
            (passing * transmit, transmit[:, None, None] * state_now + block_state),
            (passing, state_now),
        )

    start = (jnp.ones_like(transmits[0]), jnp.zeros_like(block_states[0]))
    finals, befores = lax.scan(advance, start, (transmits, block_states))
    entering_dev = device_entry(finals[0], finals[1], paired, far)
    return befores[0][:, :, None, None] * entering_dev[None] + befores[1]


def local(
    paired,
    x_in,
    gate_z,
    bc_in,
    dt_raw,
    dt_bias,
    a_rate,
    skip_d,
    conv_x_w,
    conv_x_b,
    conv_bc_w,
    conv_bc_b,
    norm_gain,
    segment_ids,
):
    tok_rows = x_in.shape[0]
    channels = x_in.shape[1]
    head_count = dt_raw.shape[0]
    block_count = tok_rows // GROUP
    rim_rows = CONV - 1
    bc_width = bc_in.shape[1]
    rims = passed_along(
        jnp.concatenate(
            [
                x_in[tok_rows - rim_rows :],
                bc_in[tok_rows - rim_rows :],
                segment_ids[tok_rows - rim_rows :, None].astype(jnp.bfloat16),
            ],
            axis=1,
        ),
        "ctx",
        1,
    )
    rim_x = rims[:, :channels]
    rim_bc = rims[:, channels : channels + bc_width]
    rim_segment = rims[:, channels + bc_width].astype(jnp.int32)
    ids = gather_rounds(segment_ids[tok_rows - 1 :], "ctx", 0, 2)
    ids, rim_x = lax.optimization_barrier((ids, rim_x))
    x_conv = conv_rows(rim_x, x_in, rim_segment, segment_ids, conv_x_w, conv_x_b)
    ids = gather_rounds(ids, "ctx", 2, 4)
    ids, x_conv = lax.optimization_barrier((ids, x_conv))
    bc_conv = causal_conv(rim_bc, bc_in, rim_segment, segment_ids, conv_bc_w, conv_bc_b)
    step_size = jax.nn.softplus(dt_raw + dt_bias[:, None])
    log_decay = -step_size * a_rate[:, None]
    cum_decay = jnp.transpose(
        jnp.cumsum(log_decay.reshape(head_count, block_count, GROUP), axis=2), (1, 0, 2)
    )
    step_blocks = jnp.transpose(step_size.reshape(head_count, block_count, GROUP), (1, 0, 2))
    seg_blocks = segment_ids.reshape(block_count, GROUP)
    seg_before = jnp.concatenate([rim_segment[rim_rows - 1 :], seg_blocks[:-1, -1]])
    x_blocks = x_conv.reshape(block_count, GROUP, head_count, HEAD_DIM)
    b_blocks = bc_conv[:, :STATE].reshape(block_count, GROUP, STATE)
    c_blocks = bc_conv[:, STATE:].reshape(block_count, GROUP, STATE)

    def state_of(item):
        x_group, b_group, steps_here, decay_here, segment, before = item
        return state_part(x_group, b_group, steps_here, decay_here, segment, before)

    def intra_of(item):
        x_group, b_group, c_group, steps_here, decay_here, segment = item
        return mixing_part(x_group, b_group, c_group, steps_here, decay_here, segment)

    block_states, transmits = blockwise(
        state_of, (x_blocks, b_blocks, step_blocks, cum_decay, seg_blocks, seg_before)
    )
    intra_items = (x_blocks, b_blocks, c_blocks, step_blocks, cum_decay, seg_blocks)
    ids = gather_rounds(ids, "ctx", 4, lax.axis_size("ctx").bit_length())
    ids, block_states = lax.optimization_barrier((ids, block_states))
    far = [*long_runs(ids, paired, tok_rows), intra_items]
    entering = chain_states(block_states, transmits, paired, far)
    y_intra = blockwise(intra_of, far[2])

    def enter_of(item):
        c_group, decay_here, segment, before, entering_here = item
        return entry_part(c_group, entering_here, decay_here, segment, before)

    y_state = blockwise(enter_of, (c_blocks, cum_decay, seg_blocks, seg_before, entering))
    y_blocks = y_intra + y_state
    x_heads = x_conv.reshape(tok_rows, head_count, HEAD_DIM).astype(jnp.float32)
    y_total = y_blocks.reshape(tok_rows, head_count, HEAD_DIM) + skip_d[None, :, None] * x_heads
    gated = y_total.reshape(tok_rows, channels) * jax.nn.silu(gate_z.astype(jnp.float32))
    local_sq = jnp.sum(gated * gated, axis=1)
    total_sq = lax.psum(local_sq, "tp")
    scale = lax.rsqrt(total_sq / INNER + epsilon)
    return (gated * scale[:, None] * norm_gain.astype(jnp.float32)).astype(jnp.bfloat16)


def cores_paired(mesh):
    row = mesh.devices[:, 0] if mesh.devices.ndim == 2 else mesh.devices.reshape(-1)
    if len(row) % 2:
        return False
    try:
        for lo, hi in zip(row[0::2], row[1::2]):
            if tuple(lo.coords) != tuple(hi.coords) or lo.core_on_chip == hi.core_on_chip:
                return False
    except AttributeError:
        return False
    return True


def solution(mesh):
    in_specs = (
        P("ctx", "tp"),
        P("ctx", "tp"),
        P("ctx", None),
        P("tp", "ctx"),
        P("tp"),
        P("tp"),
        P("tp"),
        P(None, "tp"),
        P("tp"),
        P(),
        P(),
        P("tp"),
        P("ctx"),
    )
    out_specs = P("ctx", "tp")
    paired = cores_paired(mesh)
    return jax.shard_map(functools.partial(local, paired), mesh=mesh, in_specs=in_specs, out_specs=out_specs, check_vma=False)
```

```python
import functools

import jax
import jax.numpy as jnp
from jax import lax
from jax.experimental import pallas as pl
from jax.experimental.pallas import tpu as pltpu
from jax.sharding import PartitionSpec as P

HEAD_DIM = 64
STATE = 128
GROUP = 256
CONV = 4
INNER = 8192


epsilon = 1e-05


def passed_along(value, axis, steps):
    count = lax.axis_size(axis)
    leading, last = (max(0, -steps), min(count, count - steps))
    return lax.ppermute(value, axis, [(source, source + steps) for source in range(leading, last)])


def causal_conv(rim_vals, values, rim_segment, segment, weight, offset_bias):
    extended = jnp.concatenate([rim_vals, values], axis=0)
    ext_segment = jnp.concatenate([rim_segment, segment], axis=0)
    length = values.shape[0]
    summed = jnp.zeros(values.shape, jnp.float32) + offset_bias.astype(jnp.float32)
    for offset in range(CONV):
        visible = (ext_segment[offset : offset + length] == segment).astype(jnp.float32)
        summed = (
            summed
            + weight[offset].astype(jnp.float32)
            * extended[offset : offset + length].astype(jnp.float32)
            * visible[:, None]
        )
    return jax.nn.silu(summed).astype(jnp.bfloat16)


def conv_rows_kernel(rim_ref, x_ref, w_ref, b_ref, vis_ref, o_ref):
    rows = x_ref.shape[0]
    here = x_ref[...].astype(jnp.float32)
    rim = jnp.concatenate(
        [rim_ref[...].astype(jnp.float32), jnp.zeros((rows - rim_ref.shape[0],) + here.shape[1:], jnp.float32)]
    )
    row = lax.broadcasted_iota(jnp.int32, here.shape, 0)
    summed = b_ref[...].astype(jnp.float32) + w_ref[CONV - 1 : CONV, :].astype(jnp.float32) * here
    for offset in range(CONV - 1):
        lag = CONV - 1 - offset
        early = pltpu.roll(rim, rows - offset, 0) if offset else rim
        seen = jnp.where(row < lag, early, pltpu.roll(here, lag, 0))
        summed = summed + w_ref[offset : offset + 1, :].astype(jnp.float32) * seen * vis_ref[offset]
    o_ref[...] = jnp.transpose(jax.nn.silu(summed)).astype(o_ref.dtype)


def conv_rows(rim_vals, values, rim_segment, segment, weight, offset_bias):
    rows, width = values.shape
    ext_segment = jnp.concatenate([rim_segment, segment], axis=0)
    vis = jnp.stack(
        [(ext_segment[k : k + rows] == segment).astype(jnp.float32) for k in range(CONV - 1)]
    )[:, :, None]
    rim8 = jnp.concatenate([rim_vals, jnp.zeros((8 - rim_vals.shape[0], width), rim_vals.dtype)])
    tile = min(width, 1024)
    return pl.pallas_call(
        conv_rows_kernel,
        out_shape=jax.ShapeDtypeStruct((width, rows), jnp.bfloat16),
        grid=(width // tile,),
        in_specs=[
            pl.BlockSpec((8, tile), lambda j: (0, j)),
            pl.BlockSpec((rows, tile), lambda j: (0, j)),
            pl.BlockSpec((CONV, tile), lambda j: (0, j)),
            pl.BlockSpec((1, tile), lambda j: (0, j)),
            pl.BlockSpec((CONV - 1, rows, 1), lambda j: (0, 0, 0)),
        ],
        out_specs=pl.BlockSpec((tile, rows), lambda j: (j, 0)),
        cost_estimate=pl.CostEstimate(
            flops=20 * rows * width, transcendentals=rows * width, bytes_accessed=4 * rows * width
        ),
    )(rim8, values, weight, offset_bias.reshape(1, width), vis).T


def scale_rows_kernel(g_ref, s_ref, n_ref, o_ref):
    o_ref[...] = jnp.transpose(g_ref[...] * s_ref[...] * n_ref[...]).astype(o_ref.dtype)


def scale_rows(gated, scale, gain):
    rows, width = gated.shape
    tile = min(width, 1024)
    return pl.pallas_call(
        scale_rows_kernel,
        out_shape=jax.ShapeDtypeStruct((rows, width), jnp.bfloat16),
        grid=(width // tile,),
        in_specs=[
            pl.BlockSpec((tile, rows), lambda j: (j, 0)),
            pl.BlockSpec((1, rows), lambda j: (0, 0)),
            pl.BlockSpec((tile, 1), lambda j: (j, 0)),
        ],
        out_specs=pl.BlockSpec((rows, tile), lambda j: (0, j)),
        cost_estimate=pl.CostEstimate(flops=2 * rows * width, transcendentals=0, bytes_accessed=6 * rows * width),
    )(gated.T, scale[None, :], gain.astype(jnp.float32)[:, None])


def mixing_part(x_group, b_group, c_group, step_size, cum_decay, segment):
    places = jnp.arange(segment.shape[0])
    visible = jnp.logical_and(
        places[:, None] >= places[None, :], segment[:, None] == segment[None, :]
    )
    scores = jnp.einsum("in,jn->ij", c_group, b_group, preferred_element_type=jnp.float32)
    exponent = jnp.where(visible[None], cum_decay[:, :, None] - cum_decay[:, None, :], -jnp.inf)
    mixing = (scores[None] * jnp.exp(exponent) * step_size[:, None, :]).astype(jnp.bfloat16)
    return jnp.einsum("hij,jhp->ihp", mixing, x_group, preferred_element_type=jnp.float32)


def state_part(x_group, b_group, step_size, cum_decay, segment, seg_before):
    closing = cum_decay[:, -1:]
    tail_mask = (segment == segment[-1]).astype(jnp.float32)
    factor = jnp.exp(closing - cum_decay) * step_size * tail_mask[None]
    weighted = (b_group.astype(jnp.float32)[None] * factor[:, :, None]).astype(jnp.bfloat16)
    block_state = jnp.einsum("hjn,jhp->hpn", weighted, x_group, preferred_element_type=jnp.float32)
    transmit = jnp.exp(cum_decay[:, -1]) * (segment[-1] == seg_before).astype(jnp.float32)
    return (block_state, transmit)


def entry_part(c_group, entering, cum_decay, segment, seg_before):
    packed = entering.astype(jnp.bfloat16)
    reach = jnp.exp(cum_decay) * (segment == seg_before).astype(jnp.float32)[None]
    product = jnp.einsum("in,hpn->ihp", c_group, packed, preferred_element_type=jnp.float32)
    return product * jnp.transpose(reach)[:, :, None]


def shifted(value, axis, steps, count):
    return lax.ppermute(value, axis, [(s, s + steps) for s in range(count - steps)])


def scan_round(transmit, state, axis, shift, count):
    far_t, far_s = shifted((transmit, state), axis, shift, count)
    return transmit * far_t, transmit[:, None, None] * far_s + state


def scan_rounds(carry, axis, stride, span, count, far):
    near, needed, rider = far
    carry, rider = lax.optimization_barrier((carry, rider))
    far[2] = rider
    transmit, state = shifted(carry, axis, stride, count)
    covered = 1
    while covered < min(span - 1, near):
        transmit, state = scan_round(transmit, state, axis, stride * covered, count)
        covered *= 2
    if covered < span - 1:

        def rest(carried):
            t, s = carried
            reach = covered
            while reach < span - 1:
                t, s = scan_round(t, s, axis, stride * reach, count)
                reach *= 2
            return t, s

        transmit, state = lax.cond(needed, rest, lambda carried: carried, (transmit, state))
    return state


def gather_round(value, axis, size):
    count = lax.axis_size(axis)
    if count & (count - 1):
        return lax.all_gather(value, axis, tiled=True) if size == 1 else value
    if size >= count:
        return value
    place = lax.axis_index(axis)
    other = lax.ppermute(value, axis, [(s, s ^ size) for s in range(count)])
    return jnp.where(
        (place & size) == 0,
        jnp.concatenate([value, other]),
        jnp.concatenate([other, value]),
    )


def gather_rounds(value, axis, first, last):
    size = 1 << first
    while size < (1 << last):
        value = gather_round(value, axis, size)
        size *= 2
    return value


def long_runs(ids, paired, tok_rows):
    count = lax.axis_size("ctx")
    longest = (count * tok_rows // 4 - 1) // tok_rows
    group = 2 if paired else 1
    near = 1
    while near * group <= longest:
        near *= 2
    window = near * group
    joined = jnp.concatenate([jnp.zeros((1,), jnp.int32), (ids[1:] == ids[:-1]).astype(jnp.int32)])
    if window > count:
        return near, jnp.zeros((), jnp.bool_)
    breaks = jnp.cumsum(1 - joined)
    ahead = jnp.concatenate([jnp.zeros((1,), jnp.int32), breaks[:-window]])
    return near, jnp.any(breaks[window - 1 :] - ahead == 0)


def blockwise(f, items):
    if jax.tree.leaves(items)[0].shape[0] == 1:
        out = f(jax.tree.map(lambda a: a[0], items))
        return jax.tree.map(lambda a: a[None], out)
    return lax.map(f, items)


def device_entry(dev_transmit, dev_state, paired, far):
    count = lax.axis_size("ctx")
    if not paired:
        return scan_rounds((dev_transmit, dev_state), "ctx", 1, count, count, far)
    heads = dev_state.shape[0]
    half = heads // 2
    core = lax.axis_index("ctx") % 2
    swap = [(s, s ^ 1) for s in range(count)]
    own_lo = core * half
    give = lax.dynamic_slice_in_dim(dev_state, half - own_lo, half, 0)
    other_t, other_s = lax.ppermute((dev_transmit, give), "ctx", swap)
    mine_s = lax.dynamic_slice_in_dim(dev_state, own_lo, half, 0)
    mine_t = lax.dynamic_slice_in_dim(dev_transmit, own_lo, half, 0)
    peer_t = lax.dynamic_slice_in_dim(other_t, own_lo, half, 0)
    first = core == 0
    chip_s = jnp.where(first, peer_t[:, None, None] * mine_s + other_s, mine_t[:, None, None] * other_s + mine_s)
    chip_t = mine_t * peer_t
    entering = scan_rounds((chip_t, chip_s), "ctx", 2, count // 2, count, far)
    lead_t = jnp.where(first, mine_t, peer_t)
    lead_s = jnp.where(first, mine_s, other_s)
    second = lead_t[:, None, None] * entering + lead_s
    back = lax.ppermute(jnp.where(first, second, entering), "ctx", swap)
    mine = jnp.where(first, entering, second)
    low = jnp.where(first, mine, back)
    high = jnp.where(first, back, mine)
    return jnp.concatenate([low, high], axis=0)


def chain_states(block_states, transmits, paired, far):

    def advance(carried, item):
        passing, state_now = carried
        transmit, block_state = item
        return (
            (passing * transmit, transmit[:, None, None] * state_now + block_state),
            (passing, state_now),
        )

    start = (jnp.ones_like(transmits[0]), jnp.zeros_like(block_states[0]))
    finals, befores = lax.scan(advance, start, (transmits, block_states))
    entering_dev = device_entry(finals[0], finals[1], paired, far)
    return befores[0][:, :, None, None] * entering_dev[None] + befores[1]


def local(
    paired,
    x_in,
    gate_z,
    bc_in,
    dt_raw,
    dt_bias,
    a_rate,
    skip_d,
    conv_x_w,
    conv_x_b,
    conv_bc_w,
    conv_bc_b,
    norm_gain,
    segment_ids,
):
    tok_rows = x_in.shape[0]
    channels = x_in.shape[1]
    head_count = dt_raw.shape[0]
    block_count = tok_rows // GROUP
    rim_rows = CONV - 1
    bc_width = bc_in.shape[1]
    rims = passed_along(
        jnp.concatenate(
            [
                x_in[tok_rows - rim_rows :],
                bc_in[tok_rows - rim_rows :],
                segment_ids[tok_rows - rim_rows :, None].astype(jnp.bfloat16),
            ],
            axis=1,
        ),
        "ctx",
        1,
    )
    rim_x = rims[:, :channels]
    rim_bc = rims[:, channels : channels + bc_width]
    rim_segment = rims[:, channels + bc_width].astype(jnp.int32)
    ids = gather_rounds(segment_ids[tok_rows - 1 :], "ctx", 0, 2)
    ids, rim_x = lax.optimization_barrier((ids, rim_x))
    x_conv = conv_rows(rim_x, x_in, rim_segment, segment_ids, conv_x_w, conv_x_b)
    ids = gather_rounds(ids, "ctx", 2, 4)
    ids, x_conv = lax.optimization_barrier((ids, x_conv))
    bc_conv = causal_conv(rim_bc, bc_in, rim_segment, segment_ids, conv_bc_w, conv_bc_b)
    step_size = jax.nn.softplus(dt_raw + dt_bias[:, None])
    log_decay = -step_size * a_rate[:, None]
    cum_decay = jnp.transpose(
        jnp.cumsum(log_decay.reshape(head_count, block_count, GROUP), axis=2), (1, 0, 2)
    )
    step_blocks = jnp.transpose(step_size.reshape(head_count, block_count, GROUP), (1, 0, 2))
    seg_blocks = segment_ids.reshape(block_count, GROUP)
    seg_before = jnp.concatenate([rim_segment[rim_rows - 1 :], seg_blocks[:-1, -1]])
    x_blocks = x_conv.reshape(block_count, GROUP, head_count, HEAD_DIM)
    b_blocks = bc_conv[:, :STATE].reshape(block_count, GROUP, STATE)
    c_blocks = bc_conv[:, STATE:].reshape(block_count, GROUP, STATE)

    def state_of(item):
        x_group, b_group, steps_here, decay_here, segment, before = item
        return state_part(x_group, b_group, steps_here, decay_here, segment, before)

    def intra_of(item):
        x_group, b_group, c_group, steps_here, decay_here, segment = item
        return mixing_part(x_group, b_group, c_group, steps_here, decay_here, segment)

    block_states, transmits = blockwise(
        state_of, (x_blocks, b_blocks, step_blocks, cum_decay, seg_blocks, seg_before)
    )
    intra_items = (x_blocks, b_blocks, c_blocks, step_blocks, cum_decay, seg_blocks)
    ids = gather_rounds(ids, "ctx", 4, lax.axis_size("ctx").bit_length())
    ids, block_states = lax.optimization_barrier((ids, block_states))
    far = [*long_runs(ids, paired, tok_rows), intra_items]
    entering = chain_states(block_states, transmits, paired, far)
    y_intra = blockwise(intra_of, far[2])

    def enter_of(item):
        c_group, decay_here, segment, before, entering_here = item
        return entry_part(c_group, entering_here, decay_here, segment, before)

    y_state = blockwise(enter_of, (c_blocks, cum_decay, seg_blocks, seg_before, entering))
    y_blocks = y_intra + y_state
    x_heads = x_conv.reshape(tok_rows, head_count, HEAD_DIM).astype(jnp.float32)
    y_total = y_blocks.reshape(tok_rows, head_count, HEAD_DIM) + skip_d[None, :, None] * x_heads
    gated = y_total.reshape(tok_rows, channels) * jax.nn.silu(gate_z.astype(jnp.float32))
    local_sq = jnp.sum(gated * gated, axis=1)
    total_sq = lax.psum(local_sq, "tp")
    scale = lax.rsqrt(total_sq / INNER + epsilon)
    return scale_rows(gated, scale, norm_gain)


def cores_paired(mesh):
    row = mesh.devices[:, 0] if mesh.devices.ndim == 2 else mesh.devices.reshape(-1)
    if len(row) % 2:
        return False
    try:
        for lo, hi in zip(row[0::2], row[1::2]):
            if tuple(lo.coords) != tuple(hi.coords) or lo.core_on_chip == hi.core_on_chip:
                return False
    except AttributeError:
        return False
    return True


def solution(mesh):
    in_specs = (
        P("ctx", "tp"),
        P("ctx", "tp"),
        P("ctx", None),
        P("tp", "ctx"),
        P("tp"),
        P("tp"),
        P("tp"),
        P(None, "tp"),
        P("tp"),
        P(),
        P(),
        P("tp"),
        P("ctx"),
    )
    out_specs = P("ctx", "tp")
    paired = cores_paired(mesh)
    return jax.shard_map(functools.partial(local, paired), mesh=mesh, in_specs=in_specs, out_specs=out_specs, check_vma=False)
```

```python
import functools

import jax
import jax.numpy as jnp
from jax import lax
from jax.experimental import pallas as pl
from jax.experimental.pallas import tpu as pltpu
from jax.sharding import PartitionSpec as P

HEAD_DIM = 64
STATE = 128
GROUP = 256
CONV = 4
INNER = 8192


epsilon = 1e-05


def passed_along(value, axis, steps):
    count = lax.axis_size(axis)
    leading, last = (max(0, -steps), min(count, count - steps))
    return lax.ppermute(value, axis, [(source, source + steps) for source in range(leading, last)])


def causal_conv(rim_vals, values, rim_segment, segment, weight, offset_bias):
    extended = jnp.concatenate([rim_vals, values], axis=0)
    ext_segment = jnp.concatenate([rim_segment, segment], axis=0)
    length = values.shape[0]
    summed = jnp.zeros(values.shape, jnp.float32) + offset_bias.astype(jnp.float32)
    for offset in range(CONV):
        visible = (ext_segment[offset : offset + length] == segment).astype(jnp.float32)
        summed = (
            summed
            + weight[offset].astype(jnp.float32)
            * extended[offset : offset + length].astype(jnp.float32)
            * visible[:, None]
        )
    return jax.nn.silu(summed).astype(jnp.bfloat16)


def conv_rows_kernel(rim_ref, x_ref, w_ref, b_ref, vis_ref, o_ref):
    rows = x_ref.shape[0]
    here = x_ref[...].astype(jnp.float32)
    rim = jnp.concatenate(
        [rim_ref[...].astype(jnp.float32), jnp.zeros((rows - rim_ref.shape[0],) + here.shape[1:], jnp.float32)]
    )
    row = lax.broadcasted_iota(jnp.int32, here.shape, 0)
    summed = b_ref[...].astype(jnp.float32) + w_ref[CONV - 1 : CONV, :].astype(jnp.float32) * here
    for offset in range(CONV - 1):
        lag = CONV - 1 - offset
        early = pltpu.roll(rim, rows - offset, 0) if offset else rim
        seen = jnp.where(row < lag, early, pltpu.roll(here, lag, 0))
        summed = summed + w_ref[offset : offset + 1, :].astype(jnp.float32) * seen * vis_ref[offset]
    o_ref[...] = jnp.transpose(jax.nn.silu(summed)).astype(o_ref.dtype)


def conv_rows(rim_vals, values, rim_segment, segment, weight, offset_bias):
    rows, width = values.shape
    ext_segment = jnp.concatenate([rim_segment, segment], axis=0)
    vis = jnp.stack(
        [(ext_segment[k : k + rows] == segment).astype(jnp.float32) for k in range(CONV - 1)]
    )[:, :, None]
    rim8 = jnp.concatenate([rim_vals, jnp.zeros((8 - rim_vals.shape[0], width), rim_vals.dtype)])
    tile = min(width, 1024)
    return pl.pallas_call(
        conv_rows_kernel,
        out_shape=jax.ShapeDtypeStruct((width, rows), jnp.bfloat16),
        grid=(width // tile,),
        in_specs=[
            pl.BlockSpec((8, tile), lambda j: (0, j)),
            pl.BlockSpec((rows, tile), lambda j: (0, j)),
            pl.BlockSpec((CONV, tile), lambda j: (0, j)),
            pl.BlockSpec((1, tile), lambda j: (0, j)),
            pl.BlockSpec((CONV - 1, rows, 1), lambda j: (0, 0, 0)),
        ],
        out_specs=pl.BlockSpec((tile, rows), lambda j: (j, 0)),
        cost_estimate=pl.CostEstimate(
            flops=20 * rows * width, transcendentals=rows * width, bytes_accessed=4 * rows * width
        ),
    )(rim8, values, weight, offset_bias.reshape(1, width), vis).T


def scale_rows_kernel(g_ref, s_ref, n_ref, o_ref):
    o_ref[...] = jnp.transpose(g_ref[...] * s_ref[...] * n_ref[...]).astype(o_ref.dtype)


def scale_rows(gated, scale, gain):
    rows, width = gated.shape
    tile = min(width, 1024)
    return pl.pallas_call(
        scale_rows_kernel,
        out_shape=jax.ShapeDtypeStruct((rows, width), jnp.bfloat16),
        grid=(width // tile,),
        in_specs=[
            pl.BlockSpec((tile, rows), lambda j: (j, 0)),
            pl.BlockSpec((1, rows), lambda j: (0, 0)),
            pl.BlockSpec((tile, 1), lambda j: (j, 0)),
        ],
        out_specs=pl.BlockSpec((rows, tile), lambda j: (0, j)),
        cost_estimate=pl.CostEstimate(flops=2 * rows * width, transcendentals=0, bytes_accessed=6 * rows * width),
    )(gated.T, scale[None, :], gain.astype(jnp.float32)[:, None])


def mixing_part(x_group, b_group, c_group, step_size, cum_decay, segment):
    places = jnp.arange(segment.shape[0])
    visible = jnp.logical_and(
        places[:, None] >= places[None, :], segment[:, None] == segment[None, :]
    )
    scores = jnp.einsum("in,jn->ij", c_group, b_group, preferred_element_type=jnp.float32)
    exponent = jnp.where(visible[None], cum_decay[:, :, None] - cum_decay[:, None, :], -jnp.inf)
    mixing = (scores[None] * jnp.exp(exponent) * step_size[:, None, :]).astype(jnp.bfloat16)
    return jnp.einsum("hij,jhp->ihp", mixing, x_group, preferred_element_type=jnp.float32)


def state_part(x_group, b_group, step_size, cum_decay, segment, seg_before):
    closing = cum_decay[:, -1:]
    tail_mask = (segment == segment[-1]).astype(jnp.float32)
    factor = jnp.exp(closing - cum_decay) * step_size * tail_mask[None]
    weighted = (b_group.astype(jnp.float32)[None] * factor[:, :, None]).astype(jnp.bfloat16)
    block_state = jnp.einsum("hjn,jhp->hpn", weighted, x_group, preferred_element_type=jnp.float32)
    transmit = jnp.exp(cum_decay[:, -1]) * (segment[-1] == seg_before).astype(jnp.float32)
    return (block_state, transmit)


def entry_part(c_group, entering, cum_decay, segment, seg_before):
    packed = entering.astype(jnp.bfloat16)
    reach = jnp.exp(cum_decay) * (segment == seg_before).astype(jnp.float32)[None]
    product = jnp.einsum("in,hpn->ihp", c_group, packed, preferred_element_type=jnp.float32)
    return product * jnp.transpose(reach)[:, :, None]


def shifted(value, axis, steps, count):
    return lax.ppermute(value, axis, [(s, s + steps) for s in range(count - steps)])


def scan_round(transmit, state, axis, shift, count):
    far_t, far_s = shifted((transmit, state), axis, shift, count)
    return transmit * far_t, transmit[:, None, None] * far_s + state


def scan_rounds(carry, axis, stride, span, count, far):
    near, needed, rider, work = far
    carry, rider = lax.optimization_barrier((carry, rider))
    transmit, state = shifted(carry, axis, stride, count)
    (transmit, state), far[2] = lax.optimization_barrier(((transmit, state), work(rider)))
    covered = 1
    while covered < min(span - 1, near):
        transmit, state = scan_round(transmit, state, axis, stride * covered, count)
        covered *= 2
    if covered < span - 1:

        def rest(carried):
            t, s = carried
            reach = covered
            while reach < span - 1:
                t, s = scan_round(t, s, axis, stride * reach, count)
                reach *= 2
            return t, s

        transmit, state = lax.cond(needed, rest, lambda carried: carried, (transmit, state))
    return state


def gather_round(value, axis, size):
    count = lax.axis_size(axis)
    if count & (count - 1):
        return lax.all_gather(value, axis, tiled=True) if size == 1 else value
    if size >= count:
        return value
    place = lax.axis_index(axis)
    other = lax.ppermute(value, axis, [(s, s ^ size) for s in range(count)])
    return jnp.where(
        (place & size) == 0,
        jnp.concatenate([value, other]),
        jnp.concatenate([other, value]),
    )


def gather_rounds(value, axis, first, last):
    size = 1 << first
    while size < (1 << last):
        value = gather_round(value, axis, size)
        size *= 2
    return value


def long_runs(ids, paired, tok_rows):
    count = lax.axis_size("ctx")
    longest = (count * tok_rows // 4 - 1) // tok_rows
    group = 2 if paired else 1
    near = 1
    while near * group <= longest:
        near *= 2
    window = near * group
    joined = jnp.concatenate([jnp.zeros((1,), jnp.int32), (ids[1:] == ids[:-1]).astype(jnp.int32)])
    if window > count:
        return near, jnp.zeros((), jnp.bool_)
    breaks = jnp.cumsum(1 - joined)
    ahead = jnp.concatenate([jnp.zeros((1,), jnp.int32), breaks[:-window]])
    return near, jnp.any(breaks[window - 1 :] - ahead == 0)


def blockwise(f, items):
    if jax.tree.leaves(items)[0].shape[0] == 1:
        out = f(jax.tree.map(lambda a: a[0], items))
        return jax.tree.map(lambda a: a[None], out)
    return lax.map(f, items)


def device_entry(dev_transmit, dev_state, paired, far):
    count = lax.axis_size("ctx")
    if not paired:
        return scan_rounds((dev_transmit, dev_state), "ctx", 1, count, count, far)
    heads = dev_state.shape[0]
    half = heads // 2
    core = lax.axis_index("ctx") % 2
    swap = [(s, s ^ 1) for s in range(count)]
    own_lo = core * half
    give = lax.dynamic_slice_in_dim(dev_state, half - own_lo, half, 0)
    other_t, other_s = lax.ppermute((dev_transmit, give), "ctx", swap)
    mine_s = lax.dynamic_slice_in_dim(dev_state, own_lo, half, 0)
    mine_t = lax.dynamic_slice_in_dim(dev_transmit, own_lo, half, 0)
    peer_t = lax.dynamic_slice_in_dim(other_t, own_lo, half, 0)
    first = core == 0
    chip_s = jnp.where(first, peer_t[:, None, None] * mine_s + other_s, mine_t[:, None, None] * other_s + mine_s)
    chip_t = mine_t * peer_t
    entering = scan_rounds((chip_t, chip_s), "ctx", 2, count // 2, count, far)
    lead_t = jnp.where(first, mine_t, peer_t)
    lead_s = jnp.where(first, mine_s, other_s)
    second = lead_t[:, None, None] * entering + lead_s
    back = lax.ppermute(jnp.where(first, second, entering), "ctx", swap)
    mine = jnp.where(first, entering, second)
    low = jnp.where(first, mine, back)
    high = jnp.where(first, back, mine)
    return jnp.concatenate([low, high], axis=0)


def chain_states(block_states, transmits, paired, far):

    def advance(carried, item):
        passing, state_now = carried
        transmit, block_state = item
        return (
            (passing * transmit, transmit[:, None, None] * state_now + block_state),
            (passing, state_now),
        )

    start = (jnp.ones_like(transmits[0]), jnp.zeros_like(block_states[0]))
    finals, befores = lax.scan(advance, start, (transmits, block_states))
    entering_dev = device_entry(finals[0], finals[1], paired, far)
    return befores[0][:, :, None, None] * entering_dev[None] + befores[1]


def local(
    paired,
    x_in,
    gate_z,
    bc_in,
    dt_raw,
    dt_bias,
    a_rate,
    skip_d,
    conv_x_w,
    conv_x_b,
    conv_bc_w,
    conv_bc_b,
    norm_gain,
    segment_ids,
):
    tok_rows = x_in.shape[0]
    channels = x_in.shape[1]
    head_count = dt_raw.shape[0]
    block_count = tok_rows // GROUP
    rim_rows = CONV - 1
    bc_width = bc_in.shape[1]
    rims = passed_along(
        jnp.concatenate(
            [
                x_in[tok_rows - rim_rows :],
                bc_in[tok_rows - rim_rows :],
                segment_ids[tok_rows - rim_rows :, None].astype(jnp.bfloat16),
            ],
            axis=1,
        ),
        "ctx",
        1,
    )
    rim_x = rims[:, :channels]
    rim_bc = rims[:, channels : channels + bc_width]
    rim_segment = rims[:, channels + bc_width].astype(jnp.int32)
    ids = gather_rounds(segment_ids[tok_rows - 1 :], "ctx", 0, 2)
    ids, rim_x = lax.optimization_barrier((ids, rim_x))
    x_conv = conv_rows(rim_x, x_in, rim_segment, segment_ids, conv_x_w, conv_x_b)
    ids = gather_rounds(ids, "ctx", 2, 4)
    ids, x_conv = lax.optimization_barrier((ids, x_conv))
    bc_conv = causal_conv(rim_bc, bc_in, rim_segment, segment_ids, conv_bc_w, conv_bc_b)
    step_size = jax.nn.softplus(dt_raw + dt_bias[:, None])
    log_decay = -step_size * a_rate[:, None]
    cum_decay = jnp.transpose(
        jnp.cumsum(log_decay.reshape(head_count, block_count, GROUP), axis=2), (1, 0, 2)
    )
    step_blocks = jnp.transpose(step_size.reshape(head_count, block_count, GROUP), (1, 0, 2))
    seg_blocks = segment_ids.reshape(block_count, GROUP)
    seg_before = jnp.concatenate([rim_segment[rim_rows - 1 :], seg_blocks[:-1, -1]])
    x_blocks = x_conv.reshape(block_count, GROUP, head_count, HEAD_DIM)
    b_blocks = bc_conv[:, :STATE].reshape(block_count, GROUP, STATE)
    c_blocks = bc_conv[:, STATE:].reshape(block_count, GROUP, STATE)

    def state_of(item):
        x_group, b_group, steps_here, decay_here, segment, before = item
        return state_part(x_group, b_group, steps_here, decay_here, segment, before)

    def intra_of(item):
        x_group, b_group, c_group, steps_here, decay_here, segment = item
        return mixing_part(x_group, b_group, c_group, steps_here, decay_here, segment)

    block_states, transmits = blockwise(
        state_of, (x_blocks, b_blocks, step_blocks, cum_decay, seg_blocks, seg_before)
    )
    intra_items = (x_blocks, b_blocks, c_blocks, step_blocks, cum_decay, seg_blocks)
    ids = gather_rounds(ids, "ctx", 4, lax.axis_size("ctx").bit_length())
    ids, block_states = lax.optimization_barrier((ids, block_states))
    far = [*long_runs(ids, paired, tok_rows), intra_items, functools.partial(blockwise, intra_of)]
    entering = chain_states(block_states, transmits, paired, far)
    y_intra = far[2]

    def enter_of(item):
        c_group, decay_here, segment, before, entering_here = item
        return entry_part(c_group, entering_here, decay_here, segment, before)

    y_state = blockwise(enter_of, (c_blocks, cum_decay, seg_blocks, seg_before, entering))
    y_blocks = y_intra + y_state
    x_heads = x_conv.reshape(tok_rows, head_count, HEAD_DIM).astype(jnp.float32)
    y_total = y_blocks.reshape(tok_rows, head_count, HEAD_DIM) + skip_d[None, :, None] * x_heads
    gated = y_total.reshape(tok_rows, channels) * jax.nn.silu(gate_z.astype(jnp.float32))
    local_sq = jnp.sum(gated * gated, axis=1)
    total_sq = lax.psum(local_sq, "tp")
    scale = lax.rsqrt(total_sq / INNER + epsilon)
    return scale_rows(gated, scale, norm_gain)


def cores_paired(mesh):
    row = mesh.devices[:, 0] if mesh.devices.ndim == 2 else mesh.devices.reshape(-1)
    if len(row) % 2:
        return False
    try:
        for lo, hi in zip(row[0::2], row[1::2]):
            if tuple(lo.coords) != tuple(hi.coords) or lo.core_on_chip == hi.core_on_chip:
                return False
    except AttributeError:
        return False
    return True


def solution(mesh):
    in_specs = (
        P("ctx", "tp"),
        P("ctx", "tp"),
        P("ctx", None),
        P("tp", "ctx"),
        P("tp"),
        P("tp"),
        P("tp"),
        P(None, "tp"),
        P("tp"),
        P(),
        P(),
        P("tp"),
        P("ctx"),
    )
    out_specs = P("ctx", "tp")
    paired = cores_paired(mesh)
    return jax.shard_map(functools.partial(local, paired), mesh=mesh, in_specs=in_specs, out_specs=out_specs, check_vma=False)
```

```python
import functools

import jax
import jax.numpy as jnp
from jax import lax
from jax.experimental import pallas as pl
from jax.experimental.pallas import tpu as pltpu
from jax.sharding import PartitionSpec as P

HEAD_DIM = 64
STATE = 128
GROUP = 256
CONV = 4
INNER = 8192


epsilon = 1e-05


def passed_along(value, axis, steps):
    count = lax.axis_size(axis)
    leading, last = (max(0, -steps), min(count, count - steps))
    return lax.ppermute(value, axis, [(source, source + steps) for source in range(leading, last)])


def causal_conv(rim_vals, values, rim_segment, segment, weight, offset_bias):
    extended = jnp.concatenate([rim_vals, values], axis=0)
    ext_segment = jnp.concatenate([rim_segment, segment], axis=0)
    length = values.shape[0]
    summed = jnp.zeros(values.shape, jnp.float32) + offset_bias.astype(jnp.float32)
    for offset in range(CONV):
        visible = (ext_segment[offset : offset + length] == segment).astype(jnp.float32)
        summed = (
            summed
            + weight[offset].astype(jnp.float32)
            * extended[offset : offset + length].astype(jnp.float32)
            * visible[:, None]
        )
    return jax.nn.silu(summed).astype(jnp.bfloat16)


def conv_rows_kernel(rim_ref, x_ref, w_ref, b_ref, vis_ref, o_ref):
    rows = x_ref.shape[0]
    here = x_ref[...].astype(jnp.float32)
    rim = jnp.concatenate(
        [rim_ref[...].astype(jnp.float32), jnp.zeros((rows - rim_ref.shape[0],) + here.shape[1:], jnp.float32)]
    )
    row = lax.broadcasted_iota(jnp.int32, here.shape, 0)
    summed = b_ref[...].astype(jnp.float32) + w_ref[CONV - 1 : CONV, :].astype(jnp.float32) * here
    for offset in range(CONV - 1):
        lag = CONV - 1 - offset
        early = pltpu.roll(rim, rows - offset, 0) if offset else rim
        seen = jnp.where(row < lag, early, pltpu.roll(here, lag, 0))
        summed = summed + w_ref[offset : offset + 1, :].astype(jnp.float32) * seen * vis_ref[offset]
    o_ref[...] = jnp.transpose(jax.nn.silu(summed)).astype(o_ref.dtype)


def conv_rows(rim_vals, values, rim_segment, segment, weight, offset_bias):
    rows, width = values.shape
    ext_segment = jnp.concatenate([rim_segment, segment], axis=0)
    vis = jnp.stack(
        [(ext_segment[k : k + rows] == segment).astype(jnp.float32) for k in range(CONV - 1)]
    )[:, :, None]
    rim8 = jnp.concatenate([rim_vals, jnp.zeros((8 - rim_vals.shape[0], width), rim_vals.dtype)])
    tile = min(width, 1024)
    return pl.pallas_call(
        conv_rows_kernel,
        out_shape=jax.ShapeDtypeStruct((width, rows), jnp.bfloat16),
        grid=(width // tile,),
        in_specs=[
            pl.BlockSpec((8, tile), lambda j: (0, j)),
            pl.BlockSpec((rows, tile), lambda j: (0, j)),
            pl.BlockSpec((CONV, tile), lambda j: (0, j)),
            pl.BlockSpec((1, tile), lambda j: (0, j)),
            pl.BlockSpec((CONV - 1, rows, 1), lambda j: (0, 0, 0)),
        ],
        out_specs=pl.BlockSpec((tile, rows), lambda j: (j, 0)),
        cost_estimate=pl.CostEstimate(
            flops=20 * rows * width, transcendentals=rows * width, bytes_accessed=4 * rows * width
        ),
    )(rim8, values, weight, offset_bias.reshape(1, width), vis).T


def scale_rows_kernel(g_ref, s_ref, n_ref, o_ref):
    o_ref[...] = jnp.transpose(g_ref[...] * s_ref[...] * n_ref[...]).astype(o_ref.dtype)


def scale_rows(gated, scale, gain):
    rows, width = gated.shape
    tile = min(width, 1024)
    return pl.pallas_call(
        scale_rows_kernel,
        out_shape=jax.ShapeDtypeStruct((rows, width), jnp.bfloat16),
        grid=(width // tile,),
        in_specs=[
            pl.BlockSpec((tile, rows), lambda j: (j, 0)),
            pl.BlockSpec((1, rows), lambda j: (0, 0)),
            pl.BlockSpec((tile, 1), lambda j: (j, 0)),
        ],
        out_specs=pl.BlockSpec((rows, tile), lambda j: (0, j)),
        cost_estimate=pl.CostEstimate(flops=2 * rows * width, transcendentals=0, bytes_accessed=6 * rows * width),
    )(gated.T, scale[None, :], gain.astype(jnp.float32)[:, None])


def mixing_part(x_group, b_group, c_group, step_size, cum_decay, segment):
    places = jnp.arange(segment.shape[0])
    visible = jnp.logical_and(
        places[:, None] >= places[None, :], segment[:, None] == segment[None, :]
    )
    scores = jnp.einsum("in,jn->ij", c_group, b_group, preferred_element_type=jnp.float32)
    exponent = jnp.where(visible[None], cum_decay[:, :, None] - cum_decay[:, None, :], -jnp.inf)
    mixing = (scores[None] * jnp.exp(exponent) * step_size[:, None, :]).astype(jnp.bfloat16)
    return jnp.einsum("hij,jhp->ihp", mixing, x_group, preferred_element_type=jnp.float32)


def state_part(x_group, b_group, step_size, cum_decay, segment, seg_before):
    closing = cum_decay[:, -1:]
    tail_mask = (segment == segment[-1]).astype(jnp.float32)
    factor = jnp.exp(closing - cum_decay) * step_size * tail_mask[None]
    weighted = (b_group.astype(jnp.float32)[None] * factor[:, :, None]).astype(jnp.bfloat16)
    block_state = jnp.einsum("hjn,jhp->hpn", weighted, x_group, preferred_element_type=jnp.float32)
    transmit = jnp.exp(cum_decay[:, -1]) * (segment[-1] == seg_before).astype(jnp.float32)
    return (block_state, transmit)


def entry_part(c_group, entering, cum_decay, segment, seg_before):
    packed = entering.astype(jnp.bfloat16)
    reach = jnp.exp(cum_decay) * (segment == seg_before).astype(jnp.float32)[None]
    product = jnp.einsum("in,hpn->ihp", c_group, packed, preferred_element_type=jnp.float32)
    return product * jnp.transpose(reach)[:, :, None]


def shifted(value, axis, steps, count):
    return lax.ppermute(value, axis, [(s, s + steps) for s in range(count - steps)])


def shifted_pair(pair, axis, shift, count):
    transmit, state = pair
    heads = state.shape[0]
    packed = jnp.concatenate(
        [state.reshape(heads, -1), jnp.broadcast_to(transmit[:, None], (heads, 128))], axis=1
    )
    moved = shifted(packed, axis, shift, count)
    return moved[:, -1], moved[:, :-128].reshape(state.shape)


def scan_round(transmit, state, axis, shift, count):
    far_t, far_s = shifted_pair((transmit, state), axis, shift, count)
    return transmit * far_t, transmit[:, None, None] * far_s + state


def scan_rounds(carry, axis, stride, span, count, far):
    near, needed, rider = far
    carry, rider = lax.optimization_barrier((carry, rider))
    far[2] = rider
    transmit, state = shifted_pair(carry, axis, stride, count)
    covered = 1
    while covered < min(span - 1, near):
        transmit, state = scan_round(transmit, state, axis, stride * covered, count)
        covered *= 2
    if covered < span - 1:

        def rest(carried):
            t, s = carried
            reach = covered
            while reach < span - 1:
                t, s = scan_round(t, s, axis, stride * reach, count)
                reach *= 2
            return t, s

        transmit, state = lax.cond(needed, rest, lambda carried: carried, (transmit, state))
    return state


def gather_round(value, axis, size):
    count = lax.axis_size(axis)
    if count & (count - 1):
        return lax.all_gather(value, axis, tiled=True) if size == 1 else value
    if size >= count:
        return value
    place = lax.axis_index(axis)
    other = lax.ppermute(value, axis, [(s, s ^ size) for s in range(count)])
    return jnp.where(
        (place & size) == 0,
        jnp.concatenate([value, other]),
        jnp.concatenate([other, value]),
    )


def gather_rounds(value, axis, first, last):
    size = 1 << first
    while size < (1 << last):
        value = gather_round(value, axis, size)
        size *= 2
    return value


def long_runs(ids, paired, tok_rows):
    count = lax.axis_size("ctx")
    longest = (count * tok_rows // 4 - 1) // tok_rows
    group = 2 if paired else 1
    near = 1
    while near * group <= longest:
        near *= 2
    window = near * group
    joined = jnp.concatenate([jnp.zeros((1,), jnp.int32), (ids[1:] == ids[:-1]).astype(jnp.int32)])
    if window > count:
        return near, jnp.zeros((), jnp.bool_)
    breaks = jnp.cumsum(1 - joined)
    ahead = jnp.concatenate([jnp.zeros((1,), jnp.int32), breaks[:-window]])
    return near, jnp.any(breaks[window - 1 :] - ahead == 0)


def blockwise(f, items):
    if jax.tree.leaves(items)[0].shape[0] == 1:
        out = f(jax.tree.map(lambda a: a[0], items))
        return jax.tree.map(lambda a: a[None], out)
    return lax.map(f, items)


def device_entry(dev_transmit, dev_state, paired, far):
    count = lax.axis_size("ctx")
    if not paired:
        return scan_rounds((dev_transmit, dev_state), "ctx", 1, count, count, far)
    heads = dev_state.shape[0]
    half = heads // 2
    core = lax.axis_index("ctx") % 2
    swap = [(s, s ^ 1) for s in range(count)]
    own_lo = core * half
    give = lax.dynamic_slice_in_dim(dev_state, half - own_lo, half, 0)
    other_t, other_s = lax.ppermute((dev_transmit, give), "ctx", swap)
    mine_s = lax.dynamic_slice_in_dim(dev_state, own_lo, half, 0)
    mine_t = lax.dynamic_slice_in_dim(dev_transmit, own_lo, half, 0)
    peer_t = lax.dynamic_slice_in_dim(other_t, own_lo, half, 0)
    first = core == 0
    chip_s = jnp.where(first, peer_t[:, None, None] * mine_s + other_s, mine_t[:, None, None] * other_s + mine_s)
    chip_t = mine_t * peer_t
    entering = scan_rounds((chip_t, chip_s), "ctx", 2, count // 2, count, far)
    lead_t = jnp.where(first, mine_t, peer_t)
    lead_s = jnp.where(first, mine_s, other_s)
    second = lead_t[:, None, None] * entering + lead_s
    back = lax.ppermute(jnp.where(first, second, entering), "ctx", swap)
    mine = jnp.where(first, entering, second)
    low = jnp.where(first, mine, back)
    high = jnp.where(first, back, mine)
    return jnp.concatenate([low, high], axis=0)


def chain_states(block_states, transmits, paired, far):

    def advance(carried, item):
        passing, state_now = carried
        transmit, block_state = item
        return (
            (passing * transmit, transmit[:, None, None] * state_now + block_state),
            (passing, state_now),
        )

    start = (jnp.ones_like(transmits[0]), jnp.zeros_like(block_states[0]))
    finals, befores = lax.scan(advance, start, (transmits, block_states))
    entering_dev = device_entry(finals[0], finals[1], paired, far)
    return befores[0][:, :, None, None] * entering_dev[None] + befores[1]


def local(
    paired,
    x_in,
    gate_z,
    bc_in,
    dt_raw,
    dt_bias,
    a_rate,
    skip_d,
    conv_x_w,
    conv_x_b,
    conv_bc_w,
    conv_bc_b,
    norm_gain,
    segment_ids,
):
    tok_rows = x_in.shape[0]
    channels = x_in.shape[1]
    head_count = dt_raw.shape[0]
    block_count = tok_rows // GROUP
    rim_rows = CONV - 1
    bc_width = bc_in.shape[1]
    rims = passed_along(
        jnp.concatenate(
            [
                x_in[tok_rows - rim_rows :],
                bc_in[tok_rows - rim_rows :],
                segment_ids[tok_rows - rim_rows :, None].astype(jnp.bfloat16),
            ],
            axis=1,
        ),
        "ctx",
        1,
    )
    rim_x = rims[:, :channels]
    rim_bc = rims[:, channels : channels + bc_width]
    rim_segment = rims[:, channels + bc_width].astype(jnp.int32)
    ids = gather_rounds(segment_ids[tok_rows - 1 :], "ctx", 0, 2)
    ids, rim_x = lax.optimization_barrier((ids, rim_x))
    x_conv = conv_rows(rim_x, x_in, rim_segment, segment_ids, conv_x_w, conv_x_b)
    ids = gather_rounds(ids, "ctx", 2, 4)
    ids, x_conv = lax.optimization_barrier((ids, x_conv))
    bc_conv = causal_conv(rim_bc, bc_in, rim_segment, segment_ids, conv_bc_w, conv_bc_b)
    step_size = jax.nn.softplus(dt_raw + dt_bias[:, None])
    log_decay = -step_size * a_rate[:, None]
    cum_decay = jnp.transpose(
        jnp.cumsum(log_decay.reshape(head_count, block_count, GROUP), axis=2), (1, 0, 2)
    )
    step_blocks = jnp.transpose(step_size.reshape(head_count, block_count, GROUP), (1, 0, 2))
    seg_blocks = segment_ids.reshape(block_count, GROUP)
    seg_before = jnp.concatenate([rim_segment[rim_rows - 1 :], seg_blocks[:-1, -1]])
    x_blocks = x_conv.reshape(block_count, GROUP, head_count, HEAD_DIM)
    b_blocks = bc_conv[:, :STATE].reshape(block_count, GROUP, STATE)
    c_blocks = bc_conv[:, STATE:].reshape(block_count, GROUP, STATE)

    def state_of(item):
        x_group, b_group, steps_here, decay_here, segment, before = item
        return state_part(x_group, b_group, steps_here, decay_here, segment, before)

    def intra_of(item):
        x_group, b_group, c_group, steps_here, decay_here, segment = item
        return mixing_part(x_group, b_group, c_group, steps_here, decay_here, segment)

    block_states, transmits = blockwise(
        state_of, (x_blocks, b_blocks, step_blocks, cum_decay, seg_blocks, seg_before)
    )
    intra_items = (x_blocks, b_blocks, c_blocks, step_blocks, cum_decay, seg_blocks)
    ids = gather_rounds(ids, "ctx", 4, lax.axis_size("ctx").bit_length())
    ids, block_states = lax.optimization_barrier((ids, block_states))
    far = [*long_runs(ids, paired, tok_rows), intra_items]
    entering = chain_states(block_states, transmits, paired, far)
    y_intra = blockwise(intra_of, far[2])

    def enter_of(item):
        c_group, decay_here, segment, before, entering_here = item
        return entry_part(c_group, entering_here, decay_here, segment, before)

    y_state = blockwise(enter_of, (c_blocks, cum_decay, seg_blocks, seg_before, entering))
    y_blocks = y_intra + y_state
    x_heads = x_conv.reshape(tok_rows, head_count, HEAD_DIM).astype(jnp.float32)
    y_total = y_blocks.reshape(tok_rows, head_count, HEAD_DIM) + skip_d[None, :, None] * x_heads
    gated = y_total.reshape(tok_rows, channels) * jax.nn.silu(gate_z.astype(jnp.float32))
    local_sq = jnp.sum(gated * gated, axis=1)
    total_sq = lax.psum(local_sq, "tp")
    scale = lax.rsqrt(total_sq / INNER + epsilon)
    return scale_rows(gated, scale, norm_gain)


def cores_paired(mesh):
    row = mesh.devices[:, 0] if mesh.devices.ndim == 2 else mesh.devices.reshape(-1)
    if len(row) % 2:
        return False
    try:
        for lo, hi in zip(row[0::2], row[1::2]):
            if tuple(lo.coords) != tuple(hi.coords) or lo.core_on_chip == hi.core_on_chip:
                return False
    except AttributeError:
        return False
    return True


def solution(mesh):
    in_specs = (
        P("ctx", "tp"),
        P("ctx", "tp"),
        P("ctx", None),
        P("tp", "ctx"),
        P("tp"),
        P("tp"),
        P("tp"),
        P(None, "tp"),
        P("tp"),
        P(),
        P(),
        P("tp"),
        P("ctx"),
    )
    out_specs = P("ctx", "tp")
    paired = cores_paired(mesh)
    return jax.shard_map(functools.partial(local, paired), mesh=mesh, in_specs=in_specs, out_specs=out_specs, check_vma=False)
```

```python
import functools

import jax
import jax.numpy as jnp
from jax import lax
from jax.experimental import pallas as pl
from jax.experimental.pallas import tpu as pltpu
from jax.sharding import PartitionSpec as P

HEAD_DIM = 64
STATE = 128
GROUP = 256
CONV = 4
INNER = 8192


epsilon = 1e-05


def passed_along(value, axis, steps):
    count = lax.axis_size(axis)
    leading, last = (max(0, -steps), min(count, count - steps))
    return lax.ppermute(value, axis, [(source, source + steps) for source in range(leading, last)])


def causal_conv(rim_vals, values, rim_segment, segment, weight, offset_bias):
    extended = jnp.concatenate([rim_vals, values], axis=0)
    ext_segment = jnp.concatenate([rim_segment, segment], axis=0)
    length = values.shape[0]
    summed = jnp.zeros(values.shape, jnp.float32) + offset_bias.astype(jnp.float32)
    for offset in range(CONV):
        visible = (ext_segment[offset : offset + length] == segment).astype(jnp.float32)
        summed = (
            summed
            + weight[offset].astype(jnp.float32)
            * extended[offset : offset + length].astype(jnp.float32)
            * visible[:, None]
        )
    return jax.nn.silu(summed).astype(jnp.bfloat16)


def conv_rows_kernel(rim_ref, x_ref, w_ref, b_ref, vis_ref, o_ref):
    rows = x_ref.shape[0]
    here = x_ref[...].astype(jnp.float32)
    rim = jnp.concatenate(
        [rim_ref[...].astype(jnp.float32), jnp.zeros((rows - rim_ref.shape[0],) + here.shape[1:], jnp.float32)]
    )
    row = lax.broadcasted_iota(jnp.int32, here.shape, 0)
    summed = b_ref[...].astype(jnp.float32) + w_ref[CONV - 1 : CONV, :].astype(jnp.float32) * here
    for offset in range(CONV - 1):
        lag = CONV - 1 - offset
        early = pltpu.roll(rim, rows - offset, 0) if offset else rim
        seen = jnp.where(row < lag, early, pltpu.roll(here, lag, 0))
        summed = summed + w_ref[offset : offset + 1, :].astype(jnp.float32) * seen * vis_ref[offset]
    o_ref[...] = jnp.transpose(jax.nn.silu(summed)).astype(o_ref.dtype)


def conv_rows(rim_vals, values, rim_segment, segment, weight, offset_bias):
    rows, width = values.shape
    ext_segment = jnp.concatenate([rim_segment, segment], axis=0)
    vis = jnp.stack(
        [(ext_segment[k : k + rows] == segment).astype(jnp.float32) for k in range(CONV - 1)]
    )[:, :, None]
    rim8 = jnp.concatenate([rim_vals, jnp.zeros((8 - rim_vals.shape[0], width), rim_vals.dtype)])
    tile = min(width, 1024)
    return pl.pallas_call(
        conv_rows_kernel,
        out_shape=jax.ShapeDtypeStruct((width, rows), jnp.bfloat16),
        grid=(width // tile,),
        in_specs=[
            pl.BlockSpec((8, tile), lambda j: (0, j)),
            pl.BlockSpec((rows, tile), lambda j: (0, j)),
            pl.BlockSpec((CONV, tile), lambda j: (0, j)),
            pl.BlockSpec((1, tile), lambda j: (0, j)),
            pl.BlockSpec((CONV - 1, rows, 1), lambda j: (0, 0, 0)),
        ],
        out_specs=pl.BlockSpec((tile, rows), lambda j: (j, 0)),
        cost_estimate=pl.CostEstimate(
            flops=20 * rows * width, transcendentals=rows * width, bytes_accessed=4 * rows * width
        ),
    )(rim8, values, weight, offset_bias.reshape(1, width), vis).T


def scale_rows_kernel(g_ref, s_ref, n_ref, o_ref):
    o_ref[...] = jnp.transpose(g_ref[...] * s_ref[...] * n_ref[...]).astype(o_ref.dtype)


def scale_rows(gated, scale, gain):
    rows, width = gated.shape
    tile = min(width, 1024)
    return pl.pallas_call(
        scale_rows_kernel,
        out_shape=jax.ShapeDtypeStruct((rows, width), jnp.bfloat16),
        grid=(width // tile,),
        in_specs=[
            pl.BlockSpec((tile, rows), lambda j: (j, 0)),
            pl.BlockSpec((1, rows), lambda j: (0, 0)),
            pl.BlockSpec((tile, 1), lambda j: (j, 0)),
        ],
        out_specs=pl.BlockSpec((rows, tile), lambda j: (0, j)),
        cost_estimate=pl.CostEstimate(flops=2 * rows * width, transcendentals=0, bytes_accessed=6 * rows * width),
    )(gated.T, scale[None, :], gain.astype(jnp.float32)[:, None])


def mixing_part(x_group, b_group, c_group, step_size, cum_decay, segment):
    places = jnp.arange(segment.shape[0])
    visible = jnp.logical_and(
        places[:, None] >= places[None, :], segment[:, None] == segment[None, :]
    )
    scores = jnp.einsum("in,jn->ij", c_group, b_group, preferred_element_type=jnp.float32)
    exponent = jnp.where(visible[None], cum_decay[:, :, None] - cum_decay[:, None, :], -jnp.inf)
    mixing = (scores[None] * jnp.exp(exponent) * step_size[:, None, :]).astype(jnp.bfloat16)
    return jnp.einsum("hij,jhp->ihp", mixing, x_group, preferred_element_type=jnp.float32)


def state_part(x_group, b_group, step_size, cum_decay, segment, seg_before):
    closing = cum_decay[:, -1:]
    tail_mask = (segment == segment[-1]).astype(jnp.float32)
    factor = jnp.exp(closing - cum_decay) * step_size * tail_mask[None]
    weighted = (b_group.astype(jnp.float32)[None] * factor[:, :, None]).astype(jnp.bfloat16)
    block_state = jnp.einsum("hjn,jhp->hpn", weighted, x_group, preferred_element_type=jnp.float32)
    transmit = jnp.exp(cum_decay[:, -1]) * (segment[-1] == seg_before).astype(jnp.float32)
    return (block_state, transmit)


def entry_part(c_group, entering, cum_decay, segment, seg_before):
    packed = entering.astype(jnp.bfloat16)
    reach = jnp.exp(cum_decay) * (segment == seg_before).astype(jnp.float32)[None]
    product = jnp.einsum("in,hpn->ihp", c_group, packed, preferred_element_type=jnp.float32)
    return product * jnp.transpose(reach)[:, :, None]


def shifted(value, axis, steps, count):
    return lax.ppermute(value, axis, [(s, s + steps) for s in range(count - steps)])


def scan_round(transmit, state, axis, shift, count):
    far_t, far_s = shifted((transmit, state), axis, shift, count)
    return transmit * far_t, transmit[:, None, None] * far_s + state


def scan_rounds(carry, axis, stride, span, count, far):
    near, needed, rider = far
    carry, rider = lax.optimization_barrier((carry, rider))
    far[2] = rider
    transmit, state = shifted(carry, axis, stride, count)
    covered = 1
    while covered < min(span - 1, near):
        transmit, state = scan_round(transmit, state, axis, stride * covered, count)
        covered *= 2
    if covered < span - 1:

        def rest(carried):
            t, s = carried
            reach = covered
            while reach < span - 1:
                t, s = scan_round(t, s, axis, stride * reach, count)
                reach *= 2
            return t, s

        transmit, state = lax.cond(needed, rest, lambda carried: carried, (transmit, state))
    return state


def long_runs(ids, paired, tok_rows):
    count = lax.axis_size("ctx")
    longest = (count * tok_rows // 4 - 1) // tok_rows
    group = 2 if paired else 1
    near = 1
    while near * group <= longest:
        near *= 2
    window = near * group
    joined = jnp.concatenate([jnp.zeros((1,), jnp.int32), (ids[1:] == ids[:-1]).astype(jnp.int32)])
    if window > count:
        return near, jnp.zeros((), jnp.bool_)
    breaks = jnp.cumsum(1 - joined)
    ahead = jnp.concatenate([jnp.zeros((1,), jnp.int32), breaks[:-window]])
    return near, jnp.any(breaks[window - 1 :] - ahead == 0)


def blockwise(f, items):
    if jax.tree.leaves(items)[0].shape[0] == 1:
        out = f(jax.tree.map(lambda a: a[0], items))
        return jax.tree.map(lambda a: a[None], out)
    return lax.map(f, items)


def device_entry(dev_transmit, dev_state, paired, far):
    count = lax.axis_size("ctx")
    if not paired:
        return scan_rounds((dev_transmit, dev_state), "ctx", 1, count, count, far)
    heads = dev_state.shape[0]
    half = heads // 2
    core = lax.axis_index("ctx") % 2
    swap = [(s, s ^ 1) for s in range(count)]
    own_lo = core * half
    give = lax.dynamic_slice_in_dim(dev_state, half - own_lo, half, 0)
    other_t, other_s = lax.ppermute((dev_transmit, give), "ctx", swap)
    mine_s = lax.dynamic_slice_in_dim(dev_state, own_lo, half, 0)
    mine_t = lax.dynamic_slice_in_dim(dev_transmit, own_lo, half, 0)
    peer_t = lax.dynamic_slice_in_dim(other_t, own_lo, half, 0)
    first = core == 0
    chip_s = jnp.where(first, peer_t[:, None, None] * mine_s + other_s, mine_t[:, None, None] * other_s + mine_s)
    chip_t = mine_t * peer_t
    entering = scan_rounds((chip_t, chip_s), "ctx", 2, count // 2, count, far)
    lead_t = jnp.where(first, mine_t, peer_t)
    lead_s = jnp.where(first, mine_s, other_s)
    second = lead_t[:, None, None] * entering + lead_s
    back = lax.ppermute(jnp.where(first, second, entering), "ctx", swap)
    mine = jnp.where(first, entering, second)
    low = jnp.where(first, mine, back)
    high = jnp.where(first, back, mine)
    return jnp.concatenate([low, high], axis=0)


def chain_states(block_states, transmits, paired, far):

    def advance(carried, item):
        passing, state_now = carried
        transmit, block_state = item
        return (
            (passing * transmit, transmit[:, None, None] * state_now + block_state),
            (passing, state_now),
        )

    start = (jnp.ones_like(transmits[0]), jnp.zeros_like(block_states[0]))
    finals, befores = lax.scan(advance, start, (transmits, block_states))
    entering_dev = device_entry(finals[0], finals[1], paired, far)
    return befores[0][:, :, None, None] * entering_dev[None] + befores[1]


def local(
    paired,
    x_in,
    gate_z,
    bc_in,
    dt_raw,
    dt_bias,
    a_rate,
    skip_d,
    conv_x_w,
    conv_x_b,
    conv_bc_w,
    conv_bc_b,
    norm_gain,
    segment_ids,
):
    tok_rows = x_in.shape[0]
    channels = x_in.shape[1]
    head_count = dt_raw.shape[0]
    block_count = tok_rows // GROUP
    rim_rows = CONV - 1
    bc_width = bc_in.shape[1]
    rims = passed_along(
        jnp.concatenate(
            [
                x_in[tok_rows - rim_rows :],
                bc_in[tok_rows - rim_rows :],
                segment_ids[tok_rows - rim_rows :, None].astype(jnp.bfloat16),
            ],
            axis=1,
        ),
        "ctx",
        1,
    )
    rim_x = rims[:, :channels]
    rim_bc = rims[:, channels : channels + bc_width]
    rim_segment = rims[:, channels + bc_width].astype(jnp.int32)
    x_conv = conv_rows(rim_x, x_in, rim_segment, segment_ids, conv_x_w, conv_x_b)
    bc_conv = causal_conv(rim_bc, bc_in, rim_segment, segment_ids, conv_bc_w, conv_bc_b)
    step_size = jax.nn.softplus(dt_raw + dt_bias[:, None])
    log_decay = -step_size * a_rate[:, None]
    cum_decay = jnp.transpose(
        jnp.cumsum(log_decay.reshape(head_count, block_count, GROUP), axis=2), (1, 0, 2)
    )
    step_blocks = jnp.transpose(step_size.reshape(head_count, block_count, GROUP), (1, 0, 2))
    seg_blocks = segment_ids.reshape(block_count, GROUP)
    seg_before = jnp.concatenate([rim_segment[rim_rows - 1 :], seg_blocks[:-1, -1]])
    x_blocks = x_conv.reshape(block_count, GROUP, head_count, HEAD_DIM)
    b_blocks = bc_conv[:, :STATE].reshape(block_count, GROUP, STATE)
    c_blocks = bc_conv[:, STATE:].reshape(block_count, GROUP, STATE)

    def state_of(item):
        x_group, b_group, steps_here, decay_here, segment, before = item
        return state_part(x_group, b_group, steps_here, decay_here, segment, before)

    def intra_of(item):
        x_group, b_group, c_group, steps_here, decay_here, segment = item
        return mixing_part(x_group, b_group, c_group, steps_here, decay_here, segment)

    block_states, transmits = blockwise(
        state_of, (x_blocks, b_blocks, step_blocks, cum_decay, seg_blocks, seg_before)
    )
    intra_items = (x_blocks, b_blocks, c_blocks, step_blocks, cum_decay, seg_blocks)
    ids = lax.all_gather(segment_ids[tok_rows - 1 :], "ctx", tiled=True)
    ids, block_states = lax.optimization_barrier((ids, block_states))
    far = [*long_runs(ids, paired, tok_rows), intra_items]
    entering = chain_states(block_states, transmits, paired, far)
    y_intra = blockwise(intra_of, far[2])

    def enter_of(item):
        c_group, decay_here, segment, before, entering_here = item
        return entry_part(c_group, entering_here, decay_here, segment, before)

    y_state = blockwise(enter_of, (c_blocks, cum_decay, seg_blocks, seg_before, entering))
    y_blocks = y_intra + y_state
    x_heads = x_conv.reshape(tok_rows, head_count, HEAD_DIM).astype(jnp.float32)
    y_total = y_blocks.reshape(tok_rows, head_count, HEAD_DIM) + skip_d[None, :, None] * x_heads
    gated = y_total.reshape(tok_rows, channels) * jax.nn.silu(gate_z.astype(jnp.float32))
    local_sq = jnp.sum(gated * gated, axis=1)
    total_sq = lax.psum(local_sq, "tp")
    scale = lax.rsqrt(total_sq / INNER + epsilon)
    return scale_rows(gated, scale, norm_gain)


def cores_paired(mesh):
    row = mesh.devices[:, 0] if mesh.devices.ndim == 2 else mesh.devices.reshape(-1)
    if len(row) % 2:
        return False
    try:
        for lo, hi in zip(row[0::2], row[1::2]):
            if tuple(lo.coords) != tuple(hi.coords) or lo.core_on_chip == hi.core_on_chip:
                return False
    except AttributeError:
        return False
    return True


def solution(mesh):
    in_specs = (
        P("ctx", "tp"),
        P("ctx", "tp"),
        P("ctx", None),
        P("tp", "ctx"),
        P("tp"),
        P("tp"),
        P("tp"),
        P(None, "tp"),
        P("tp"),
        P(),
        P(),
        P("tp"),
        P("ctx"),
    )
    out_specs = P("ctx", "tp")
    paired = cores_paired(mesh)
    return jax.shard_map(functools.partial(local, paired), mesh=mesh, in_specs=in_specs, out_specs=out_specs, check_vma=False)
```

```python
import functools

import jax
import jax.numpy as jnp
from jax import lax
from jax.experimental import pallas as pl
from jax.experimental.pallas import tpu as pltpu
from jax.sharding import PartitionSpec as P

HEAD_DIM = 64
STATE = 128
GROUP = 256
CONV = 4
INNER = 8192


epsilon = 1e-05


def passed_along(value, axis, steps):
    count = lax.axis_size(axis)
    leading, last = (max(0, -steps), min(count, count - steps))
    return lax.ppermute(value, axis, [(source, source + steps) for source in range(leading, last)])


def causal_conv(rim_vals, values, rim_segment, segment, weight, offset_bias):
    extended = jnp.concatenate([rim_vals, values], axis=0)
    ext_segment = jnp.concatenate([rim_segment, segment], axis=0)
    length = values.shape[0]
    summed = jnp.zeros(values.shape, jnp.float32) + offset_bias.astype(jnp.float32)
    for offset in range(CONV):
        visible = (ext_segment[offset : offset + length] == segment).astype(jnp.float32)
        summed = (
            summed
            + weight[offset].astype(jnp.float32)
            * extended[offset : offset + length].astype(jnp.float32)
            * visible[:, None]
        )
    return jax.nn.silu(summed).astype(jnp.bfloat16)


def conv_rows_kernel(rim_ref, x_ref, w_ref, b_ref, vis_ref, o_ref):
    rows = x_ref.shape[0]
    here = x_ref[...].astype(jnp.float32)
    rim = jnp.concatenate(
        [rim_ref[...].astype(jnp.float32), jnp.zeros((rows - rim_ref.shape[0],) + here.shape[1:], jnp.float32)]
    )
    row = lax.broadcasted_iota(jnp.int32, here.shape, 0)
    summed = b_ref[...].astype(jnp.float32) + w_ref[CONV - 1 : CONV, :].astype(jnp.float32) * here
    for offset in range(CONV - 1):
        lag = CONV - 1 - offset
        early = pltpu.roll(rim, rows - offset, 0) if offset else rim
        seen = jnp.where(row < lag, early, pltpu.roll(here, lag, 0))
        summed = summed + w_ref[offset : offset + 1, :].astype(jnp.float32) * seen * vis_ref[offset]
    o_ref[...] = jnp.transpose(jax.nn.silu(summed)).astype(o_ref.dtype)


def conv_rows(rim_vals, values, rim_segment, segment, weight, offset_bias):
    rows, width = values.shape
    ext_segment = jnp.concatenate([rim_segment, segment], axis=0)
    vis = jnp.stack(
        [(ext_segment[k : k + rows] == segment).astype(jnp.float32) for k in range(CONV - 1)]
    )[:, :, None]
    rim8 = jnp.concatenate([rim_vals, jnp.zeros((8 - rim_vals.shape[0], width), rim_vals.dtype)])
    tile = min(width, 1024)
    return pl.pallas_call(
        conv_rows_kernel,
        out_shape=jax.ShapeDtypeStruct((width, rows), jnp.bfloat16),
        grid=(width // tile,),
        in_specs=[
            pl.BlockSpec((8, tile), lambda j: (0, j)),
            pl.BlockSpec((rows, tile), lambda j: (0, j)),
            pl.BlockSpec((CONV, tile), lambda j: (0, j)),
            pl.BlockSpec((1, tile), lambda j: (0, j)),
            pl.BlockSpec((CONV - 1, rows, 1), lambda j: (0, 0, 0)),
        ],
        out_specs=pl.BlockSpec((tile, rows), lambda j: (j, 0)),
        cost_estimate=pl.CostEstimate(
            flops=20 * rows * width, transcendentals=rows * width, bytes_accessed=4 * rows * width
        ),
    )(rim8, values, weight, offset_bias.reshape(1, width), vis).T


def scale_rows_kernel(g_ref, s_ref, n_ref, o_ref):
    o_ref[...] = jnp.transpose(g_ref[...] * s_ref[...] * n_ref[...]).astype(o_ref.dtype)


def scale_rows(gated, scale, gain):
    rows, width = gated.shape
    tile = min(width, 1024)
    return pl.pallas_call(
        scale_rows_kernel,
        out_shape=jax.ShapeDtypeStruct((rows, width), jnp.bfloat16),
        grid=(width // tile,),
        in_specs=[
            pl.BlockSpec((tile, rows), lambda j: (j, 0)),
            pl.BlockSpec((1, rows), lambda j: (0, 0)),
            pl.BlockSpec((tile, 1), lambda j: (j, 0)),
        ],
        out_specs=pl.BlockSpec((rows, tile), lambda j: (0, j)),
        cost_estimate=pl.CostEstimate(flops=2 * rows * width, transcendentals=0, bytes_accessed=6 * rows * width),
    )(gated.T, scale[None, :], gain.astype(jnp.float32)[:, None])


def mixing_kernel(scores_ref, seg_col_ref, seg_row_ref, cum_col_ref, cum_row_ref, step_ref, x_ref, o_ref):
    tokens = scores_ref.shape[0]
    row = lax.broadcasted_iota(jnp.int32, (tokens, tokens), 0)
    col = lax.broadcasted_iota(jnp.int32, (tokens, tokens), 1)
    visible = jnp.logical_and(row >= col, seg_col_ref[...] == seg_row_ref[...])
    scores = scores_ref[...]
    for k in range(cum_row_ref.shape[0]):
        exponent = jnp.where(visible, cum_col_ref[k] - cum_row_ref[k : k + 1, :], -jnp.inf)
        mixing = (scores * jnp.exp(exponent) * step_ref[k : k + 1, :]).astype(jnp.bfloat16)
        rows = pl.ds(k * HEAD_DIM, HEAD_DIM)
        o_ref[rows, :] = lax.dot_general(
            x_ref[rows, :], mixing, (((1,), (1,)), ((), ())), preferred_element_type=jnp.float32
        )


def mixing_part(x_group, b_group, c_group, step_size, cum_decay, segment):
    tokens, heads, width = x_group.shape
    scores = jnp.einsum("in,jn->ij", c_group, b_group, preferred_element_type=jnp.float32)
    x_t = x_group.reshape(tokens, heads * width).T
    per = 8 if heads % 8 == 0 else heads
    out = pl.pallas_call(
        mixing_kernel,
        out_shape=jax.ShapeDtypeStruct((heads * width, tokens), jnp.float32),
        grid=(heads // per,),
        in_specs=[
            pl.BlockSpec((tokens, tokens), lambda g: (0, 0)),
            pl.BlockSpec((tokens, 1), lambda g: (0, 0)),
            pl.BlockSpec((1, tokens), lambda g: (0, 0)),
            pl.BlockSpec((per, tokens, 1), lambda g: (g, 0, 0)),
            pl.BlockSpec((per, tokens), lambda g: (g, 0)),
            pl.BlockSpec((per, tokens), lambda g: (g, 0)),
            pl.BlockSpec((per * width, tokens), lambda g: (g, 0)),
        ],
        out_specs=pl.BlockSpec((per * width, tokens), lambda g: (g, 0)),
        cost_estimate=pl.CostEstimate(
            flops=2 * tokens * tokens * heads * width + 6 * tokens * tokens * heads,
            transcendentals=tokens * tokens * heads,
            bytes_accessed=6 * tokens * heads * width,
        ),
    )(
        scores,
        segment[:, None],
        segment[None, :],
        cum_decay[:, :, None],
        cum_decay,
        step_size,
        x_t,
    )
    return out.T.reshape(tokens, heads, width)


def state_part(x_group, b_group, step_size, cum_decay, segment, seg_before):
    closing = cum_decay[:, -1:]
    tail_mask = (segment == segment[-1]).astype(jnp.float32)
    factor = jnp.exp(closing - cum_decay) * step_size * tail_mask[None]
    weighted = (b_group.astype(jnp.float32)[None] * factor[:, :, None]).astype(jnp.bfloat16)
    block_state = jnp.einsum("hjn,jhp->hpn", weighted, x_group, preferred_element_type=jnp.float32)
    transmit = jnp.exp(cum_decay[:, -1]) * (segment[-1] == seg_before).astype(jnp.float32)
    return (block_state, transmit)


def entry_part(c_group, entering, cum_decay, segment, seg_before):
    packed = entering.astype(jnp.bfloat16)
    reach = jnp.exp(cum_decay) * (segment == seg_before).astype(jnp.float32)[None]
    product = jnp.einsum("in,hpn->ihp", c_group, packed, preferred_element_type=jnp.float32)
    return product * jnp.transpose(reach)[:, :, None]


def shifted(value, axis, steps, count):
    return lax.ppermute(value, axis, [(s, s + steps) for s in range(count - steps)])


def scan_round(transmit, state, axis, shift, count):
    far_t, far_s = shifted((transmit, state), axis, shift, count)
    return transmit * far_t, transmit[:, None, None] * far_s + state


def scan_rounds(carry, axis, stride, span, count, far):
    near, needed, rider = far
    carry, rider = lax.optimization_barrier((carry, rider))
    far[2] = rider
    transmit, state = shifted(carry, axis, stride, count)
    covered = 1
    while covered < min(span - 1, near):
        transmit, state = scan_round(transmit, state, axis, stride * covered, count)
        covered *= 2
    if covered < span - 1:

        def rest(carried):
            t, s = carried
            reach = covered
            while reach < span - 1:
                t, s = scan_round(t, s, axis, stride * reach, count)
                reach *= 2
            return t, s

        transmit, state = lax.cond(needed, rest, lambda carried: carried, (transmit, state))
    return state


def gather_round(value, axis, size):
    count = lax.axis_size(axis)
    if count & (count - 1):
        return lax.all_gather(value, axis, tiled=True) if size == 1 else value
    if size >= count:
        return value
    place = lax.axis_index(axis)
    other = lax.ppermute(value, axis, [(s, s ^ size) for s in range(count)])
    return jnp.where(
        (place & size) == 0,
        jnp.concatenate([value, other]),
        jnp.concatenate([other, value]),
    )


def gather_rounds(value, axis, first, last):
    size = 1 << first
    while size < (1 << last):
        value = gather_round(value, axis, size)
        size *= 2
    return value


def long_runs(ids, paired, tok_rows):
    count = lax.axis_size("ctx")
    longest = (count * tok_rows // 4 - 1) // tok_rows
    group = 2 if paired else 1
    near = 1
    while near * group <= longest:
        near *= 2
    window = near * group
    joined = jnp.concatenate([jnp.zeros((1,), jnp.int32), (ids[1:] == ids[:-1]).astype(jnp.int32)])
    if window > count:
        return near, jnp.zeros((), jnp.bool_)
    breaks = jnp.cumsum(1 - joined)
    ahead = jnp.concatenate([jnp.zeros((1,), jnp.int32), breaks[:-window]])
    return near, jnp.any(breaks[window - 1 :] - ahead == 0)


def blockwise(f, items):
    if jax.tree.leaves(items)[0].shape[0] == 1:
        out = f(jax.tree.map(lambda a: a[0], items))
        return jax.tree.map(lambda a: a[None], out)
    return lax.map(f, items)


def device_entry(dev_transmit, dev_state, paired, far):
    count = lax.axis_size("ctx")
    if not paired:
        return scan_rounds((dev_transmit, dev_state), "ctx", 1, count, count, far)
    heads = dev_state.shape[0]
    half = heads // 2
    core = lax.axis_index("ctx") % 2
    swap = [(s, s ^ 1) for s in range(count)]
    own_lo = core * half
    give = lax.dynamic_slice_in_dim(dev_state, half - own_lo, half, 0)
    other_t, other_s = lax.ppermute((dev_transmit, give), "ctx", swap)
    mine_s = lax.dynamic_slice_in_dim(dev_state, own_lo, half, 0)
    mine_t = lax.dynamic_slice_in_dim(dev_transmit, own_lo, half, 0)
    peer_t = lax.dynamic_slice_in_dim(other_t, own_lo, half, 0)
    first = core == 0
    chip_s = jnp.where(first, peer_t[:, None, None] * mine_s + other_s, mine_t[:, None, None] * other_s + mine_s)
    chip_t = mine_t * peer_t
    entering = scan_rounds((chip_t, chip_s), "ctx", 2, count // 2, count, far)
    lead_t = jnp.where(first, mine_t, peer_t)
    lead_s = jnp.where(first, mine_s, other_s)
    second = lead_t[:, None, None] * entering + lead_s
    back = lax.ppermute(jnp.where(first, second, entering), "ctx", swap)
    mine = jnp.where(first, entering, second)
    low = jnp.where(first, mine, back)
    high = jnp.where(first, back, mine)
    return jnp.concatenate([low, high], axis=0)


def chain_states(block_states, transmits, paired, far):

    def advance(carried, item):
        passing, state_now = carried
        transmit, block_state = item
        return (
            (passing * transmit, transmit[:, None, None] * state_now + block_state),
            (passing, state_now),
        )

    start = (jnp.ones_like(transmits[0]), jnp.zeros_like(block_states[0]))
    finals, befores = lax.scan(advance, start, (transmits, block_states))
    entering_dev = device_entry(finals[0], finals[1], paired, far)
    return befores[0][:, :, None, None] * entering_dev[None] + befores[1]


def local(
    paired,
    x_in,
    gate_z,
    bc_in,
    dt_raw,
    dt_bias,
    a_rate,
    skip_d,
    conv_x_w,
    conv_x_b,
    conv_bc_w,
    conv_bc_b,
    norm_gain,
    segment_ids,
):
    tok_rows = x_in.shape[0]
    channels = x_in.shape[1]
    head_count = dt_raw.shape[0]
    block_count = tok_rows // GROUP
    rim_rows = CONV - 1
    bc_width = bc_in.shape[1]
    rims = passed_along(
        jnp.concatenate(
            [
                x_in[tok_rows - rim_rows :],
                bc_in[tok_rows - rim_rows :],
                segment_ids[tok_rows - rim_rows :, None].astype(jnp.bfloat16),
            ],
            axis=1,
        ),
        "ctx",
        1,
    )
    rim_x = rims[:, :channels]
    rim_bc = rims[:, channels : channels + bc_width]
    rim_segment = rims[:, channels + bc_width].astype(jnp.int32)
    ids = gather_rounds(segment_ids[tok_rows - 1 :], "ctx", 0, 2)
    ids, rim_x = lax.optimization_barrier((ids, rim_x))
    x_conv = conv_rows(rim_x, x_in, rim_segment, segment_ids, conv_x_w, conv_x_b)
    ids = gather_rounds(ids, "ctx", 2, 4)
    ids, x_conv = lax.optimization_barrier((ids, x_conv))
    bc_conv = causal_conv(rim_bc, bc_in, rim_segment, segment_ids, conv_bc_w, conv_bc_b)
    step_size = jax.nn.softplus(dt_raw + dt_bias[:, None])
    log_decay = -step_size * a_rate[:, None]
    cum_decay = jnp.transpose(
        jnp.cumsum(log_decay.reshape(head_count, block_count, GROUP), axis=2), (1, 0, 2)
    )
    step_blocks = jnp.transpose(step_size.reshape(head_count, block_count, GROUP), (1, 0, 2))
    seg_blocks = segment_ids.reshape(block_count, GROUP)
    seg_before = jnp.concatenate([rim_segment[rim_rows - 1 :], seg_blocks[:-1, -1]])
    x_blocks = x_conv.reshape(block_count, GROUP, head_count, HEAD_DIM)
    b_blocks = bc_conv[:, :STATE].reshape(block_count, GROUP, STATE)
    c_blocks = bc_conv[:, STATE:].reshape(block_count, GROUP, STATE)

    def state_of(item):
        x_group, b_group, steps_here, decay_here, segment, before = item
        return state_part(x_group, b_group, steps_here, decay_here, segment, before)

    def intra_of(item):
        x_group, b_group, c_group, steps_here, decay_here, segment = item
        return mixing_part(x_group, b_group, c_group, steps_here, decay_here, segment)

    block_states, transmits = blockwise(
        state_of, (x_blocks, b_blocks, step_blocks, cum_decay, seg_blocks, seg_before)
    )
    intra_items = (x_blocks, b_blocks, c_blocks, step_blocks, cum_decay, seg_blocks)
    ids = gather_rounds(ids, "ctx", 4, lax.axis_size("ctx").bit_length())
    ids, block_states = lax.optimization_barrier((ids, block_states))
    far = [*long_runs(ids, paired, tok_rows), intra_items]
    entering = chain_states(block_states, transmits, paired, far)
    y_intra = blockwise(intra_of, far[2])

    def enter_of(item):
        c_group, decay_here, segment, before, entering_here = item
        return entry_part(c_group, entering_here, decay_here, segment, before)

    y_state = blockwise(enter_of, (c_blocks, cum_decay, seg_blocks, seg_before, entering))
    y_blocks = y_intra + y_state
    x_heads = x_conv.reshape(tok_rows, head_count, HEAD_DIM).astype(jnp.float32)
    y_total = y_blocks.reshape(tok_rows, head_count, HEAD_DIM) + skip_d[None, :, None] * x_heads
    gated = y_total.reshape(tok_rows, channels) * jax.nn.silu(gate_z.astype(jnp.float32))
    local_sq = jnp.sum(gated * gated, axis=1)
    total_sq = lax.psum(local_sq, "tp")
    scale = lax.rsqrt(total_sq / INNER + epsilon)
    return scale_rows(gated, scale, norm_gain)


def cores_paired(mesh):
    row = mesh.devices[:, 0] if mesh.devices.ndim == 2 else mesh.devices.reshape(-1)
    if len(row) % 2:
        return False
    try:
        for lo, hi in zip(row[0::2], row[1::2]):
            if tuple(lo.coords) != tuple(hi.coords) or lo.core_on_chip == hi.core_on_chip:
                return False
    except AttributeError:
        return False
    return True


def solution(mesh):
    in_specs = (
        P("ctx", "tp"),
        P("ctx", "tp"),
        P("ctx", None),
        P("tp", "ctx"),
        P("tp"),
        P("tp"),
        P("tp"),
        P(None, "tp"),
        P("tp"),
        P(),
        P(),
        P("tp"),
        P("ctx"),
    )
    out_specs = P("ctx", "tp")
    paired = cores_paired(mesh)
    return jax.shard_map(functools.partial(local, paired), mesh=mesh, in_specs=in_specs, out_specs=out_specs, check_vma=False)
```

```python
import functools

import jax
import jax.numpy as jnp
from jax import lax
from jax.experimental import pallas as pl
from jax.experimental.pallas import tpu as pltpu
from jax.sharding import PartitionSpec as P

HEAD_DIM = 64
STATE = 128
GROUP = 256
CONV = 4
INNER = 8192


epsilon = 1e-05


def passed_along(value, axis, steps):
    count = lax.axis_size(axis)
    leading, last = (max(0, -steps), min(count, count - steps))
    return lax.ppermute(value, axis, [(source, source + steps) for source in range(leading, last)])


def causal_conv(rim_vals, values, rim_segment, segment, weight, offset_bias):
    extended = jnp.concatenate([rim_vals, values], axis=0)
    ext_segment = jnp.concatenate([rim_segment, segment], axis=0)
    length = values.shape[0]
    summed = jnp.zeros(values.shape, jnp.float32) + offset_bias.astype(jnp.float32)
    for offset in range(CONV):
        visible = (ext_segment[offset : offset + length] == segment).astype(jnp.float32)
        summed = (
            summed
            + weight[offset].astype(jnp.float32)
            * extended[offset : offset + length].astype(jnp.float32)
            * visible[:, None]
        )
    return jax.nn.silu(summed).astype(jnp.bfloat16)


def conv_rows_kernel(rim_ref, x_ref, w_ref, b_ref, vis_ref, o_ref):
    rows = x_ref.shape[0]
    here = x_ref[...].astype(jnp.float32)
    rim = jnp.concatenate(
        [rim_ref[...].astype(jnp.float32), jnp.zeros((rows - rim_ref.shape[0],) + here.shape[1:], jnp.float32)]
    )
    row = lax.broadcasted_iota(jnp.int32, here.shape, 0)
    summed = b_ref[...].astype(jnp.float32) + w_ref[CONV - 1 : CONV, :].astype(jnp.float32) * here
    for offset in range(CONV - 1):
        lag = CONV - 1 - offset
        early = pltpu.roll(rim, rows - offset, 0) if offset else rim
        seen = jnp.where(row < lag, early, pltpu.roll(here, lag, 0))
        summed = summed + w_ref[offset : offset + 1, :].astype(jnp.float32) * seen * vis_ref[offset]
    o_ref[...] = jnp.transpose(jax.nn.silu(summed)).astype(o_ref.dtype)


def conv_rows(rim_vals, values, rim_segment, segment, weight, offset_bias):
    rows, width = values.shape
    ext_segment = jnp.concatenate([rim_segment, segment], axis=0)
    vis = jnp.stack(
        [(ext_segment[k : k + rows] == segment).astype(jnp.float32) for k in range(CONV - 1)]
    )[:, :, None]
    rim8 = jnp.concatenate([rim_vals, jnp.zeros((8 - rim_vals.shape[0], width), rim_vals.dtype)])
    tile = min(width, 1024)
    return pl.pallas_call(
        conv_rows_kernel,
        out_shape=jax.ShapeDtypeStruct((width, rows), jnp.bfloat16),
        grid=(width // tile,),
        in_specs=[
            pl.BlockSpec((8, tile), lambda j: (0, j)),
            pl.BlockSpec((rows, tile), lambda j: (0, j)),
            pl.BlockSpec((CONV, tile), lambda j: (0, j)),
            pl.BlockSpec((1, tile), lambda j: (0, j)),
            pl.BlockSpec((CONV - 1, rows, 1), lambda j: (0, 0, 0)),
        ],
        out_specs=pl.BlockSpec((tile, rows), lambda j: (j, 0)),
        cost_estimate=pl.CostEstimate(
            flops=20 * rows * width, transcendentals=rows * width, bytes_accessed=4 * rows * width
        ),
    )(rim8, values, weight, offset_bias.reshape(1, width), vis).T


def scale_rows_kernel(g_ref, s_ref, n_ref, o_ref):
    o_ref[...] = jnp.transpose(g_ref[...] * s_ref[...] * n_ref[...]).astype(o_ref.dtype)


def scale_rows(gated, scale, gain):
    rows, width = gated.shape
    tile = min(width, 1024)
    return pl.pallas_call(
        scale_rows_kernel,
        out_shape=jax.ShapeDtypeStruct((rows, width), jnp.bfloat16),
        grid=(width // tile,),
        in_specs=[
            pl.BlockSpec((tile, rows), lambda j: (j, 0)),
            pl.BlockSpec((1, rows), lambda j: (0, 0)),
            pl.BlockSpec((tile, 1), lambda j: (j, 0)),
        ],
        out_specs=pl.BlockSpec((rows, tile), lambda j: (0, j)),
        cost_estimate=pl.CostEstimate(flops=2 * rows * width, transcendentals=0, bytes_accessed=6 * rows * width),
    )(gated.T, scale[None, :], gain.astype(jnp.float32)[:, None])


def mixing_kernel(scores_ref, seg_col_ref, seg_row_ref, cum_col_ref, cum_row_ref, step_ref, x_ref, o_ref):
    tokens = scores_ref.shape[0]
    row = lax.broadcasted_iota(jnp.int32, (tokens, tokens), 0)
    col = lax.broadcasted_iota(jnp.int32, (tokens, tokens), 1)
    visible = jnp.logical_and(col >= row, seg_col_ref[...] == seg_row_ref[...])
    scores = scores_ref[...]
    for k in range(cum_row_ref.shape[0]):
        exponent = jnp.where(visible, cum_row_ref[k : k + 1, :] - cum_col_ref[k], -jnp.inf)
        mixing = (scores * jnp.exp(exponent) * step_ref[k]).astype(jnp.bfloat16)
        rows = pl.ds(k * HEAD_DIM, HEAD_DIM)
        o_ref[rows, :] = jnp.dot(x_ref[rows, :], mixing, preferred_element_type=jnp.float32)


def mixing_part(x_group, b_group, c_group, step_size, cum_decay, segment):
    tokens, heads, width = x_group.shape
    scores = jnp.einsum("jn,in->ji", b_group, c_group, preferred_element_type=jnp.float32)
    x_t = x_group.reshape(tokens, heads * width).T
    per = 8 if heads % 8 == 0 else heads
    out = pl.pallas_call(
        mixing_kernel,
        out_shape=jax.ShapeDtypeStruct((heads * width, tokens), jnp.float32),
        grid=(heads // per,),
        in_specs=[
            pl.BlockSpec((tokens, tokens), lambda g: (0, 0)),
            pl.BlockSpec((tokens, 1), lambda g: (0, 0)),
            pl.BlockSpec((1, tokens), lambda g: (0, 0)),
            pl.BlockSpec((per, tokens, 1), lambda g: (g, 0, 0)),
            pl.BlockSpec((per, tokens), lambda g: (g, 0)),
            pl.BlockSpec((per, tokens, 1), lambda g: (g, 0, 0)),
            pl.BlockSpec((per * width, tokens), lambda g: (g, 0)),
        ],
        out_specs=pl.BlockSpec((per * width, tokens), lambda g: (g, 0)),
        cost_estimate=pl.CostEstimate(
            flops=2 * tokens * tokens * heads * width + 6 * tokens * tokens * heads,
            transcendentals=tokens * tokens * heads,
            bytes_accessed=6 * tokens * heads * width,
        ),
    )(
        scores,
        segment[:, None],
        segment[None, :],
        cum_decay[:, :, None],
        cum_decay,
        step_size[:, :, None],
        x_t,
    )
    return out.T.reshape(tokens, heads, width)


def state_part(x_group, b_group, step_size, cum_decay, segment, seg_before):
    closing = cum_decay[:, -1:]
    tail_mask = (segment == segment[-1]).astype(jnp.float32)
    factor = jnp.exp(closing - cum_decay) * step_size * tail_mask[None]
    weighted = (b_group.astype(jnp.float32)[None] * factor[:, :, None]).astype(jnp.bfloat16)
    block_state = jnp.einsum("hjn,jhp->hpn", weighted, x_group, preferred_element_type=jnp.float32)
    transmit = jnp.exp(cum_decay[:, -1]) * (segment[-1] == seg_before).astype(jnp.float32)
    return (block_state, transmit)


def entry_part(c_group, entering, cum_decay, segment, seg_before):
    packed = entering.astype(jnp.bfloat16)
    reach = jnp.exp(cum_decay) * (segment == seg_before).astype(jnp.float32)[None]
    product = jnp.einsum("in,hpn->ihp", c_group, packed, preferred_element_type=jnp.float32)
    return product * jnp.transpose(reach)[:, :, None]


def shifted(value, axis, steps, count):
    return lax.ppermute(value, axis, [(s, s + steps) for s in range(count - steps)])


def scan_round(transmit, state, axis, shift, count):
    far_t, far_s = shifted((transmit, state), axis, shift, count)
    return transmit * far_t, transmit[:, None, None] * far_s + state


def scan_rounds(carry, axis, stride, span, count, far):
    near, needed, rider = far
    carry, rider = lax.optimization_barrier((carry, rider))
    far[2] = rider
    transmit, state = shifted(carry, axis, stride, count)
    covered = 1
    while covered < min(span - 1, near):
        transmit, state = scan_round(transmit, state, axis, stride * covered, count)
        covered *= 2
    if covered < span - 1:

        def rest(carried):
            t, s = carried
            reach = covered
            while reach < span - 1:
                t, s = scan_round(t, s, axis, stride * reach, count)
                reach *= 2
            return t, s

        transmit, state = lax.cond(needed, rest, lambda carried: carried, (transmit, state))
    return state


def gather_round(value, axis, size):
    count = lax.axis_size(axis)
    if count & (count - 1):
        return lax.all_gather(value, axis, tiled=True) if size == 1 else value
    if size >= count:
        return value
    place = lax.axis_index(axis)
    other = lax.ppermute(value, axis, [(s, s ^ size) for s in range(count)])
    return jnp.where(
        (place & size) == 0,
        jnp.concatenate([value, other]),
        jnp.concatenate([other, value]),
    )


def gather_rounds(value, axis, first, last):
    size = 1 << first
    while size < (1 << last):
        value = gather_round(value, axis, size)
        size *= 2
    return value


def long_runs(ids, paired, tok_rows):
    count = lax.axis_size("ctx")
    longest = (count * tok_rows // 4 - 1) // tok_rows
    group = 2 if paired else 1
    near = 1
    while near * group <= longest:
        near *= 2
    window = near * group
    joined = jnp.concatenate([jnp.zeros((1,), jnp.int32), (ids[1:] == ids[:-1]).astype(jnp.int32)])
    if window > count:
        return near, jnp.zeros((), jnp.bool_)
    breaks = jnp.cumsum(1 - joined)
    ahead = jnp.concatenate([jnp.zeros((1,), jnp.int32), breaks[:-window]])
    return near, jnp.any(breaks[window - 1 :] - ahead == 0)


def blockwise(f, items):
    if jax.tree.leaves(items)[0].shape[0] == 1:
        out = f(jax.tree.map(lambda a: a[0], items))
        return jax.tree.map(lambda a: a[None], out)
    return lax.map(f, items)


def device_entry(dev_transmit, dev_state, paired, far):
    count = lax.axis_size("ctx")
    if not paired:
        return scan_rounds((dev_transmit, dev_state), "ctx", 1, count, count, far)
    heads = dev_state.shape[0]
    half = heads // 2
    core = lax.axis_index("ctx") % 2
    swap = [(s, s ^ 1) for s in range(count)]
    own_lo = core * half
    give = lax.dynamic_slice_in_dim(dev_state, half - own_lo, half, 0)
    other_t, other_s = lax.ppermute((dev_transmit, give), "ctx", swap)
    mine_s = lax.dynamic_slice_in_dim(dev_state, own_lo, half, 0)
    mine_t = lax.dynamic_slice_in_dim(dev_transmit, own_lo, half, 0)
    peer_t = lax.dynamic_slice_in_dim(other_t, own_lo, half, 0)
    first = core == 0
    chip_s = jnp.where(first, peer_t[:, None, None] * mine_s + other_s, mine_t[:, None, None] * other_s + mine_s)
    chip_t = mine_t * peer_t
    entering = scan_rounds((chip_t, chip_s), "ctx", 2, count // 2, count, far)
    lead_t = jnp.where(first, mine_t, peer_t)
    lead_s = jnp.where(first, mine_s, other_s)
    second = lead_t[:, None, None] * entering + lead_s
    back = lax.ppermute(jnp.where(first, second, entering), "ctx", swap)
    mine = jnp.where(first, entering, second)
    low = jnp.where(first, mine, back)
    high = jnp.where(first, back, mine)
    return jnp.concatenate([low, high], axis=0)


def chain_states(block_states, transmits, paired, far):

    def advance(carried, item):
        passing, state_now = carried
        transmit, block_state = item
        return (
            (passing * transmit, transmit[:, None, None] * state_now + block_state),
            (passing, state_now),
        )

    start = (jnp.ones_like(transmits[0]), jnp.zeros_like(block_states[0]))
    finals, befores = lax.scan(advance, start, (transmits, block_states))
    entering_dev = device_entry(finals[0], finals[1], paired, far)
    return befores[0][:, :, None, None] * entering_dev[None] + befores[1]


def local(
    paired,
    x_in,
    gate_z,
    bc_in,
    dt_raw,
    dt_bias,
    a_rate,
    skip_d,
    conv_x_w,
    conv_x_b,
    conv_bc_w,
    conv_bc_b,
    norm_gain,
    segment_ids,
):
    tok_rows = x_in.shape[0]
    channels = x_in.shape[1]
    head_count = dt_raw.shape[0]
    block_count = tok_rows // GROUP
    rim_rows = CONV - 1
    bc_width = bc_in.shape[1]
    rims = passed_along(
        jnp.concatenate(
            [
                x_in[tok_rows - rim_rows :],
                bc_in[tok_rows - rim_rows :],
                segment_ids[tok_rows - rim_rows :, None].astype(jnp.bfloat16),
            ],
            axis=1,
        ),
        "ctx",
        1,
    )
    rim_x = rims[:, :channels]
    rim_bc = rims[:, channels : channels + bc_width]
    rim_segment = rims[:, channels + bc_width].astype(jnp.int32)
    ids = gather_rounds(segment_ids[tok_rows - 1 :], "ctx", 0, 2)
    ids, rim_x = lax.optimization_barrier((ids, rim_x))
    x_conv = conv_rows(rim_x, x_in, rim_segment, segment_ids, conv_x_w, conv_x_b)
    ids = gather_rounds(ids, "ctx", 2, 4)
    ids, x_conv = lax.optimization_barrier((ids, x_conv))
    bc_conv = causal_conv(rim_bc, bc_in, rim_segment, segment_ids, conv_bc_w, conv_bc_b)
    step_size = jax.nn.softplus(dt_raw + dt_bias[:, None])
    log_decay = -step_size * a_rate[:, None]
    cum_decay = jnp.transpose(
        jnp.cumsum(log_decay.reshape(head_count, block_count, GROUP), axis=2), (1, 0, 2)
    )
    step_blocks = jnp.transpose(step_size.reshape(head_count, block_count, GROUP), (1, 0, 2))
    seg_blocks = segment_ids.reshape(block_count, GROUP)
    seg_before = jnp.concatenate([rim_segment[rim_rows - 1 :], seg_blocks[:-1, -1]])
    x_blocks = x_conv.reshape(block_count, GROUP, head_count, HEAD_DIM)
    b_blocks = bc_conv[:, :STATE].reshape(block_count, GROUP, STATE)
    c_blocks = bc_conv[:, STATE:].reshape(block_count, GROUP, STATE)

    def state_of(item):
        x_group, b_group, steps_here, decay_here, segment, before = item
        return state_part(x_group, b_group, steps_here, decay_here, segment, before)

    def intra_of(item):
        x_group, b_group, c_group, steps_here, decay_here, segment = item
        return mixing_part(x_group, b_group, c_group, steps_here, decay_here, segment)

    block_states, transmits = blockwise(
        state_of, (x_blocks, b_blocks, step_blocks, cum_decay, seg_blocks, seg_before)
    )
    intra_items = (x_blocks, b_blocks, c_blocks, step_blocks, cum_decay, seg_blocks)
    ids = gather_rounds(ids, "ctx", 4, lax.axis_size("ctx").bit_length())
    ids, block_states = lax.optimization_barrier((ids, block_states))
    far = [*long_runs(ids, paired, tok_rows), intra_items]
    entering = chain_states(block_states, transmits, paired, far)
    y_intra = blockwise(intra_of, far[2])

    def enter_of(item):
        c_group, decay_here, segment, before, entering_here = item
        return entry_part(c_group, entering_here, decay_here, segment, before)

    y_state = blockwise(enter_of, (c_blocks, cum_decay, seg_blocks, seg_before, entering))
    y_blocks = y_intra + y_state
    x_heads = x_conv.reshape(tok_rows, head_count, HEAD_DIM).astype(jnp.float32)
    y_total = y_blocks.reshape(tok_rows, head_count, HEAD_DIM) + skip_d[None, :, None] * x_heads
    gated = y_total.reshape(tok_rows, channels) * jax.nn.silu(gate_z.astype(jnp.float32))
    local_sq = jnp.sum(gated * gated, axis=1)
    total_sq = lax.psum(local_sq, "tp")
    scale = lax.rsqrt(total_sq / INNER + epsilon)
    return scale_rows(gated, scale, norm_gain)


def cores_paired(mesh):
    row = mesh.devices[:, 0] if mesh.devices.ndim == 2 else mesh.devices.reshape(-1)
    if len(row) % 2:
        return False
    try:
        for lo, hi in zip(row[0::2], row[1::2]):
            if tuple(lo.coords) != tuple(hi.coords) or lo.core_on_chip == hi.core_on_chip:
                return False
    except AttributeError:
        return False
    return True


def solution(mesh):
    in_specs = (
        P("ctx", "tp"),
        P("ctx", "tp"),
        P("ctx", None),
        P("tp", "ctx"),
        P("tp"),
        P("tp"),
        P("tp"),
        P(None, "tp"),
        P("tp"),
        P(),
        P(),
        P("tp"),
        P("ctx"),
    )
    out_specs = P("ctx", "tp")
    paired = cores_paired(mesh)
    return jax.shard_map(functools.partial(local, paired), mesh=mesh, in_specs=in_specs, out_specs=out_specs, check_vma=False)
```

```python
import functools

import jax
import jax.numpy as jnp
from jax import lax
from jax.experimental import pallas as pl
from jax.experimental.pallas import tpu as pltpu
from jax.sharding import PartitionSpec as P

HEAD_DIM = 64
STATE = 128
GROUP = 256
CONV = 4
INNER = 8192


epsilon = 1e-05


def passed_along(value, axis, steps):
    count = lax.axis_size(axis)
    leading, last = (max(0, -steps), min(count, count - steps))
    return lax.ppermute(value, axis, [(source, source + steps) for source in range(leading, last)])


def causal_conv(rim_vals, values, rim_segment, segment, weight, offset_bias):
    extended = jnp.concatenate([rim_vals, values], axis=0)
    ext_segment = jnp.concatenate([rim_segment, segment], axis=0)
    length = values.shape[0]
    summed = jnp.zeros(values.shape, jnp.float32) + offset_bias.astype(jnp.float32)
    for offset in range(CONV):
        visible = (ext_segment[offset : offset + length] == segment).astype(jnp.float32)
        summed = (
            summed
            + weight[offset].astype(jnp.float32)
            * extended[offset : offset + length].astype(jnp.float32)
            * visible[:, None]
        )
    return jax.nn.silu(summed).astype(jnp.bfloat16)


def conv_rows_kernel(rim_ref, x_ref, w_ref, b_ref, vis_ref, o_ref):
    rows = x_ref.shape[0]
    here = x_ref[...].astype(jnp.float32)
    rim = jnp.concatenate(
        [rim_ref[...].astype(jnp.float32), jnp.zeros((rows - rim_ref.shape[0],) + here.shape[1:], jnp.float32)]
    )
    row = lax.broadcasted_iota(jnp.int32, here.shape, 0)
    summed = b_ref[...].astype(jnp.float32) + w_ref[CONV - 1 : CONV, :].astype(jnp.float32) * here
    for offset in range(CONV - 1):
        lag = CONV - 1 - offset
        early = pltpu.roll(rim, rows - offset, 0) if offset else rim
        seen = jnp.where(row < lag, early, pltpu.roll(here, lag, 0))
        summed = summed + w_ref[offset : offset + 1, :].astype(jnp.float32) * seen * vis_ref[offset]
    o_ref[...] = jnp.transpose(jax.nn.silu(summed)).astype(o_ref.dtype)


def conv_rows(rim_vals, values, rim_segment, segment, weight, offset_bias):
    rows, width = values.shape
    ext_segment = jnp.concatenate([rim_segment, segment], axis=0)
    vis = jnp.stack(
        [(ext_segment[k : k + rows] == segment).astype(jnp.float32) for k in range(CONV - 1)]
    )[:, :, None]
    rim8 = jnp.concatenate([rim_vals, jnp.zeros((8 - rim_vals.shape[0], width), rim_vals.dtype)])
    tile = min(width, 1024)
    return pl.pallas_call(
        conv_rows_kernel,
        out_shape=jax.ShapeDtypeStruct((width, rows), jnp.bfloat16),
        grid=(width // tile,),
        in_specs=[
            pl.BlockSpec((8, tile), lambda j: (0, j)),
            pl.BlockSpec((rows, tile), lambda j: (0, j)),
            pl.BlockSpec((CONV, tile), lambda j: (0, j)),
            pl.BlockSpec((1, tile), lambda j: (0, j)),
            pl.BlockSpec((CONV - 1, rows, 1), lambda j: (0, 0, 0)),
        ],
        out_specs=pl.BlockSpec((tile, rows), lambda j: (j, 0)),
        cost_estimate=pl.CostEstimate(
            flops=20 * rows * width, transcendentals=rows * width, bytes_accessed=4 * rows * width
        ),
    )(rim8, values, weight, offset_bias.reshape(1, width), vis).T


def scale_rows_kernel(g_ref, s_ref, n_ref, o_ref):
    o_ref[...] = jnp.transpose(g_ref[...] * s_ref[...] * n_ref[...]).astype(o_ref.dtype)


def scale_rows(gated, scale, gain):
    rows, width = gated.shape
    tile = min(width, 2048)
    return pl.pallas_call(
        scale_rows_kernel,
        out_shape=jax.ShapeDtypeStruct((rows, width), jnp.bfloat16),
        grid=(width // tile,),
        in_specs=[
            pl.BlockSpec((tile, rows), lambda j: (j, 0)),
            pl.BlockSpec((1, rows), lambda j: (0, 0)),
            pl.BlockSpec((tile, 1), lambda j: (j, 0)),
        ],
        out_specs=pl.BlockSpec((rows, tile), lambda j: (0, j)),
        cost_estimate=pl.CostEstimate(flops=2 * rows * width, transcendentals=0, bytes_accessed=6 * rows * width),
    )(gated.T, scale[None, :], gain.astype(jnp.float32)[:, None])


def mixing_part(x_group, b_group, c_group, step_size, cum_decay, segment):
    places = jnp.arange(segment.shape[0])
    visible = jnp.logical_and(
        places[:, None] >= places[None, :], segment[:, None] == segment[None, :]
    )
    scores = jnp.einsum("in,jn->ij", c_group, b_group, preferred_element_type=jnp.float32)
    exponent = jnp.where(visible[None], cum_decay[:, :, None] - cum_decay[:, None, :], -jnp.inf)
    mixing = (scores[None] * jnp.exp(exponent) * step_size[:, None, :]).astype(jnp.bfloat16)
    return jnp.einsum("hij,jhp->ihp", mixing, x_group, preferred_element_type=jnp.float32)


def state_part(x_group, b_group, step_size, cum_decay, segment, seg_before):
    closing = cum_decay[:, -1:]
    tail_mask = (segment == segment[-1]).astype(jnp.float32)
    factor = jnp.exp(closing - cum_decay) * step_size * tail_mask[None]
    weighted = (b_group.astype(jnp.float32)[None] * factor[:, :, None]).astype(jnp.bfloat16)
    block_state = jnp.einsum("hjn,jhp->hpn", weighted, x_group, preferred_element_type=jnp.float32)
    transmit = jnp.exp(cum_decay[:, -1]) * (segment[-1] == seg_before).astype(jnp.float32)
    return (block_state, transmit)


def entry_part(c_group, entering, cum_decay, segment, seg_before):
    packed = entering.astype(jnp.bfloat16)
    reach = jnp.exp(cum_decay) * (segment == seg_before).astype(jnp.float32)[None]
    product = jnp.einsum("in,hpn->ihp", c_group, packed, preferred_element_type=jnp.float32)
    return product * jnp.transpose(reach)[:, :, None]


def shifted(value, axis, steps, count):
    return lax.ppermute(value, axis, [(s, s + steps) for s in range(count - steps)])


def scan_round(transmit, state, axis, shift, count):
    far_t, far_s = shifted((transmit, state), axis, shift, count)
    return transmit * far_t, transmit[:, None, None] * far_s + state


def scan_rounds(carry, axis, stride, span, count, far):
    near, needed, rider = far
    carry, rider = lax.optimization_barrier((carry, rider))
    far[2] = rider
    transmit, state = shifted(carry, axis, stride, count)
    covered = 1
    while covered < min(span - 1, near):
        transmit, state = scan_round(transmit, state, axis, stride * covered, count)
        covered *= 2
    if covered < span - 1:

        def rest(carried):
            t, s = carried
            reach = covered
            while reach < span - 1:
                t, s = scan_round(t, s, axis, stride * reach, count)
                reach *= 2
            return t, s

        transmit, state = lax.cond(needed, rest, lambda carried: carried, (transmit, state))
    return state


def gather_round(value, axis, size):
    count = lax.axis_size(axis)
    if count & (count - 1):
        return lax.all_gather(value, axis, tiled=True) if size == 1 else value
    if size >= count:
        return value
    place = lax.axis_index(axis)
    other = lax.ppermute(value, axis, [(s, s ^ size) for s in range(count)])
    return jnp.where(
        (place & size) == 0,
        jnp.concatenate([value, other]),
        jnp.concatenate([other, value]),
    )


def gather_rounds(value, axis, first, last):
    size = 1 << first
    while size < (1 << last):
        value = gather_round(value, axis, size)
        size *= 2
    return value


def long_runs(ids, paired, tok_rows):
    count = lax.axis_size("ctx")
    longest = (count * tok_rows // 4 - 1) // tok_rows
    group = 2 if paired else 1
    near = 1
    while near * group <= longest:
        near *= 2
    window = near * group
    joined = jnp.concatenate([jnp.zeros((1,), jnp.int32), (ids[1:] == ids[:-1]).astype(jnp.int32)])
    if window > count:
        return near, jnp.zeros((), jnp.bool_)
    breaks = jnp.cumsum(1 - joined)
    ahead = jnp.concatenate([jnp.zeros((1,), jnp.int32), breaks[:-window]])
    return near, jnp.any(breaks[window - 1 :] - ahead == 0)


def blockwise(f, items):
    if jax.tree.leaves(items)[0].shape[0] == 1:
        out = f(jax.tree.map(lambda a: a[0], items))
        return jax.tree.map(lambda a: a[None], out)
    return lax.map(f, items)


def device_entry(dev_transmit, dev_state, paired, far):
    count = lax.axis_size("ctx")
    if not paired:
        return scan_rounds((dev_transmit, dev_state), "ctx", 1, count, count, far)
    heads = dev_state.shape[0]
    half = heads // 2
    core = lax.axis_index("ctx") % 2
    swap = [(s, s ^ 1) for s in range(count)]
    own_lo = core * half
    give = lax.dynamic_slice_in_dim(dev_state, half - own_lo, half, 0)
    other_t, other_s = lax.ppermute((dev_transmit, give), "ctx", swap)
    mine_s = lax.dynamic_slice_in_dim(dev_state, own_lo, half, 0)
    mine_t = lax.dynamic_slice_in_dim(dev_transmit, own_lo, half, 0)
    peer_t = lax.dynamic_slice_in_dim(other_t, own_lo, half, 0)
    first = core == 0
    chip_s = jnp.where(first, peer_t[:, None, None] * mine_s + other_s, mine_t[:, None, None] * other_s + mine_s)
    chip_t = mine_t * peer_t
    entering = scan_rounds((chip_t, chip_s), "ctx", 2, count // 2, count, far)
    lead_t = jnp.where(first, mine_t, peer_t)
    lead_s = jnp.where(first, mine_s, other_s)
    second = lead_t[:, None, None] * entering + lead_s
    back = lax.ppermute(jnp.where(first, second, entering), "ctx", swap)
    mine = jnp.where(first, entering, second)
    low = jnp.where(first, mine, back)
    high = jnp.where(first, back, mine)
    return jnp.concatenate([low, high], axis=0)


def chain_states(block_states, transmits, paired, far):

    def advance(carried, item):
        passing, state_now = carried
        transmit, block_state = item
        return (
            (passing * transmit, transmit[:, None, None] * state_now + block_state),
            (passing, state_now),
        )

    start = (jnp.ones_like(transmits[0]), jnp.zeros_like(block_states[0]))
    finals, befores = lax.scan(advance, start, (transmits, block_states))
    entering_dev = device_entry(finals[0], finals[1], paired, far)
    return befores[0][:, :, None, None] * entering_dev[None] + befores[1]


def local(
    paired,
    x_in,
    gate_z,
    bc_in,
    dt_raw,
    dt_bias,
    a_rate,
    skip_d,
    conv_x_w,
    conv_x_b,
    conv_bc_w,
    conv_bc_b,
    norm_gain,
    segment_ids,
):
    tok_rows = x_in.shape[0]
    channels = x_in.shape[1]
    head_count = dt_raw.shape[0]
    block_count = tok_rows // GROUP
    rim_rows = CONV - 1
    bc_width = bc_in.shape[1]
    rims = passed_along(
        jnp.concatenate(
            [
                x_in[tok_rows - rim_rows :],
                bc_in[tok_rows - rim_rows :],
                segment_ids[tok_rows - rim_rows :, None].astype(jnp.bfloat16),
            ],
            axis=1,
        ),
        "ctx",
        1,
    )
    rim_x = rims[:, :channels]
    rim_bc = rims[:, channels : channels + bc_width]
    rim_segment = rims[:, channels + bc_width].astype(jnp.int32)
    ids = gather_rounds(segment_ids[tok_rows - 1 :], "ctx", 0, 2)
    ids, rim_x = lax.optimization_barrier((ids, rim_x))
    x_conv = conv_rows(rim_x, x_in, rim_segment, segment_ids, conv_x_w, conv_x_b)
    ids = gather_rounds(ids, "ctx", 2, 4)
    ids, x_conv = lax.optimization_barrier((ids, x_conv))
    bc_conv = causal_conv(rim_bc, bc_in, rim_segment, segment_ids, conv_bc_w, conv_bc_b)
    step_size = jax.nn.softplus(dt_raw + dt_bias[:, None])
    log_decay = -step_size * a_rate[:, None]
    cum_decay = jnp.transpose(
        jnp.cumsum(log_decay.reshape(head_count, block_count, GROUP), axis=2), (1, 0, 2)
    )
    step_blocks = jnp.transpose(step_size.reshape(head_count, block_count, GROUP), (1, 0, 2))
    seg_blocks = segment_ids.reshape(block_count, GROUP)
    seg_before = jnp.concatenate([rim_segment[rim_rows - 1 :], seg_blocks[:-1, -1]])
    x_blocks = x_conv.reshape(block_count, GROUP, head_count, HEAD_DIM)
    b_blocks = bc_conv[:, :STATE].reshape(block_count, GROUP, STATE)
    c_blocks = bc_conv[:, STATE:].reshape(block_count, GROUP, STATE)

    def state_of(item):
        x_group, b_group, steps_here, decay_here, segment, before = item
        return state_part(x_group, b_group, steps_here, decay_here, segment, before)

    def intra_of(item):
        x_group, b_group, c_group, steps_here, decay_here, segment = item
        return mixing_part(x_group, b_group, c_group, steps_here, decay_here, segment)

    block_states, transmits = blockwise(
        state_of, (x_blocks, b_blocks, step_blocks, cum_decay, seg_blocks, seg_before)
    )
    intra_items = (x_blocks, b_blocks, c_blocks, step_blocks, cum_decay, seg_blocks)
    ids = gather_rounds(ids, "ctx", 4, lax.axis_size("ctx").bit_length())
    ids, block_states = lax.optimization_barrier((ids, block_states))
    far = [*long_runs(ids, paired, tok_rows), intra_items]
    entering = chain_states(block_states, transmits, paired, far)
    y_intra = blockwise(intra_of, far[2])

    def enter_of(item):
        c_group, decay_here, segment, before, entering_here = item
        return entry_part(c_group, entering_here, decay_here, segment, before)

    y_state = blockwise(enter_of, (c_blocks, cum_decay, seg_blocks, seg_before, entering))
    y_blocks = y_intra + y_state
    x_heads = x_conv.reshape(tok_rows, head_count, HEAD_DIM).astype(jnp.float32)
    y_total = y_blocks.reshape(tok_rows, head_count, HEAD_DIM) + skip_d[None, :, None] * x_heads
    gated = y_total.reshape(tok_rows, channels) * jax.nn.silu(gate_z.astype(jnp.float32))
    local_sq = jnp.sum(gated * gated, axis=1)
    total_sq = lax.psum(local_sq, "tp")
    scale = lax.rsqrt(total_sq / INNER + epsilon)
    return scale_rows(gated, scale, norm_gain)


def cores_paired(mesh):
    row = mesh.devices[:, 0] if mesh.devices.ndim == 2 else mesh.devices.reshape(-1)
    if len(row) % 2:
        return False
    try:
        for lo, hi in zip(row[0::2], row[1::2]):
            if tuple(lo.coords) != tuple(hi.coords) or lo.core_on_chip == hi.core_on_chip:
                return False
    except AttributeError:
        return False
    return True


def solution(mesh):
    in_specs = (
        P("ctx", "tp"),
        P("ctx", "tp"),
        P("ctx", None),
        P("tp", "ctx"),
        P("tp"),
        P("tp"),
        P("tp"),
        P(None, "tp"),
        P("tp"),
        P(),
        P(),
        P("tp"),
        P("ctx"),
    )
    out_specs = P("ctx", "tp")
    paired = cores_paired(mesh)
    return jax.shard_map(functools.partial(local, paired), mesh=mesh, in_specs=in_specs, out_specs=out_specs, check_vma=False)
```

```python
import functools

import jax
import jax.numpy as jnp
from jax import lax
from jax.experimental import pallas as pl
from jax.experimental.pallas import tpu as pltpu
from jax.sharding import PartitionSpec as P

HEAD_DIM = 64
STATE = 128
GROUP = 256
CONV = 4
INNER = 8192


epsilon = 1e-05


def passed_along(value, axis, steps):
    count = lax.axis_size(axis)
    leading, last = (max(0, -steps), min(count, count - steps))
    return lax.ppermute(value, axis, [(source, source + steps) for source in range(leading, last)])


def causal_conv(rim_vals, values, rim_segment, segment, weight, offset_bias):
    extended = jnp.concatenate([rim_vals, values], axis=0)
    ext_segment = jnp.concatenate([rim_segment, segment], axis=0)
    length = values.shape[0]
    summed = jnp.zeros(values.shape, jnp.float32) + offset_bias.astype(jnp.float32)
    for offset in range(CONV):
        visible = (ext_segment[offset : offset + length] == segment).astype(jnp.float32)
        summed = (
            summed
            + weight[offset].astype(jnp.float32)
            * extended[offset : offset + length].astype(jnp.float32)
            * visible[:, None]
        )
    return jax.nn.silu(summed).astype(jnp.bfloat16)


def conv_rows_kernel(rim_ref, x_ref, w_ref, b_ref, vis_ref, o_ref):
    rows = x_ref.shape[0]
    here = x_ref[...].astype(jnp.float32)
    rim = jnp.concatenate(
        [rim_ref[...].astype(jnp.float32), jnp.zeros((rows - rim_ref.shape[0],) + here.shape[1:], jnp.float32)]
    )
    row = lax.broadcasted_iota(jnp.int32, here.shape, 0)
    summed = b_ref[...].astype(jnp.float32) + w_ref[CONV - 1 : CONV, :].astype(jnp.float32) * here
    for offset in range(CONV - 1):
        lag = CONV - 1 - offset
        early = pltpu.roll(rim, rows - offset, 0) if offset else rim
        seen = jnp.where(row < lag, early, pltpu.roll(here, lag, 0))
        summed = summed + w_ref[offset : offset + 1, :].astype(jnp.float32) * seen * vis_ref[offset]
    o_ref[...] = jnp.transpose(jax.nn.silu(summed)).astype(o_ref.dtype)


def conv_rows(rim_vals, values, rim_segment, segment, weight, offset_bias):
    rows, width = values.shape
    ext_segment = jnp.concatenate([rim_segment, segment], axis=0)
    vis = jnp.stack(
        [(ext_segment[k : k + rows] == segment).astype(jnp.float32) for k in range(CONV - 1)]
    )[:, :, None]
    rim8 = jnp.concatenate([rim_vals, jnp.zeros((8 - rim_vals.shape[0], width), rim_vals.dtype)])
    tile = min(width, 2048)
    return pl.pallas_call(
        conv_rows_kernel,
        out_shape=jax.ShapeDtypeStruct((width, rows), jnp.bfloat16),
        grid=(width // tile,),
        in_specs=[
            pl.BlockSpec((8, tile), lambda j: (0, j)),
            pl.BlockSpec((rows, tile), lambda j: (0, j)),
            pl.BlockSpec((CONV, tile), lambda j: (0, j)),
            pl.BlockSpec((1, tile), lambda j: (0, j)),
            pl.BlockSpec((CONV - 1, rows, 1), lambda j: (0, 0, 0)),
        ],
        out_specs=pl.BlockSpec((tile, rows), lambda j: (j, 0)),
        cost_estimate=pl.CostEstimate(
            flops=20 * rows * width, transcendentals=rows * width, bytes_accessed=4 * rows * width
        ),
    )(rim8, values, weight, offset_bias.reshape(1, width), vis).T


def scale_rows_kernel(g_ref, s_ref, n_ref, o_ref):
    o_ref[...] = jnp.transpose(g_ref[...] * s_ref[...] * n_ref[...]).astype(o_ref.dtype)


def scale_rows(gated, scale, gain):
    rows, width = gated.shape
    tile = min(width, 2048)
    return pl.pallas_call(
        scale_rows_kernel,
        out_shape=jax.ShapeDtypeStruct((rows, width), jnp.bfloat16),
        grid=(width // tile,),
        in_specs=[
            pl.BlockSpec((tile, rows), lambda j: (j, 0)),
            pl.BlockSpec((1, rows), lambda j: (0, 0)),
            pl.BlockSpec((tile, 1), lambda j: (j, 0)),
        ],
        out_specs=pl.BlockSpec((rows, tile), lambda j: (0, j)),
        cost_estimate=pl.CostEstimate(flops=2 * rows * width, transcendentals=0, bytes_accessed=6 * rows * width),
    )(gated.T, scale[None, :], gain.astype(jnp.float32)[:, None])


def mixing_part(x_group, b_group, c_group, step_size, cum_decay, segment):
    places = jnp.arange(segment.shape[0])
    visible = jnp.logical_and(
        places[:, None] >= places[None, :], segment[:, None] == segment[None, :]
    )
    scores = jnp.einsum("in,jn->ij", c_group, b_group, preferred_element_type=jnp.float32)
    exponent = jnp.where(visible[None], cum_decay[:, :, None] - cum_decay[:, None, :], -jnp.inf)
    mixing = (scores[None] * jnp.exp(exponent) * step_size[:, None, :]).astype(jnp.bfloat16)
    return jnp.einsum("hij,jhp->ihp", mixing, x_group, preferred_element_type=jnp.float32)


def state_part(x_group, b_group, step_size, cum_decay, segment, seg_before):
    closing = cum_decay[:, -1:]
    tail_mask = (segment == segment[-1]).astype(jnp.float32)
    factor = jnp.exp(closing - cum_decay) * step_size * tail_mask[None]
    weighted = (b_group.astype(jnp.float32)[None] * factor[:, :, None]).astype(jnp.bfloat16)
    block_state = jnp.einsum("hjn,jhp->hpn", weighted, x_group, preferred_element_type=jnp.float32)
    transmit = jnp.exp(cum_decay[:, -1]) * (segment[-1] == seg_before).astype(jnp.float32)
    return (block_state, transmit)


def entry_part(c_group, entering, cum_decay, segment, seg_before):
    packed = entering.astype(jnp.bfloat16)
    reach = jnp.exp(cum_decay) * (segment == seg_before).astype(jnp.float32)[None]
    product = jnp.einsum("in,hpn->ihp", c_group, packed, preferred_element_type=jnp.float32)
    return product * jnp.transpose(reach)[:, :, None]


def shifted(value, axis, steps, count):
    return lax.ppermute(value, axis, [(s, s + steps) for s in range(count - steps)])


def scan_round(transmit, state, axis, shift, count):
    far_t, far_s = shifted((transmit, state), axis, shift, count)
    return transmit * far_t, transmit[:, None, None] * far_s + state


def scan_rounds(carry, axis, stride, span, count, far):
    near, needed, rider = far
    carry, rider = lax.optimization_barrier((carry, rider))
    far[2] = rider
    transmit, state = shifted(carry, axis, stride, count)
    covered = 1
    while covered < min(span - 1, near):
        transmit, state = scan_round(transmit, state, axis, stride * covered, count)
        covered *= 2
    if covered < span - 1:

        def rest(carried):
            t, s = carried
            reach = covered
            while reach < span - 1:
                t, s = scan_round(t, s, axis, stride * reach, count)
                reach *= 2
            return t, s

        transmit, state = lax.cond(needed, rest, lambda carried: carried, (transmit, state))
    return state


def gather_round(value, axis, size):
    count = lax.axis_size(axis)
    if count & (count - 1):
        return lax.all_gather(value, axis, tiled=True) if size == 1 else value
    if size >= count:
        return value
    place = lax.axis_index(axis)
    other = lax.ppermute(value, axis, [(s, s ^ size) for s in range(count)])
    return jnp.where(
        (place & size) == 0,
        jnp.concatenate([value, other]),
        jnp.concatenate([other, value]),
    )


def gather_rounds(value, axis, first, last):
    size = 1 << first
    while size < (1 << last):
        value = gather_round(value, axis, size)
        size *= 2
    return value


def long_runs(ids, paired, tok_rows):
    count = lax.axis_size("ctx")
    longest = (count * tok_rows // 4 - 1) // tok_rows
    group = 2 if paired else 1
    near = 1
    while near * group <= longest:
        near *= 2
    window = near * group
    joined = jnp.concatenate([jnp.zeros((1,), jnp.int32), (ids[1:] == ids[:-1]).astype(jnp.int32)])
    if window > count:
        return near, jnp.zeros((), jnp.bool_)
    breaks = jnp.cumsum(1 - joined)
    ahead = jnp.concatenate([jnp.zeros((1,), jnp.int32), breaks[:-window]])
    return near, jnp.any(breaks[window - 1 :] - ahead == 0)


def blockwise(f, items):
    if jax.tree.leaves(items)[0].shape[0] == 1:
        out = f(jax.tree.map(lambda a: a[0], items))
        return jax.tree.map(lambda a: a[None], out)
    return lax.map(f, items)


def device_entry(dev_transmit, dev_state, paired, far):
    count = lax.axis_size("ctx")
    if not paired:
        return scan_rounds((dev_transmit, dev_state), "ctx", 1, count, count, far)
    heads = dev_state.shape[0]
    half = heads // 2
    core = lax.axis_index("ctx") % 2
    swap = [(s, s ^ 1) for s in range(count)]
    own_lo = core * half
    give = lax.dynamic_slice_in_dim(dev_state, half - own_lo, half, 0)
    other_t, other_s = lax.ppermute((dev_transmit, give), "ctx", swap)
    mine_s = lax.dynamic_slice_in_dim(dev_state, own_lo, half, 0)
    mine_t = lax.dynamic_slice_in_dim(dev_transmit, own_lo, half, 0)
    peer_t = lax.dynamic_slice_in_dim(other_t, own_lo, half, 0)
    first = core == 0
    chip_s = jnp.where(first, peer_t[:, None, None] * mine_s + other_s, mine_t[:, None, None] * other_s + mine_s)
    chip_t = mine_t * peer_t
    entering = scan_rounds((chip_t, chip_s), "ctx", 2, count // 2, count, far)
    lead_t = jnp.where(first, mine_t, peer_t)
    lead_s = jnp.where(first, mine_s, other_s)
    second = lead_t[:, None, None] * entering + lead_s
    back = lax.ppermute(jnp.where(first, second, entering), "ctx", swap)
    mine = jnp.where(first, entering, second)
    low = jnp.where(first, mine, back)
    high = jnp.where(first, back, mine)
    return jnp.concatenate([low, high], axis=0)


def chain_states(block_states, transmits, paired, far):

    def advance(carried, item):
        passing, state_now = carried
        transmit, block_state = item
        return (
            (passing * transmit, transmit[:, None, None] * state_now + block_state),
            (passing, state_now),
        )

    start = (jnp.ones_like(transmits[0]), jnp.zeros_like(block_states[0]))
    finals, befores = lax.scan(advance, start, (transmits, block_states))
    entering_dev = device_entry(finals[0], finals[1], paired, far)
    return befores[0][:, :, None, None] * entering_dev[None] + befores[1]


def local(
    paired,
    x_in,
    gate_z,
    bc_in,
    dt_raw,
    dt_bias,
    a_rate,
    skip_d,
    conv_x_w,
    conv_x_b,
    conv_bc_w,
    conv_bc_b,
    norm_gain,
    segment_ids,
):
    tok_rows = x_in.shape[0]
    channels = x_in.shape[1]
    head_count = dt_raw.shape[0]
    block_count = tok_rows // GROUP
    rim_rows = CONV - 1
    bc_width = bc_in.shape[1]
    rims = passed_along(
        jnp.concatenate(
            [
                x_in[tok_rows - rim_rows :],
                bc_in[tok_rows - rim_rows :],
                segment_ids[tok_rows - rim_rows :, None].astype(jnp.bfloat16),
            ],
            axis=1,
        ),
        "ctx",
        1,
    )
    rim_x = rims[:, :channels]
    rim_bc = rims[:, channels : channels + bc_width]
    rim_segment = rims[:, channels + bc_width].astype(jnp.int32)
    ids = gather_rounds(segment_ids[tok_rows - 1 :], "ctx", 0, 2)
    ids, rim_x = lax.optimization_barrier((ids, rim_x))
    x_conv = conv_rows(rim_x, x_in, rim_segment, segment_ids, conv_x_w, conv_x_b)
    ids = gather_rounds(ids, "ctx", 2, 4)
    ids, x_conv = lax.optimization_barrier((ids, x_conv))
    bc_conv = causal_conv(rim_bc, bc_in, rim_segment, segment_ids, conv_bc_w, conv_bc_b)
    step_size = jax.nn.softplus(dt_raw + dt_bias[:, None])
    log_decay = -step_size * a_rate[:, None]
    cum_decay = jnp.transpose(
        jnp.cumsum(log_decay.reshape(head_count, block_count, GROUP), axis=2), (1, 0, 2)
    )
    step_blocks = jnp.transpose(step_size.reshape(head_count, block_count, GROUP), (1, 0, 2))
    seg_blocks = segment_ids.reshape(block_count, GROUP)
    seg_before = jnp.concatenate([rim_segment[rim_rows - 1 :], seg_blocks[:-1, -1]])
    x_blocks = x_conv.reshape(block_count, GROUP, head_count, HEAD_DIM)
    b_blocks = bc_conv[:, :STATE].reshape(block_count, GROUP, STATE)
    c_blocks = bc_conv[:, STATE:].reshape(block_count, GROUP, STATE)

    def state_of(item):
        x_group, b_group, steps_here, decay_here, segment, before = item
        return state_part(x_group, b_group, steps_here, decay_here, segment, before)

    def intra_of(item):
        x_group, b_group, c_group, steps_here, decay_here, segment = item
        return mixing_part(x_group, b_group, c_group, steps_here, decay_here, segment)

    block_states, transmits = blockwise(
        state_of, (x_blocks, b_blocks, step_blocks, cum_decay, seg_blocks, seg_before)
    )
    intra_items = (x_blocks, b_blocks, c_blocks, step_blocks, cum_decay, seg_blocks)
    ids = gather_rounds(ids, "ctx", 4, lax.axis_size("ctx").bit_length())
    ids, block_states = lax.optimization_barrier((ids, block_states))
    far = [*long_runs(ids, paired, tok_rows), intra_items]
    entering = chain_states(block_states, transmits, paired, far)
    y_intra = blockwise(intra_of, far[2])

    def enter_of(item):
        c_group, decay_here, segment, before, entering_here = item
        return entry_part(c_group, entering_here, decay_here, segment, before)

    y_state = blockwise(enter_of, (c_blocks, cum_decay, seg_blocks, seg_before, entering))
    y_blocks = y_intra + y_state
    x_heads = x_conv.reshape(tok_rows, head_count, HEAD_DIM).astype(jnp.float32)
    y_total = y_blocks.reshape(tok_rows, head_count, HEAD_DIM) + skip_d[None, :, None] * x_heads
    gated = y_total.reshape(tok_rows, channels) * jax.nn.silu(gate_z.astype(jnp.float32))
    local_sq = jnp.sum(gated * gated, axis=1)
    total_sq = lax.psum(local_sq, "tp")
    scale = lax.rsqrt(total_sq / INNER + epsilon)
    return scale_rows(gated, scale, norm_gain)


def cores_paired(mesh):
    row = mesh.devices[:, 0] if mesh.devices.ndim == 2 else mesh.devices.reshape(-1)
    if len(row) % 2:
        return False
    try:
        for lo, hi in zip(row[0::2], row[1::2]):
            if tuple(lo.coords) != tuple(hi.coords) or lo.core_on_chip == hi.core_on_chip:
                return False
    except AttributeError:
        return False
    return True


def solution(mesh):
    in_specs = (
        P("ctx", "tp"),
        P("ctx", "tp"),
        P("ctx", None),
        P("tp", "ctx"),
        P("tp"),
        P("tp"),
        P("tp"),
        P(None, "tp"),
        P("tp"),
        P(),
        P(),
        P("tp"),
        P("ctx"),
    )
    out_specs = P("ctx", "tp")
    paired = cores_paired(mesh)
    return jax.shard_map(functools.partial(local, paired), mesh=mesh, in_specs=in_specs, out_specs=out_specs, check_vma=False)
```

```python
import functools

import jax
import jax.numpy as jnp
from jax import lax
from jax.experimental import pallas as pl
from jax.experimental.pallas import tpu as pltpu
from jax.sharding import PartitionSpec as P

HEAD_DIM = 64
STATE = 128
GROUP = 256
CONV = 4
INNER = 8192


epsilon = 1e-05


def passed_along(value, axis, steps):
    count = lax.axis_size(axis)
    leading, last = (max(0, -steps), min(count, count - steps))
    return lax.ppermute(value, axis, [(source, source + steps) for source in range(leading, last)])


def causal_conv(rim_vals, values, rim_segment, segment, weight, offset_bias):
    extended = jnp.concatenate([rim_vals, values], axis=0)
    ext_segment = jnp.concatenate([rim_segment, segment], axis=0)
    length = values.shape[0]
    summed = jnp.zeros(values.shape, jnp.float32) + offset_bias.astype(jnp.float32)
    for offset in range(CONV):
        visible = (ext_segment[offset : offset + length] == segment).astype(jnp.float32)
        summed = (
            summed
            + weight[offset].astype(jnp.float32)
            * extended[offset : offset + length].astype(jnp.float32)
            * visible[:, None]
        )
    return jax.nn.silu(summed).astype(jnp.bfloat16)


def conv_rows_kernel(rim_ref, x_ref, w_ref, b_ref, vis_ref, o_ref):
    rows = x_ref.shape[0]
    here = x_ref[...].astype(jnp.float32)
    rim = jnp.concatenate(
        [rim_ref[...].astype(jnp.float32), jnp.zeros((rows - rim_ref.shape[0],) + here.shape[1:], jnp.float32)]
    )
    row = lax.broadcasted_iota(jnp.int32, here.shape, 0)
    summed = b_ref[...].astype(jnp.float32) + w_ref[CONV - 1 : CONV, :].astype(jnp.float32) * here
    for offset in range(CONV - 1):
        lag = CONV - 1 - offset
        early = pltpu.roll(rim, rows - offset, 0) if offset else rim
        seen = jnp.where(row < lag, early, pltpu.roll(here, lag, 0))
        summed = summed + w_ref[offset : offset + 1, :].astype(jnp.float32) * seen * vis_ref[offset]
    o_ref[...] = jnp.transpose(jax.nn.silu(summed)).astype(o_ref.dtype)


def conv_rows(rim_vals, values, rim_segment, segment, weight, offset_bias):
    rows, width = values.shape
    ext_segment = jnp.concatenate([rim_segment, segment], axis=0)
    vis = jnp.stack(
        [(ext_segment[k : k + rows] == segment).astype(jnp.float32) for k in range(CONV - 1)]
    )[:, :, None]
    rim8 = jnp.concatenate([rim_vals, jnp.zeros((8 - rim_vals.shape[0], width), rim_vals.dtype)])
    tile = min(width, 2048)
    return pl.pallas_call(
        conv_rows_kernel,
        out_shape=jax.ShapeDtypeStruct((width, rows), jnp.bfloat16),
        grid=(width // tile,),
        in_specs=[
            pl.BlockSpec((8, tile), lambda j: (0, j)),
            pl.BlockSpec((rows, tile), lambda j: (0, j)),
            pl.BlockSpec((CONV, tile), lambda j: (0, j)),
            pl.BlockSpec((1, tile), lambda j: (0, j)),
            pl.BlockSpec((CONV - 1, rows, 1), lambda j: (0, 0, 0)),
        ],
        out_specs=pl.BlockSpec((tile, rows), lambda j: (j, 0)),
        cost_estimate=pl.CostEstimate(
            flops=20 * rows * width, transcendentals=rows * width, bytes_accessed=4 * rows * width
        ),
    )(rim8, values, weight, offset_bias.reshape(1, width), vis).T


def scale_rows_kernel(g_ref, s_ref, n_ref, o_ref):
    o_ref[...] = jnp.transpose(g_ref[...] * s_ref[...] * n_ref[...]).astype(o_ref.dtype)


def scale_rows(gated, scale, gain):
    rows, width = gated.shape
    tile = min(width, 2048)
    return pl.pallas_call(
        scale_rows_kernel,
        out_shape=jax.ShapeDtypeStruct((rows, width), jnp.bfloat16),
        grid=(width // tile,),
        in_specs=[
            pl.BlockSpec((tile, rows), lambda j: (j, 0)),
            pl.BlockSpec((1, rows), lambda j: (0, 0)),
            pl.BlockSpec((tile, 1), lambda j: (j, 0)),
        ],
        out_specs=pl.BlockSpec((rows, tile), lambda j: (0, j)),
        cost_estimate=pl.CostEstimate(flops=2 * rows * width, transcendentals=0, bytes_accessed=6 * rows * width),
    )(gated.T, scale[None, :], gain.astype(jnp.float32)[:, None])


def mixing_part(x_group, b_group, c_group, step_size, cum_decay, segment):
    places = jnp.arange(segment.shape[0])
    visible = jnp.logical_and(
        places[:, None] >= places[None, :], segment[:, None] == segment[None, :]
    )
    scores = jnp.einsum("in,jn->ij", c_group, b_group, preferred_element_type=jnp.float32)
    exponent = jnp.where(visible[None], cum_decay[:, :, None] - cum_decay[:, None, :], -jnp.inf)
    mixing = (scores[None] * jnp.exp(exponent) * step_size[:, None, :]).astype(jnp.bfloat16)
    return jnp.einsum("hij,jhp->ihp", mixing, x_group, preferred_element_type=jnp.float32)


def state_part(x_group, b_group, step_size, cum_decay, segment, seg_before):
    closing = cum_decay[:, -1:]
    tail_mask = (segment == segment[-1]).astype(jnp.float32)
    factor = jnp.exp(closing - cum_decay) * step_size * tail_mask[None]
    weighted = (b_group.astype(jnp.float32)[None] * factor[:, :, None]).astype(jnp.bfloat16)
    block_state = jnp.einsum("hjn,jhp->hpn", weighted, x_group, preferred_element_type=jnp.float32)
    transmit = jnp.exp(cum_decay[:, -1]) * (segment[-1] == seg_before).astype(jnp.float32)
    return (block_state, transmit)


def entry_part(c_group, entering, cum_decay, segment, seg_before):
    packed = entering.astype(jnp.bfloat16)
    reach = jnp.exp(cum_decay) * (segment == seg_before).astype(jnp.float32)[None]
    product = jnp.einsum("in,hpn->ihp", c_group, packed, preferred_element_type=jnp.float32)
    return product * jnp.transpose(reach)[:, :, None]


def shifted(value, axis, steps, count):
    return lax.ppermute(value, axis, [(s, s + steps) for s in range(count - steps)])


def scan_round(transmit, state, axis, shift, count):
    far_t, far_s = shifted((transmit, state), axis, shift, count)
    return transmit * far_t, transmit[:, None, None] * far_s + state


def scan_rounds(carry, axis, stride, span, count, far):
    near, needed, rider = far
    carry, rider = lax.optimization_barrier((carry, rider))
    far[2] = rider
    transmit, state = shifted(carry, axis, stride, count)
    covered = 1
    while covered < min(span - 1, near):
        transmit, state = scan_round(transmit, state, axis, stride * covered, count)
        covered *= 2
    if covered < span - 1:

        def rest(carried):
            t, s = carried
            reach = covered
            while reach < span - 1:
                t, s = scan_round(t, s, axis, stride * reach, count)
                reach *= 2
            return t, s

        transmit, state = lax.cond(needed, rest, lambda carried: carried, (transmit, state))
    return state


def gather_round(value, axis, size):
    count = lax.axis_size(axis)
    if count & (count - 1):
        return lax.all_gather(value, axis, tiled=True) if size == 1 else value
    if size >= count:
        return value
    place = lax.axis_index(axis)
    other = lax.ppermute(value, axis, [(s, s ^ size) for s in range(count)])
    return jnp.where(
        (place & size) == 0,
        jnp.concatenate([value, other]),
        jnp.concatenate([other, value]),
    )


def gather_rounds(value, axis, first, last):
    size = 1 << first
    while size < (1 << last):
        value = gather_round(value, axis, size)
        size *= 2
    return value


def long_runs(ids, paired, tok_rows):
    count = lax.axis_size("ctx")
    longest = (count * tok_rows // 4 - 1) // tok_rows
    group = 2 if paired else 1
    near = 1
    while near * group <= longest:
        near *= 2
    window = near * group
    joined = jnp.concatenate([jnp.zeros((1,), jnp.int32), (ids[1:] == ids[:-1]).astype(jnp.int32)])
    if window > count:
        return near, jnp.zeros((), jnp.bool_)
    breaks = jnp.cumsum(1 - joined)
    ahead = jnp.concatenate([jnp.zeros((1,), jnp.int32), breaks[:-window]])
    return near, jnp.any(breaks[window - 1 :] - ahead == 0)


def blockwise(f, items):
    if jax.tree.leaves(items)[0].shape[0] == 1:
        out = f(jax.tree.map(lambda a: a[0], items))
        return jax.tree.map(lambda a: a[None], out)
    return lax.map(f, items)


def device_entry(dev_transmit, dev_state, paired, far, split=None):
    count = lax.axis_size("ctx")
    if not paired:
        return scan_rounds((dev_transmit, dev_state), "ctx", 1, count, count, far)
    core = lax.axis_index("ctx") % 2
    swap = [(s, s ^ 1) for s in range(count)]
    if split is None:
        half = dev_state.shape[0] // 2
        own_lo = core * half
        give_s = lax.dynamic_slice_in_dim(dev_state, half - own_lo, half, 0)
        give_t = lax.dynamic_slice_in_dim(dev_transmit, half - own_lo, half, 0)
        mine_s = lax.dynamic_slice_in_dim(dev_state, own_lo, half, 0)
        mine_t = lax.dynamic_slice_in_dim(dev_transmit, own_lo, half, 0)
    else:
        give_s, give_t, mine_s, mine_t = split
    peer_t, other_s = lax.ppermute((give_t, give_s), "ctx", swap)
    first = core == 0
    chip_s = jnp.where(first, peer_t[:, None, None] * mine_s + other_s, mine_t[:, None, None] * other_s + mine_s)
    chip_t = mine_t * peer_t
    entering = scan_rounds((chip_t, chip_s), "ctx", 2, count // 2, count, far)
    lead_t = jnp.where(first, mine_t, peer_t)
    lead_s = jnp.where(first, mine_s, other_s)
    second = lead_t[:, None, None] * entering + lead_s
    back = lax.ppermute(jnp.where(first, second, entering), "ctx", swap)
    mine = jnp.where(first, entering, second)
    low = jnp.where(first, mine, back)
    high = jnp.where(first, back, mine)
    return jnp.concatenate([low, high], axis=0)


def chain_states(block_states, transmits, paired, far):

    def advance(carried, item):
        passing, state_now = carried
        transmit, block_state = item
        return (
            (passing * transmit, transmit[:, None, None] * state_now + block_state),
            (passing, state_now),
        )

    start = (jnp.ones_like(transmits[0]), jnp.zeros_like(block_states[0]))
    finals, befores = lax.scan(advance, start, (transmits, block_states))
    entering_dev = device_entry(finals[0], finals[1], paired, far)
    return befores[0][:, :, None, None] * entering_dev[None] + befores[1]


def local(
    paired,
    x_in,
    gate_z,
    bc_in,
    dt_raw,
    dt_bias,
    a_rate,
    skip_d,
    conv_x_w,
    conv_x_b,
    conv_bc_w,
    conv_bc_b,
    norm_gain,
    segment_ids,
):
    tok_rows = x_in.shape[0]
    channels = x_in.shape[1]
    head_count = dt_raw.shape[0]
    block_count = tok_rows // GROUP
    rim_rows = CONV - 1
    bc_width = bc_in.shape[1]
    rims = passed_along(
        jnp.concatenate(
            [
                x_in[tok_rows - rim_rows :],
                bc_in[tok_rows - rim_rows :],
                segment_ids[tok_rows - rim_rows :, None].astype(jnp.bfloat16),
            ],
            axis=1,
        ),
        "ctx",
        1,
    )
    rim_x = rims[:, :channels]
    rim_bc = rims[:, channels : channels + bc_width]
    rim_segment = rims[:, channels + bc_width].astype(jnp.int32)
    ids = gather_rounds(segment_ids[tok_rows - 1 :], "ctx", 0, 2)
    ids, rim_x = lax.optimization_barrier((ids, rim_x))
    x_conv = conv_rows(rim_x, x_in, rim_segment, segment_ids, conv_x_w, conv_x_b)
    ids = gather_rounds(ids, "ctx", 2, 4)
    ids, x_conv = lax.optimization_barrier((ids, x_conv))
    bc_conv = causal_conv(rim_bc, bc_in, rim_segment, segment_ids, conv_bc_w, conv_bc_b)
    step_size = jax.nn.softplus(dt_raw + dt_bias[:, None])
    log_decay = -step_size * a_rate[:, None]
    cum_decay = jnp.transpose(
        jnp.cumsum(log_decay.reshape(head_count, block_count, GROUP), axis=2), (1, 0, 2)
    )
    step_blocks = jnp.transpose(step_size.reshape(head_count, block_count, GROUP), (1, 0, 2))
    seg_blocks = segment_ids.reshape(block_count, GROUP)
    seg_before = jnp.concatenate([rim_segment[rim_rows - 1 :], seg_blocks[:-1, -1]])
    x_blocks = x_conv.reshape(block_count, GROUP, head_count, HEAD_DIM)
    b_blocks = bc_conv[:, :STATE].reshape(block_count, GROUP, STATE)
    c_blocks = bc_conv[:, STATE:].reshape(block_count, GROUP, STATE)

    def state_of(item):
        x_group, b_group, steps_here, decay_here, segment, before = item
        return state_part(x_group, b_group, steps_here, decay_here, segment, before)

    def intra_of(item):
        x_group, b_group, c_group, steps_here, decay_here, segment = item
        return mixing_part(x_group, b_group, c_group, steps_here, decay_here, segment)

    intra_items = (x_blocks, b_blocks, c_blocks, step_blocks, cum_decay, seg_blocks)
    ids = gather_rounds(ids, "ctx", 4, lax.axis_size("ctx").bit_length())
    if paired and block_count == 1:
        half = head_count // 2
        core = lax.axis_index("ctx") % 2

        def half_state(offset):
            return blockwise(
                state_of,
                (
                    lax.dynamic_slice_in_dim(x_blocks, offset, half, 2),
                    b_blocks,
                    lax.dynamic_slice_in_dim(step_blocks, offset, half, 1),
                    lax.dynamic_slice_in_dim(cum_decay, offset, half, 1),
                    seg_blocks,
                    seg_before,
                ),
            )

        give_s, give_t = half_state((1 - core) * half)
        ids, give_s = lax.optimization_barrier((ids, give_s))
        mine_s, mine_t = half_state(core * half)
        far = [*long_runs(ids, paired, tok_rows), intra_items]
        split = (give_s[0], give_t[0], mine_s[0], mine_t[0])
        entering = device_entry(None, None, paired, far, split)[None]
    else:
        block_states, transmits = blockwise(
            state_of, (x_blocks, b_blocks, step_blocks, cum_decay, seg_blocks, seg_before)
        )
        ids, block_states = lax.optimization_barrier((ids, block_states))
        far = [*long_runs(ids, paired, tok_rows), intra_items]
        entering = chain_states(block_states, transmits, paired, far)
    y_intra = blockwise(intra_of, far[2])

    def enter_of(item):
        c_group, decay_here, segment, before, entering_here = item
        return entry_part(c_group, entering_here, decay_here, segment, before)

    y_state = blockwise(enter_of, (c_blocks, cum_decay, seg_blocks, seg_before, entering))
    y_blocks = y_intra + y_state
    x_heads = x_conv.reshape(tok_rows, head_count, HEAD_DIM).astype(jnp.float32)
    y_total = y_blocks.reshape(tok_rows, head_count, HEAD_DIM) + skip_d[None, :, None] * x_heads
    gated = y_total.reshape(tok_rows, channels) * jax.nn.silu(gate_z.astype(jnp.float32))
    local_sq = jnp.sum(gated * gated, axis=1)
    total_sq = lax.psum(local_sq, "tp")
    scale = lax.rsqrt(total_sq / INNER + epsilon)
    return scale_rows(gated, scale, norm_gain)


def cores_paired(mesh):
    row = mesh.devices[:, 0] if mesh.devices.ndim == 2 else mesh.devices.reshape(-1)
    if len(row) % 2:
        return False
    try:
        for lo, hi in zip(row[0::2], row[1::2]):
            if tuple(lo.coords) != tuple(hi.coords) or lo.core_on_chip == hi.core_on_chip:
                return False
    except AttributeError:
        return False
    return True


def solution(mesh):
    in_specs = (
        P("ctx", "tp"),
        P("ctx", "tp"),
        P("ctx", None),
        P("tp", "ctx"),
        P("tp"),
        P("tp"),
        P("tp"),
        P(None, "tp"),
        P("tp"),
        P(),
        P(),
        P("tp"),
        P("ctx"),
    )
    out_specs = P("ctx", "tp")
    paired = cores_paired(mesh)
    return jax.shard_map(functools.partial(local, paired), mesh=mesh, in_specs=in_specs, out_specs=out_specs, check_vma=False)
```

```python
import functools

import jax
import jax.numpy as jnp
from jax import lax
from jax.experimental import pallas as pl
from jax.experimental.pallas import tpu as pltpu
from jax.sharding import PartitionSpec as P

HEAD_DIM = 64
STATE = 128
GROUP = 256
CONV = 4
INNER = 8192


epsilon = 1e-05


def passed_along(value, axis, steps):
    count = lax.axis_size(axis)
    leading, last = (max(0, -steps), min(count, count - steps))
    return lax.ppermute(value, axis, [(source, source + steps) for source in range(leading, last)])


def causal_conv(rim_vals, values, rim_segment, segment, weight, offset_bias):
    extended = jnp.concatenate([rim_vals, values], axis=0)
    ext_segment = jnp.concatenate([rim_segment, segment], axis=0)
    length = values.shape[0]
    summed = jnp.zeros(values.shape, jnp.float32) + offset_bias.astype(jnp.float32)
    for offset in range(CONV):
        visible = (ext_segment[offset : offset + length] == segment).astype(jnp.float32)
        summed = (
            summed
            + weight[offset].astype(jnp.float32)
            * extended[offset : offset + length].astype(jnp.float32)
            * visible[:, None]
        )
    return jax.nn.silu(summed).astype(jnp.bfloat16)


def conv_rows_kernel(rim_ref, x_ref, w_ref, b_ref, vis_ref, o_ref):
    rows = x_ref.shape[0]
    here = x_ref[...].astype(jnp.float32)
    rim = jnp.concatenate(
        [rim_ref[...].astype(jnp.float32), jnp.zeros((rows - rim_ref.shape[0],) + here.shape[1:], jnp.float32)]
    )
    row = lax.broadcasted_iota(jnp.int32, here.shape, 0)
    summed = b_ref[...].astype(jnp.float32) + w_ref[CONV - 1 : CONV, :].astype(jnp.float32) * here
    for offset in range(CONV - 1):
        lag = CONV - 1 - offset
        early = pltpu.roll(rim, rows - offset, 0) if offset else rim
        seen = jnp.where(row < lag, early, pltpu.roll(here, lag, 0))
        summed = summed + w_ref[offset : offset + 1, :].astype(jnp.float32) * seen * vis_ref[offset]
    o_ref[...] = jnp.transpose(jax.nn.silu(summed)).astype(o_ref.dtype)


def conv_rows(rim_vals, values, rim_segment, segment, weight, offset_bias):
    rows, width = values.shape
    ext_segment = jnp.concatenate([rim_segment, segment], axis=0)
    vis = jnp.stack(
        [(ext_segment[k : k + rows] == segment).astype(jnp.float32) for k in range(CONV - 1)]
    )[:, :, None]
    rim8 = jnp.concatenate([rim_vals, jnp.zeros((8 - rim_vals.shape[0], width), rim_vals.dtype)])
    tile = min(width, 2048)
    return pl.pallas_call(
        conv_rows_kernel,
        out_shape=jax.ShapeDtypeStruct((width, rows), jnp.bfloat16),
        grid=(width // tile,),
        in_specs=[
            pl.BlockSpec((8, tile), lambda j: (0, j)),
            pl.BlockSpec((rows, tile), lambda j: (0, j)),
            pl.BlockSpec((CONV, tile), lambda j: (0, j)),
            pl.BlockSpec((1, tile), lambda j: (0, j)),
            pl.BlockSpec((CONV - 1, rows, 1), lambda j: (0, 0, 0)),
        ],
        out_specs=pl.BlockSpec((tile, rows), lambda j: (j, 0)),
        cost_estimate=pl.CostEstimate(
            flops=20 * rows * width, transcendentals=rows * width, bytes_accessed=4 * rows * width
        ),
    )(rim8, values, weight, offset_bias.reshape(1, width), vis).T


def scale_rows_kernel(y_ref, z_ref, s_ref, n_ref, o_ref):
    gated = y_ref[...] * jax.nn.silu(z_ref[...].astype(jnp.float32))
    o_ref[...] = jnp.transpose(gated * s_ref[...] * n_ref[...]).astype(o_ref.dtype)


def scale_rows(y_total, gate, scale, gain):
    rows, width = y_total.shape
    tile = min(width, 2048)
    return pl.pallas_call(
        scale_rows_kernel,
        out_shape=jax.ShapeDtypeStruct((rows, width), jnp.bfloat16),
        grid=(width // tile,),
        in_specs=[
            pl.BlockSpec((tile, rows), lambda j: (j, 0)),
            pl.BlockSpec((tile, rows), lambda j: (j, 0)),
            pl.BlockSpec((1, rows), lambda j: (0, 0)),
            pl.BlockSpec((tile, 1), lambda j: (j, 0)),
        ],
        out_specs=pl.BlockSpec((rows, tile), lambda j: (0, j)),
        cost_estimate=pl.CostEstimate(flops=2 * rows * width, transcendentals=0, bytes_accessed=8 * rows * width),
    )(y_total.T, gate.T, scale[None, :], gain.astype(jnp.float32)[:, None])


def mixing_part(x_group, b_group, c_group, step_size, cum_decay, segment):
    places = jnp.arange(segment.shape[0])
    visible = jnp.logical_and(
        places[:, None] >= places[None, :], segment[:, None] == segment[None, :]
    )
    scores = jnp.einsum("in,jn->ij", c_group, b_group, preferred_element_type=jnp.float32)
    exponent = jnp.where(visible[None], cum_decay[:, :, None] - cum_decay[:, None, :], -jnp.inf)
    mixing = (scores[None] * jnp.exp(exponent) * step_size[:, None, :]).astype(jnp.bfloat16)
    return jnp.einsum("hij,jhp->ihp", mixing, x_group, preferred_element_type=jnp.float32)


def state_part(x_group, b_group, step_size, cum_decay, segment, seg_before):
    closing = cum_decay[:, -1:]
    tail_mask = (segment == segment[-1]).astype(jnp.float32)
    factor = jnp.exp(closing - cum_decay) * step_size * tail_mask[None]
    weighted = (b_group.astype(jnp.float32)[None] * factor[:, :, None]).astype(jnp.bfloat16)
    block_state = jnp.einsum("hjn,jhp->hpn", weighted, x_group, preferred_element_type=jnp.float32)
    transmit = jnp.exp(cum_decay[:, -1]) * (segment[-1] == seg_before).astype(jnp.float32)
    return (block_state, transmit)


def entry_part(c_group, entering, cum_decay, segment, seg_before):
    packed = entering.astype(jnp.bfloat16)
    reach = jnp.exp(cum_decay) * (segment == seg_before).astype(jnp.float32)[None]
    product = jnp.einsum("in,hpn->ihp", c_group, packed, preferred_element_type=jnp.float32)
    return product * jnp.transpose(reach)[:, :, None]


def shifted(value, axis, steps, count):
    return lax.ppermute(value, axis, [(s, s + steps) for s in range(count - steps)])


def scan_round(transmit, state, axis, shift, count):
    far_t, far_s = shifted((transmit, state), axis, shift, count)
    return transmit * far_t, transmit[:, None, None] * far_s + state


def scan_rounds(carry, axis, stride, span, count, far):
    near, needed, rider = far
    carry, rider = lax.optimization_barrier((carry, rider))
    far[2] = rider
    transmit, state = shifted(carry, axis, stride, count)
    covered = 1
    while covered < min(span - 1, near):
        transmit, state = scan_round(transmit, state, axis, stride * covered, count)
        covered *= 2
    if covered < span - 1:

        def rest(carried):
            t, s = carried
            reach = covered
            while reach < span - 1:
                t, s = scan_round(t, s, axis, stride * reach, count)
                reach *= 2
            return t, s

        transmit, state = lax.cond(needed, rest, lambda carried: carried, (transmit, state))
    return state


def gather_round(value, axis, size):
    count = lax.axis_size(axis)
    if count & (count - 1):
        return lax.all_gather(value, axis, tiled=True) if size == 1 else value
    if size >= count:
        return value
    place = lax.axis_index(axis)
    other = lax.ppermute(value, axis, [(s, s ^ size) for s in range(count)])
    return jnp.where(
        (place & size) == 0,
        jnp.concatenate([value, other]),
        jnp.concatenate([other, value]),
    )


def gather_rounds(value, axis, first, last):
    size = 1 << first
    while size < (1 << last):
        value = gather_round(value, axis, size)
        size *= 2
    return value


def long_runs(ids, paired, tok_rows):
    count = lax.axis_size("ctx")
    longest = (count * tok_rows // 4 - 1) // tok_rows
    group = 2 if paired else 1
    near = 1
    while near * group <= longest:
        near *= 2
    window = near * group
    joined = jnp.concatenate([jnp.zeros((1,), jnp.int32), (ids[1:] == ids[:-1]).astype(jnp.int32)])
    if window > count:
        return near, jnp.zeros((), jnp.bool_)
    breaks = jnp.cumsum(1 - joined)
    ahead = jnp.concatenate([jnp.zeros((1,), jnp.int32), breaks[:-window]])
    return near, jnp.any(breaks[window - 1 :] - ahead == 0)


def blockwise(f, items):
    if jax.tree.leaves(items)[0].shape[0] == 1:
        out = f(jax.tree.map(lambda a: a[0], items))
        return jax.tree.map(lambda a: a[None], out)
    return lax.map(f, items)


def device_entry(dev_transmit, dev_state, paired, far):
    count = lax.axis_size("ctx")
    if not paired:
        return scan_rounds((dev_transmit, dev_state), "ctx", 1, count, count, far)
    heads = dev_state.shape[0]
    half = heads // 2
    core = lax.axis_index("ctx") % 2
    swap = [(s, s ^ 1) for s in range(count)]
    own_lo = core * half
    give = lax.dynamic_slice_in_dim(dev_state, half - own_lo, half, 0)
    other_t, other_s = lax.ppermute((dev_transmit, give), "ctx", swap)
    mine_s = lax.dynamic_slice_in_dim(dev_state, own_lo, half, 0)
    mine_t = lax.dynamic_slice_in_dim(dev_transmit, own_lo, half, 0)
    peer_t = lax.dynamic_slice_in_dim(other_t, own_lo, half, 0)
    first = core == 0
    chip_s = jnp.where(first, peer_t[:, None, None] * mine_s + other_s, mine_t[:, None, None] * other_s + mine_s)
    chip_t = mine_t * peer_t
    entering = scan_rounds((chip_t, chip_s), "ctx", 2, count // 2, count, far)
    lead_t = jnp.where(first, mine_t, peer_t)
    lead_s = jnp.where(first, mine_s, other_s)
    second = lead_t[:, None, None] * entering + lead_s
    back = lax.ppermute(jnp.where(first, second, entering), "ctx", swap)
    mine = jnp.where(first, entering, second)
    low = jnp.where(first, mine, back)
    high = jnp.where(first, back, mine)
    return jnp.concatenate([low, high], axis=0)


def chain_states(block_states, transmits, paired, far):

    def advance(carried, item):
        passing, state_now = carried
        transmit, block_state = item
        return (
            (passing * transmit, transmit[:, None, None] * state_now + block_state),
            (passing, state_now),
        )

    start = (jnp.ones_like(transmits[0]), jnp.zeros_like(block_states[0]))
    finals, befores = lax.scan(advance, start, (transmits, block_states))
    entering_dev = device_entry(finals[0], finals[1], paired, far)
    return befores[0][:, :, None, None] * entering_dev[None] + befores[1]


def local(
    paired,
    x_in,
    gate_z,
    bc_in,
    dt_raw,
    dt_bias,
    a_rate,
    skip_d,
    conv_x_w,
    conv_x_b,
    conv_bc_w,
    conv_bc_b,
    norm_gain,
    segment_ids,
):
    tok_rows = x_in.shape[0]
    channels = x_in.shape[1]
    head_count = dt_raw.shape[0]
    block_count = tok_rows // GROUP
    rim_rows = CONV - 1
    bc_width = bc_in.shape[1]
    rims = passed_along(
        jnp.concatenate(
            [
                x_in[tok_rows - rim_rows :],
                bc_in[tok_rows - rim_rows :],
                segment_ids[tok_rows - rim_rows :, None].astype(jnp.bfloat16),
            ],
            axis=1,
        ),
        "ctx",
        1,
    )
    rim_x = rims[:, :channels]
    rim_bc = rims[:, channels : channels + bc_width]
    rim_segment = rims[:, channels + bc_width].astype(jnp.int32)
    ids = gather_rounds(segment_ids[tok_rows - 1 :], "ctx", 0, 2)
    ids, rim_x = lax.optimization_barrier((ids, rim_x))
    x_conv = conv_rows(rim_x, x_in, rim_segment, segment_ids, conv_x_w, conv_x_b)
    ids = gather_rounds(ids, "ctx", 2, 4)
    ids, x_conv = lax.optimization_barrier((ids, x_conv))
    bc_conv = causal_conv(rim_bc, bc_in, rim_segment, segment_ids, conv_bc_w, conv_bc_b)
    step_size = jax.nn.softplus(dt_raw + dt_bias[:, None])
    log_decay = -step_size * a_rate[:, None]
    cum_decay = jnp.transpose(
        jnp.cumsum(log_decay.reshape(head_count, block_count, GROUP), axis=2), (1, 0, 2)
    )
    step_blocks = jnp.transpose(step_size.reshape(head_count, block_count, GROUP), (1, 0, 2))
    seg_blocks = segment_ids.reshape(block_count, GROUP)
    seg_before = jnp.concatenate([rim_segment[rim_rows - 1 :], seg_blocks[:-1, -1]])
    x_blocks = x_conv.reshape(block_count, GROUP, head_count, HEAD_DIM)
    b_blocks = bc_conv[:, :STATE].reshape(block_count, GROUP, STATE)
    c_blocks = bc_conv[:, STATE:].reshape(block_count, GROUP, STATE)

    def state_of(item):
        x_group, b_group, steps_here, decay_here, segment, before = item
        return state_part(x_group, b_group, steps_here, decay_here, segment, before)

    def intra_of(item):
        x_group, b_group, c_group, steps_here, decay_here, segment = item
        return mixing_part(x_group, b_group, c_group, steps_here, decay_here, segment)

    block_states, transmits = blockwise(
        state_of, (x_blocks, b_blocks, step_blocks, cum_decay, seg_blocks, seg_before)
    )
    intra_items = (x_blocks, b_blocks, c_blocks, step_blocks, cum_decay, seg_blocks)
    ids = gather_rounds(ids, "ctx", 4, lax.axis_size("ctx").bit_length())
    ids, block_states = lax.optimization_barrier((ids, block_states))
    far = [*long_runs(ids, paired, tok_rows), intra_items]
    entering = chain_states(block_states, transmits, paired, far)
    y_intra = blockwise(intra_of, far[2])

    def enter_of(item):
        c_group, decay_here, segment, before, entering_here = item
        return entry_part(c_group, entering_here, decay_here, segment, before)

    y_state = blockwise(enter_of, (c_blocks, cum_decay, seg_blocks, seg_before, entering))
    y_blocks = y_intra + y_state
    x_heads = x_conv.reshape(tok_rows, head_count, HEAD_DIM).astype(jnp.float32)
    y_total = y_blocks.reshape(tok_rows, head_count, HEAD_DIM) + skip_d[None, :, None] * x_heads
    gated = y_total.reshape(tok_rows, channels) * jax.nn.silu(gate_z.astype(jnp.float32))
    local_sq = jnp.sum(gated * gated, axis=1)
    total_sq = lax.psum(local_sq, "tp")
    scale = lax.rsqrt(total_sq / INNER + epsilon)
    return scale_rows(y_total.reshape(tok_rows, channels), gate_z, scale, norm_gain)


def cores_paired(mesh):
    row = mesh.devices[:, 0] if mesh.devices.ndim == 2 else mesh.devices.reshape(-1)
    if len(row) % 2:
        return False
    try:
        for lo, hi in zip(row[0::2], row[1::2]):
            if tuple(lo.coords) != tuple(hi.coords) or lo.core_on_chip == hi.core_on_chip:
                return False
    except AttributeError:
        return False
    return True


def solution(mesh):
    in_specs = (
        P("ctx", "tp"),
        P("ctx", "tp"),
        P("ctx", None),
        P("tp", "ctx"),
        P("tp"),
        P("tp"),
        P("tp"),
        P(None, "tp"),
        P("tp"),
        P(),
        P(),
        P("tp"),
        P("ctx"),
    )
    out_specs = P("ctx", "tp")
    paired = cores_paired(mesh)
    return jax.shard_map(functools.partial(local, paired), mesh=mesh, in_specs=in_specs, out_specs=out_specs, check_vma=False)
```

```python
import functools

import jax
import jax.numpy as jnp
from jax import lax
from jax.experimental import pallas as pl
from jax.experimental.pallas import tpu as pltpu
from jax.sharding import PartitionSpec as P

HEAD_DIM = 64
STATE = 128
GROUP = 256
CONV = 4
INNER = 8192


epsilon = 1e-05


def passed_along(value, axis, steps):
    count = lax.axis_size(axis)
    leading, last = (max(0, -steps), min(count, count - steps))
    return lax.ppermute(value, axis, [(source, source + steps) for source in range(leading, last)])


def causal_conv(rim_vals, values, rim_segment, segment, weight, offset_bias):
    extended = jnp.concatenate([rim_vals, values], axis=0)
    ext_segment = jnp.concatenate([rim_segment, segment], axis=0)
    length = values.shape[0]
    summed = jnp.zeros(values.shape, jnp.float32) + offset_bias.astype(jnp.float32)
    for offset in range(CONV):
        visible = (ext_segment[offset : offset + length] == segment).astype(jnp.float32)
        summed = (
            summed
            + weight[offset].astype(jnp.float32)
            * extended[offset : offset + length].astype(jnp.float32)
            * visible[:, None]
        )
    return jax.nn.silu(summed).astype(jnp.bfloat16)


def conv_rows_kernel(rim_ref, x_ref, w_ref, b_ref, vis_ref, o_ref):
    rows = x_ref.shape[0]
    here = x_ref[...].astype(jnp.float32)
    rim = jnp.concatenate(
        [rim_ref[...].astype(jnp.float32), jnp.zeros((rows - rim_ref.shape[0],) + here.shape[1:], jnp.float32)]
    )
    row = lax.broadcasted_iota(jnp.int32, here.shape, 0)
    summed = b_ref[...].astype(jnp.float32) + w_ref[CONV - 1 : CONV, :].astype(jnp.float32) * here
    for offset in range(CONV - 1):
        lag = CONV - 1 - offset
        early = pltpu.roll(rim, rows - offset, 0) if offset else rim
        seen = jnp.where(row < lag, early, pltpu.roll(here, lag, 0))
        summed = summed + w_ref[offset : offset + 1, :].astype(jnp.float32) * seen * vis_ref[offset]
    o_ref[...] = jnp.transpose(jax.nn.silu(summed)).astype(o_ref.dtype)


def conv_rows(rim_vals, values, rim_segment, segment, weight, offset_bias):
    rows, width = values.shape
    ext_segment = jnp.concatenate([rim_segment, segment], axis=0)
    vis = jnp.stack(
        [(ext_segment[k : k + rows] == segment).astype(jnp.float32) for k in range(CONV - 1)]
    )[:, :, None]
    rim8 = jnp.concatenate([rim_vals, jnp.zeros((8 - rim_vals.shape[0], width), rim_vals.dtype)])
    tile = min(width, 4096)
    return pl.pallas_call(
        conv_rows_kernel,
        out_shape=jax.ShapeDtypeStruct((width, rows), jnp.bfloat16),
        grid=(width // tile,),
        in_specs=[
            pl.BlockSpec((8, tile), lambda j: (0, j)),
            pl.BlockSpec((rows, tile), lambda j: (0, j)),
            pl.BlockSpec((CONV, tile), lambda j: (0, j)),
            pl.BlockSpec((1, tile), lambda j: (0, j)),
            pl.BlockSpec((CONV - 1, rows, 1), lambda j: (0, 0, 0)),
        ],
        out_specs=pl.BlockSpec((tile, rows), lambda j: (j, 0)),
        cost_estimate=pl.CostEstimate(
            flops=20 * rows * width, transcendentals=rows * width, bytes_accessed=4 * rows * width
        ),
    )(rim8, values, weight, offset_bias.reshape(1, width), vis).T


def scale_rows_kernel(g_ref, s_ref, n_ref, o_ref):
    o_ref[...] = jnp.transpose(g_ref[...] * s_ref[...] * n_ref[...]).astype(o_ref.dtype)


def scale_rows(gated, scale, gain):
    rows, width = gated.shape
    tile = min(width, 4096)
    return pl.pallas_call(
        scale_rows_kernel,
        out_shape=jax.ShapeDtypeStruct((rows, width), jnp.bfloat16),
        grid=(width // tile,),
        in_specs=[
            pl.BlockSpec((tile, rows), lambda j: (j, 0)),
            pl.BlockSpec((1, rows), lambda j: (0, 0)),
            pl.BlockSpec((tile, 1), lambda j: (j, 0)),
        ],
        out_specs=pl.BlockSpec((rows, tile), lambda j: (0, j)),
        cost_estimate=pl.CostEstimate(flops=2 * rows * width, transcendentals=0, bytes_accessed=6 * rows * width),
    )(gated.T, scale[None, :], gain.astype(jnp.float32)[:, None])


def mixing_part(x_group, b_group, c_group, step_size, cum_decay, segment):
    places = jnp.arange(segment.shape[0])
    visible = jnp.logical_and(
        places[:, None] >= places[None, :], segment[:, None] == segment[None, :]
    )
    scores = jnp.einsum("in,jn->ij", c_group, b_group, preferred_element_type=jnp.float32)
    exponent = jnp.where(visible[None], cum_decay[:, :, None] - cum_decay[:, None, :], -jnp.inf)
    mixing = (scores[None] * jnp.exp(exponent) * step_size[:, None, :]).astype(jnp.bfloat16)
    return jnp.einsum("hij,jhp->ihp", mixing, x_group, preferred_element_type=jnp.float32)


def state_part(x_group, b_group, step_size, cum_decay, segment, seg_before):
    closing = cum_decay[:, -1:]
    tail_mask = (segment == segment[-1]).astype(jnp.float32)
    factor = jnp.exp(closing - cum_decay) * step_size * tail_mask[None]
    weighted = (b_group.astype(jnp.float32)[None] * factor[:, :, None]).astype(jnp.bfloat16)
    block_state = jnp.einsum("hjn,jhp->hpn", weighted, x_group, preferred_element_type=jnp.float32)
    transmit = jnp.exp(cum_decay[:, -1]) * (segment[-1] == seg_before).astype(jnp.float32)
    return (block_state, transmit)


def entry_part(c_group, entering, cum_decay, segment, seg_before):
    packed = entering.astype(jnp.bfloat16)
    reach = jnp.exp(cum_decay) * (segment == seg_before).astype(jnp.float32)[None]
    product = jnp.einsum("in,hpn->ihp", c_group, packed, preferred_element_type=jnp.float32)
    return product * jnp.transpose(reach)[:, :, None]


def shifted(value, axis, steps, count):
    return lax.ppermute(value, axis, [(s, s + steps) for s in range(count - steps)])


def scan_round(transmit, state, axis, shift, count):
    far_t, far_s = shifted((transmit, state), axis, shift, count)
    return transmit * far_t, transmit[:, None, None] * far_s + state


def scan_rounds(carry, axis, stride, span, count, far):
    near, needed, rider = far
    carry, rider = lax.optimization_barrier((carry, rider))
    far[2] = rider
    transmit, state = shifted(carry, axis, stride, count)
    covered = 1
    while covered < min(span - 1, near):
        transmit, state = scan_round(transmit, state, axis, stride * covered, count)
        covered *= 2
    if covered < span - 1:

        def rest(carried):
            t, s = carried
            reach = covered
            while reach < span - 1:
                t, s = scan_round(t, s, axis, stride * reach, count)
                reach *= 2
            return t, s

        transmit, state = lax.cond(needed, rest, lambda carried: carried, (transmit, state))
    return state


def gather_round(value, axis, size):
    count = lax.axis_size(axis)
    if count & (count - 1):
        return lax.all_gather(value, axis, tiled=True) if size == 1 else value
    if size >= count:
        return value
    place = lax.axis_index(axis)
    other = lax.ppermute(value, axis, [(s, s ^ size) for s in range(count)])
    return jnp.where(
        (place & size) == 0,
        jnp.concatenate([value, other]),
        jnp.concatenate([other, value]),
    )


def gather_rounds(value, axis, first, last):
    size = 1 << first
    while size < (1 << last):
        value = gather_round(value, axis, size)
        size *= 2
    return value


def long_runs(ids, paired, tok_rows):
    count = lax.axis_size("ctx")
    longest = (count * tok_rows // 4 - 1) // tok_rows
    group = 2 if paired else 1
    near = 1
    while near * group <= longest:
        near *= 2
    window = near * group
    joined = jnp.concatenate([jnp.zeros((1,), jnp.int32), (ids[1:] == ids[:-1]).astype(jnp.int32)])
    if window > count:
        return near, jnp.zeros((), jnp.bool_)
    breaks = jnp.cumsum(1 - joined)
    ahead = jnp.concatenate([jnp.zeros((1,), jnp.int32), breaks[:-window]])
    return near, jnp.any(breaks[window - 1 :] - ahead == 0)


def blockwise(f, items):
    if jax.tree.leaves(items)[0].shape[0] == 1:
        out = f(jax.tree.map(lambda a: a[0], items))
        return jax.tree.map(lambda a: a[None], out)
    return lax.map(f, items)


def device_entry(dev_transmit, dev_state, paired, far):
    count = lax.axis_size("ctx")
    if not paired:
        return scan_rounds((dev_transmit, dev_state), "ctx", 1, count, count, far)
    heads = dev_state.shape[0]
    half = heads // 2
    core = lax.axis_index("ctx") % 2
    swap = [(s, s ^ 1) for s in range(count)]
    own_lo = core * half
    give = lax.dynamic_slice_in_dim(dev_state, half - own_lo, half, 0)
    other_t, other_s = lax.ppermute((dev_transmit, give), "ctx", swap)
    mine_s = lax.dynamic_slice_in_dim(dev_state, own_lo, half, 0)
    mine_t = lax.dynamic_slice_in_dim(dev_transmit, own_lo, half, 0)
    peer_t = lax.dynamic_slice_in_dim(other_t, own_lo, half, 0)
    first = core == 0
    chip_s = jnp.where(first, peer_t[:, None, None] * mine_s + other_s, mine_t[:, None, None] * other_s + mine_s)
    chip_t = mine_t * peer_t
    entering = scan_rounds((chip_t, chip_s), "ctx", 2, count // 2, count, far)
    lead_t = jnp.where(first, mine_t, peer_t)
    lead_s = jnp.where(first, mine_s, other_s)
    second = lead_t[:, None, None] * entering + lead_s
    back = lax.ppermute(jnp.where(first, second, entering), "ctx", swap)
    mine = jnp.where(first, entering, second)
    low = jnp.where(first, mine, back)
    high = jnp.where(first, back, mine)
    return jnp.concatenate([low, high], axis=0)


def chain_states(block_states, transmits, paired, far):

    def advance(carried, item):
        passing, state_now = carried
        transmit, block_state = item
        return (
            (passing * transmit, transmit[:, None, None] * state_now + block_state),
            (passing, state_now),
        )

    start = (jnp.ones_like(transmits[0]), jnp.zeros_like(block_states[0]))
    finals, befores = lax.scan(advance, start, (transmits, block_states))
    entering_dev = device_entry(finals[0], finals[1], paired, far)
    return befores[0][:, :, None, None] * entering_dev[None] + befores[1]


def local(
    paired,
    x_in,
    gate_z,
    bc_in,
    dt_raw,
    dt_bias,
    a_rate,
    skip_d,
    conv_x_w,
    conv_x_b,
    conv_bc_w,
    conv_bc_b,
    norm_gain,
    segment_ids,
):
    tok_rows = x_in.shape[0]
    channels = x_in.shape[1]
    head_count = dt_raw.shape[0]
    block_count = tok_rows // GROUP
    rim_rows = CONV - 1
    bc_width = bc_in.shape[1]
    rims = passed_along(
        jnp.concatenate(
            [
                x_in[tok_rows - rim_rows :],
                bc_in[tok_rows - rim_rows :],
                segment_ids[tok_rows - rim_rows :, None].astype(jnp.bfloat16),
            ],
            axis=1,
        ),
        "ctx",
        1,
    )
    rim_x = rims[:, :channels]
    rim_bc = rims[:, channels : channels + bc_width]
    rim_segment = rims[:, channels + bc_width].astype(jnp.int32)
    ids = gather_rounds(segment_ids[tok_rows - 1 :], "ctx", 0, 2)
    ids, rim_x = lax.optimization_barrier((ids, rim_x))
    x_conv = conv_rows(rim_x, x_in, rim_segment, segment_ids, conv_x_w, conv_x_b)
    ids = gather_rounds(ids, "ctx", 2, 4)
    ids, x_conv = lax.optimization_barrier((ids, x_conv))
    bc_conv = causal_conv(rim_bc, bc_in, rim_segment, segment_ids, conv_bc_w, conv_bc_b)
    step_size = jax.nn.softplus(dt_raw + dt_bias[:, None])
    log_decay = -step_size * a_rate[:, None]
    cum_decay = jnp.transpose(
        jnp.cumsum(log_decay.reshape(head_count, block_count, GROUP), axis=2), (1, 0, 2)
    )
    step_blocks = jnp.transpose(step_size.reshape(head_count, block_count, GROUP), (1, 0, 2))
    seg_blocks = segment_ids.reshape(block_count, GROUP)
    seg_before = jnp.concatenate([rim_segment[rim_rows - 1 :], seg_blocks[:-1, -1]])
    x_blocks = x_conv.reshape(block_count, GROUP, head_count, HEAD_DIM)
    b_blocks = bc_conv[:, :STATE].reshape(block_count, GROUP, STATE)
    c_blocks = bc_conv[:, STATE:].reshape(block_count, GROUP, STATE)

    def state_of(item):
        x_group, b_group, steps_here, decay_here, segment, before = item
        return state_part(x_group, b_group, steps_here, decay_here, segment, before)

    def intra_of(item):
        x_group, b_group, c_group, steps_here, decay_here, segment = item
        return mixing_part(x_group, b_group, c_group, steps_here, decay_here, segment)

    block_states, transmits = blockwise(
        state_of, (x_blocks, b_blocks, step_blocks, cum_decay, seg_blocks, seg_before)
    )
    intra_items = (x_blocks, b_blocks, c_blocks, step_blocks, cum_decay, seg_blocks)
    ids = gather_rounds(ids, "ctx", 4, lax.axis_size("ctx").bit_length())
    ids, block_states = lax.optimization_barrier((ids, block_states))
    far = [*long_runs(ids, paired, tok_rows), intra_items]
    entering = chain_states(block_states, transmits, paired, far)
    y_intra = blockwise(intra_of, far[2])

    def enter_of(item):
        c_group, decay_here, segment, before, entering_here = item
        return entry_part(c_group, entering_here, decay_here, segment, before)

    y_state = blockwise(enter_of, (c_blocks, cum_decay, seg_blocks, seg_before, entering))
    y_blocks = y_intra + y_state
    x_heads = x_conv.reshape(tok_rows, head_count, HEAD_DIM).astype(jnp.float32)
    y_total = y_blocks.reshape(tok_rows, head_count, HEAD_DIM) + skip_d[None, :, None] * x_heads
    gated = y_total.reshape(tok_rows, channels) * jax.nn.silu(gate_z.astype(jnp.float32))
    local_sq = jnp.sum(gated * gated, axis=1)
    total_sq = lax.psum(local_sq, "tp")
    scale = lax.rsqrt(total_sq / INNER + epsilon)
    return scale_rows(gated, scale, norm_gain)


def cores_paired(mesh):
    row = mesh.devices[:, 0] if mesh.devices.ndim == 2 else mesh.devices.reshape(-1)
    if len(row) % 2:
        return False
    try:
        for lo, hi in zip(row[0::2], row[1::2]):
            if tuple(lo.coords) != tuple(hi.coords) or lo.core_on_chip == hi.core_on_chip:
                return False
    except AttributeError:
        return False
    return True


def solution(mesh):
    in_specs = (
        P("ctx", "tp"),
        P("ctx", "tp"),
        P("ctx", None),
        P("tp", "ctx"),
        P("tp"),
        P("tp"),
        P("tp"),
        P(None, "tp"),
        P("tp"),
        P(),
        P(),
        P("tp"),
        P("ctx"),
    )
    out_specs = P("ctx", "tp")
    paired = cores_paired(mesh)
    return jax.shard_map(functools.partial(local, paired), mesh=mesh, in_specs=in_specs, out_specs=out_specs, check_vma=False)
```

```python
import functools

import jax
import jax.numpy as jnp
from jax import lax
from jax.experimental import pallas as pl
from jax.experimental.pallas import tpu as pltpu
from jax.sharding import PartitionSpec as P

HEAD_DIM = 64
STATE = 128
GROUP = 256
CONV = 4
INNER = 8192


epsilon = 1e-05


def passed_along(value, axis, steps):
    count = lax.axis_size(axis)
    leading, last = (max(0, -steps), min(count, count - steps))
    return lax.ppermute(value, axis, [(source, source + steps) for source in range(leading, last)])


def causal_conv(rim_vals, values, rim_segment, segment, weight, offset_bias):
    extended = jnp.concatenate([rim_vals, values], axis=0)
    ext_segment = jnp.concatenate([rim_segment, segment], axis=0)
    length = values.shape[0]
    summed = jnp.zeros(values.shape, jnp.float32) + offset_bias.astype(jnp.float32)
    for offset in range(CONV):
        visible = (ext_segment[offset : offset + length] == segment).astype(jnp.float32)
        summed = (
            summed
            + weight[offset].astype(jnp.float32)
            * extended[offset : offset + length].astype(jnp.float32)
            * visible[:, None]
        )
    return jax.nn.silu(summed).astype(jnp.bfloat16)


def conv_rows_kernel(rim_ref, x_ref, w_ref, b_ref, vis_ref, o_ref):
    rows = x_ref.shape[0]
    here = x_ref[...].astype(jnp.float32)
    rim = jnp.concatenate(
        [rim_ref[...].astype(jnp.float32), jnp.zeros((rows - rim_ref.shape[0],) + here.shape[1:], jnp.float32)]
    )
    row = lax.broadcasted_iota(jnp.int32, here.shape, 0)
    summed = b_ref[...].astype(jnp.float32) + w_ref[CONV - 1 : CONV, :].astype(jnp.float32) * here
    for offset in range(CONV - 1):
        lag = CONV - 1 - offset
        early = pltpu.roll(rim, rows - offset, 0) if offset else rim
        seen = jnp.where(row < lag, early, pltpu.roll(here, lag, 0))
        summed = summed + w_ref[offset : offset + 1, :].astype(jnp.float32) * seen * vis_ref[offset]
    o_ref[...] = jnp.transpose(jax.nn.silu(summed)).astype(o_ref.dtype)


def conv_rows(rim_vals, values, rim_segment, segment, weight, offset_bias):
    rows, width = values.shape
    ext_segment = jnp.concatenate([rim_segment, segment], axis=0)
    vis = jnp.stack(
        [(ext_segment[k : k + rows] == segment).astype(jnp.float32) for k in range(CONV - 1)]
    )[:, :, None]
    rim8 = jnp.concatenate([rim_vals, jnp.zeros((8 - rim_vals.shape[0], width), rim_vals.dtype)])
    tile = min(width, 2048)
    return pl.pallas_call(
        conv_rows_kernel,
        out_shape=jax.ShapeDtypeStruct((width, rows), jnp.bfloat16),
        grid=(width // tile,),
        in_specs=[
            pl.BlockSpec((8, tile), lambda j: (0, j)),
            pl.BlockSpec((rows, tile), lambda j: (0, j)),
            pl.BlockSpec((CONV, tile), lambda j: (0, j)),
            pl.BlockSpec((1, tile), lambda j: (0, j)),
            pl.BlockSpec((CONV - 1, rows, 1), lambda j: (0, 0, 0)),
        ],
        out_specs=pl.BlockSpec((tile, rows), lambda j: (j, 0)),
        cost_estimate=pl.CostEstimate(
            flops=20 * rows * width, transcendentals=rows * width, bytes_accessed=4 * rows * width
        ),
    )(rim8, values, weight, offset_bias.reshape(1, width), vis).T


def scale_rows_kernel(g_ref, s_ref, n_ref, o_ref):
    o_ref[...] = jnp.transpose(g_ref[...] * s_ref[...] * n_ref[...]).astype(o_ref.dtype)


def scale_rows(gated, scale, gain):
    rows, width = gated.shape
    tile = min(width, 2048)
    return pl.pallas_call(
        scale_rows_kernel,
        out_shape=jax.ShapeDtypeStruct((rows, width), jnp.bfloat16),
        grid=(width // tile,),
        in_specs=[
            pl.BlockSpec((tile, rows), lambda j: (j, 0)),
            pl.BlockSpec((1, rows), lambda j: (0, 0)),
            pl.BlockSpec((tile, 1), lambda j: (j, 0)),
        ],
        out_specs=pl.BlockSpec((rows, tile), lambda j: (0, j)),
        cost_estimate=pl.CostEstimate(flops=2 * rows * width, transcendentals=0, bytes_accessed=6 * rows * width),
    )(gated.T, scale[None, :], gain.astype(jnp.float32)[:, None])


def mixing_part(x_group, b_group, c_group, step_size, cum_decay, segment):
    places = jnp.arange(segment.shape[0])
    visible = jnp.logical_and(
        places[:, None] >= places[None, :], segment[:, None] == segment[None, :]
    )
    scores = jnp.einsum("in,jn->ij", c_group, b_group, preferred_element_type=jnp.float32)
    exponent = jnp.where(visible[None], cum_decay[:, :, None] - cum_decay[:, None, :], -jnp.inf)
    mixing = (scores[None] * jnp.exp(exponent) * step_size[:, None, :]).astype(jnp.bfloat16)
    return jnp.einsum("hij,jhp->ihp", mixing, x_group, preferred_element_type=jnp.float32)


def state_part(x_group, b_group, step_size, cum_decay, segment, seg_before):
    closing = cum_decay[:, -1:]
    tail_mask = (segment == segment[-1]).astype(jnp.float32)
    factor = jnp.exp(closing - cum_decay) * step_size * tail_mask[None]
    weighted = (b_group.astype(jnp.float32)[None] * factor[:, :, None]).astype(jnp.bfloat16)
    block_state = jnp.einsum("hjn,jhp->hpn", weighted, x_group, preferred_element_type=jnp.float32)
    transmit = jnp.exp(cum_decay[:, -1]) * (segment[-1] == seg_before).astype(jnp.float32)
    return (block_state, transmit)


def entry_part(c_group, entering, cum_decay, segment, seg_before):
    packed = entering.astype(jnp.bfloat16)
    reach = jnp.exp(cum_decay) * (segment == seg_before).astype(jnp.float32)[None]
    product = jnp.einsum("in,hpn->ihp", c_group, packed, preferred_element_type=jnp.float32)
    return product * jnp.transpose(reach)[:, :, None]


def shifted(value, axis, steps, count):
    return lax.ppermute(value, axis, [(s, s + steps) for s in range(count - steps)])


def scan_round(transmit, state, axis, shift, count):
    far_t, far_s = shifted((transmit, state), axis, shift, count)
    return transmit * far_t, transmit[:, None, None] * far_s + state


def scan_rounds(carry, axis, stride, span, count, far):
    near, needed, rider = far
    carry, rider = lax.optimization_barrier((carry, rider))
    far[2] = rider
    transmit, state = shifted(carry, axis, stride, count)
    covered = 1
    while covered < min(span - 1, near):
        transmit, state = scan_round(transmit, state, axis, stride * covered, count)
        covered *= 2
    if covered < span - 1:

        def rest(carried):
            t, s = carried
            reach = covered
            while reach < span - 1:
                t, s = scan_round(t, s, axis, stride * reach, count)
                reach *= 2
            return t, s

        transmit, state = lax.cond(needed, rest, lambda carried: carried, (transmit, state))
    return state


def gather_round(value, axis, size):
    count = lax.axis_size(axis)
    if count & (count - 1):
        return lax.all_gather(value, axis, tiled=True) if size == 1 else value
    if size >= count:
        return value
    place = lax.axis_index(axis)
    other = lax.ppermute(value, axis, [(s, s ^ size) for s in range(count)])
    return jnp.where(
        (place & size) == 0,
        jnp.concatenate([value, other]),
        jnp.concatenate([other, value]),
    )


def gather_rounds(value, axis, first, last):
    size = 1 << first
    while size < (1 << last):
        value = gather_round(value, axis, size)
        size *= 2
    return value


def long_runs(ids, paired, tok_rows):
    count = lax.axis_size("ctx")
    longest = (count * tok_rows // 4 - 1) // tok_rows
    group = 2 if paired else 1
    near = 1
    while near * group <= longest:
        near *= 2
    window = near * group
    joined = jnp.concatenate([jnp.zeros((1,), jnp.int32), (ids[1:] == ids[:-1]).astype(jnp.int32)])
    if window > count:
        return near, jnp.zeros((), jnp.bool_)
    breaks = jnp.cumsum(1 - joined)
    ahead = jnp.concatenate([jnp.zeros((1,), jnp.int32), breaks[:-window]])
    return near, jnp.any(breaks[window - 1 :] - ahead == 0)


def blockwise(f, items):
    if jax.tree.leaves(items)[0].shape[0] == 1:
        out = f(jax.tree.map(lambda a: a[0], items))
        return jax.tree.map(lambda a: a[None], out)
    return lax.map(f, items)


def device_entry(dev_transmit, dev_state, paired, far):
    count = lax.axis_size("ctx")
    if not paired:
        return scan_rounds((dev_transmit, dev_state), "ctx", 1, count, count, far)
    heads = dev_state.shape[0]
    half = heads // 2
    core = lax.axis_index("ctx") % 2
    swap = [(s, s ^ 1) for s in range(count)]
    own_lo = core * half
    other_t, other_all = lax.ppermute((dev_transmit, dev_state), "ctx", swap)
    other_s = lax.dynamic_slice_in_dim(other_all, own_lo, half, 0)
    mine_s = lax.dynamic_slice_in_dim(dev_state, own_lo, half, 0)
    mine_t = lax.dynamic_slice_in_dim(dev_transmit, own_lo, half, 0)
    peer_t = lax.dynamic_slice_in_dim(other_t, own_lo, half, 0)
    first = core == 0
    chip_s = jnp.where(first, peer_t[:, None, None] * mine_s + other_s, mine_t[:, None, None] * other_s + mine_s)
    chip_t = mine_t * peer_t
    entering = scan_rounds((chip_t, chip_s), "ctx", 2, count // 2, count, far)
    lead_t = jnp.where(first, mine_t, peer_t)
    lead_s = jnp.where(first, mine_s, other_s)
    second = lead_t[:, None, None] * entering + lead_s
    back = lax.ppermute(jnp.where(first, second, entering), "ctx", swap)
    mine = jnp.where(first, entering, second)
    low = jnp.where(first, mine, back)
    high = jnp.where(first, back, mine)
    return jnp.concatenate([low, high], axis=0)


def chain_states(block_states, transmits, paired, far):

    def advance(carried, item):
        passing, state_now = carried
        transmit, block_state = item
        return (
            (passing * transmit, transmit[:, None, None] * state_now + block_state),
            (passing, state_now),
        )

    start = (jnp.ones_like(transmits[0]), jnp.zeros_like(block_states[0]))
    finals, befores = lax.scan(advance, start, (transmits, block_states))
    entering_dev = device_entry(finals[0], finals[1], paired, far)
    return befores[0][:, :, None, None] * entering_dev[None] + befores[1]


def local(
    paired,
    x_in,
    gate_z,
    bc_in,
    dt_raw,
    dt_bias,
    a_rate,
    skip_d,
    conv_x_w,
    conv_x_b,
    conv_bc_w,
    conv_bc_b,
    norm_gain,
    segment_ids,
):
    tok_rows = x_in.shape[0]
    channels = x_in.shape[1]
    head_count = dt_raw.shape[0]
    block_count = tok_rows // GROUP
    rim_rows = CONV - 1
    bc_width = bc_in.shape[1]
    rims = passed_along(
        jnp.concatenate(
            [
                x_in[tok_rows - rim_rows :],
                bc_in[tok_rows - rim_rows :],
                segment_ids[tok_rows - rim_rows :, None].astype(jnp.bfloat16),
            ],
            axis=1,
        ),
        "ctx",
        1,
    )
    rim_x = rims[:, :channels]
    rim_bc = rims[:, channels : channels + bc_width]
    rim_segment = rims[:, channels + bc_width].astype(jnp.int32)
    ids = gather_rounds(segment_ids[tok_rows - 1 :], "ctx", 0, 2)
    ids, rim_x = lax.optimization_barrier((ids, rim_x))
    x_conv = conv_rows(rim_x, x_in, rim_segment, segment_ids, conv_x_w, conv_x_b)
    ids = gather_rounds(ids, "ctx", 2, 4)
    ids, x_conv = lax.optimization_barrier((ids, x_conv))
    bc_conv = causal_conv(rim_bc, bc_in, rim_segment, segment_ids, conv_bc_w, conv_bc_b)
    step_size = jax.nn.softplus(dt_raw + dt_bias[:, None])
    log_decay = -step_size * a_rate[:, None]
    cum_decay = jnp.transpose(
        jnp.cumsum(log_decay.reshape(head_count, block_count, GROUP), axis=2), (1, 0, 2)
    )
    step_blocks = jnp.transpose(step_size.reshape(head_count, block_count, GROUP), (1, 0, 2))
    seg_blocks = segment_ids.reshape(block_count, GROUP)
    seg_before = jnp.concatenate([rim_segment[rim_rows - 1 :], seg_blocks[:-1, -1]])
    x_blocks = x_conv.reshape(block_count, GROUP, head_count, HEAD_DIM)
    b_blocks = bc_conv[:, :STATE].reshape(block_count, GROUP, STATE)
    c_blocks = bc_conv[:, STATE:].reshape(block_count, GROUP, STATE)

    def state_of(item):
        x_group, b_group, steps_here, decay_here, segment, before = item
        return state_part(x_group, b_group, steps_here, decay_here, segment, before)

    def intra_of(item):
        x_group, b_group, c_group, steps_here, decay_here, segment = item
        return mixing_part(x_group, b_group, c_group, steps_here, decay_here, segment)

    block_states, transmits = blockwise(
        state_of, (x_blocks, b_blocks, step_blocks, cum_decay, seg_blocks, seg_before)
    )
    intra_items = (x_blocks, b_blocks, c_blocks, step_blocks, cum_decay, seg_blocks)
    ids = gather_rounds(ids, "ctx", 4, lax.axis_size("ctx").bit_length())
    ids, block_states = lax.optimization_barrier((ids, block_states))
    far = [*long_runs(ids, paired, tok_rows), intra_items]
    entering = chain_states(block_states, transmits, paired, far)
    y_intra = blockwise(intra_of, far[2])

    def enter_of(item):
        c_group, decay_here, segment, before, entering_here = item
        return entry_part(c_group, entering_here, decay_here, segment, before)

    y_state = blockwise(enter_of, (c_blocks, cum_decay, seg_blocks, seg_before, entering))
    y_blocks = y_intra + y_state
    x_heads = x_conv.reshape(tok_rows, head_count, HEAD_DIM).astype(jnp.float32)
    y_total = y_blocks.reshape(tok_rows, head_count, HEAD_DIM) + skip_d[None, :, None] * x_heads
    gated = y_total.reshape(tok_rows, channels) * jax.nn.silu(gate_z.astype(jnp.float32))
    local_sq = jnp.sum(gated * gated, axis=1)
    total_sq = lax.psum(local_sq, "tp")
    scale = lax.rsqrt(total_sq / INNER + epsilon)
    return scale_rows(gated, scale, norm_gain)


def cores_paired(mesh):
    row = mesh.devices[:, 0] if mesh.devices.ndim == 2 else mesh.devices.reshape(-1)
    if len(row) % 2:
        return False
    try:
        for lo, hi in zip(row[0::2], row[1::2]):
            if tuple(lo.coords) != tuple(hi.coords) or lo.core_on_chip == hi.core_on_chip:
                return False
    except AttributeError:
        return False
    return True


def solution(mesh):
    in_specs = (
        P("ctx", "tp"),
        P("ctx", "tp"),
        P("ctx", None),
        P("tp", "ctx"),
        P("tp"),
        P("tp"),
        P("tp"),
        P(None, "tp"),
        P("tp"),
        P(),
        P(),
        P("tp"),
        P("ctx"),
    )
    out_specs = P("ctx", "tp")
    paired = cores_paired(mesh)
    return jax.shard_map(functools.partial(local, paired), mesh=mesh, in_specs=in_specs, out_specs=out_specs, check_vma=False)
```

```python
import functools

import jax
import jax.numpy as jnp
from jax import lax
from jax.experimental import pallas as pl
from jax.experimental.pallas import tpu as pltpu
from jax.sharding import PartitionSpec as P

HEAD_DIM = 64
STATE = 128
GROUP = 256
CONV = 4
INNER = 8192


epsilon = 1e-05


def passed_along(value, axis, steps):
    count = lax.axis_size(axis)
    leading, last = (max(0, -steps), min(count, count - steps))
    return lax.ppermute(value, axis, [(source, source + steps) for source in range(leading, last)])


def causal_conv(rim_vals, values, rim_segment, segment, weight, offset_bias):
    extended = jnp.concatenate([rim_vals, values], axis=0)
    ext_segment = jnp.concatenate([rim_segment, segment], axis=0)
    length = values.shape[0]
    summed = jnp.zeros(values.shape, jnp.float32) + offset_bias.astype(jnp.float32)
    for offset in range(CONV):
        visible = (ext_segment[offset : offset + length] == segment).astype(jnp.float32)
        summed = (
            summed
            + weight[offset].astype(jnp.float32)
            * extended[offset : offset + length].astype(jnp.float32)
            * visible[:, None]
        )
    return jax.nn.silu(summed).astype(jnp.bfloat16)


def conv_rows_kernel(rim_ref, x_ref, w_ref, b_ref, vis_ref, o_ref):
    rows = x_ref.shape[0]
    here = x_ref[...].astype(jnp.float32)
    rim = jnp.concatenate(
        [rim_ref[...].astype(jnp.float32), jnp.zeros((rows - rim_ref.shape[0],) + here.shape[1:], jnp.float32)]
    )
    row = lax.broadcasted_iota(jnp.int32, here.shape, 0)
    summed = b_ref[...].astype(jnp.float32) + w_ref[CONV - 1 : CONV, :].astype(jnp.float32) * here
    for offset in range(CONV - 1):
        lag = CONV - 1 - offset
        early = pltpu.roll(rim, rows - offset, 0) if offset else rim
        seen = jnp.where(row < lag, early, pltpu.roll(here, lag, 0))
        summed = summed + w_ref[offset : offset + 1, :].astype(jnp.float32) * seen * vis_ref[offset]
    o_ref[...] = jnp.transpose(jax.nn.silu(summed)).astype(o_ref.dtype)


def conv_rows(rim_vals, values, rim_segment, segment, weight, offset_bias):
    rows, width = values.shape
    ext_segment = jnp.concatenate([rim_segment, segment], axis=0)
    vis = jnp.stack(
        [(ext_segment[k : k + rows] == segment).astype(jnp.float32) for k in range(CONV - 1)]
    )[:, :, None]
    rim8 = jnp.concatenate([rim_vals, jnp.zeros((8 - rim_vals.shape[0], width), rim_vals.dtype)])
    tile = min(width, 2048)
    return pl.pallas_call(
        conv_rows_kernel,
        out_shape=jax.ShapeDtypeStruct((width, rows), jnp.bfloat16),
        grid=(width // tile,),
        in_specs=[
            pl.BlockSpec((8, tile), lambda j: (0, j)),
            pl.BlockSpec((rows, tile), lambda j: (0, j)),
            pl.BlockSpec((CONV, tile), lambda j: (0, j)),
            pl.BlockSpec((1, tile), lambda j: (0, j)),
            pl.BlockSpec((CONV - 1, rows, 1), lambda j: (0, 0, 0)),
        ],
        out_specs=pl.BlockSpec((tile, rows), lambda j: (j, 0)),
        cost_estimate=pl.CostEstimate(
            flops=20 * rows * width, transcendentals=rows * width, bytes_accessed=4 * rows * width
        ),
    )(rim8, values, weight, offset_bias.reshape(1, width), vis).T


def scale_rows_kernel(g_ref, s_ref, n_ref, o_ref):
    o_ref[...] = jnp.transpose(g_ref[...] * s_ref[...] * n_ref[...]).astype(o_ref.dtype)


def scale_rows(gated, scale, gain):
    rows, width = gated.shape
    tile = min(width, 2048)
    return pl.pallas_call(
        scale_rows_kernel,
        out_shape=jax.ShapeDtypeStruct((rows, width), jnp.bfloat16),
        grid=(width // tile,),
        in_specs=[
            pl.BlockSpec((tile, rows), lambda j: (j, 0)),
            pl.BlockSpec((1, rows), lambda j: (0, 0)),
            pl.BlockSpec((tile, 1), lambda j: (j, 0)),
        ],
        out_specs=pl.BlockSpec((rows, tile), lambda j: (0, j)),
        cost_estimate=pl.CostEstimate(flops=2 * rows * width, transcendentals=0, bytes_accessed=6 * rows * width),
    )(gated.T, scale[None, :], gain.astype(jnp.float32)[:, None])


def mixing_part(x_group, b_group, c_group, step_size, cum_decay, segment):
    places = jnp.arange(segment.shape[0])
    visible = jnp.logical_and(
        places[:, None] >= places[None, :], segment[:, None] == segment[None, :]
    )
    scores = jnp.einsum("in,jn->ij", c_group, b_group, preferred_element_type=jnp.float32)
    exponent = jnp.where(visible[None], cum_decay[:, :, None] - cum_decay[:, None, :], -jnp.inf)
    mixing = (scores[None] * jnp.exp(exponent) * step_size[:, None, :]).astype(jnp.bfloat16)
    return jnp.einsum("hij,jhp->ihp", mixing, x_group, preferred_element_type=jnp.float32)


def state_part(x_group, b_group, step_size, cum_decay, segment, seg_before):
    closing = cum_decay[:, -1:]
    tail_mask = (segment == segment[-1]).astype(jnp.float32)
    factor = jnp.exp(closing - cum_decay) * step_size * tail_mask[None]
    weighted = (b_group.astype(jnp.float32)[None] * factor[:, :, None]).astype(jnp.bfloat16)
    block_state = jnp.einsum("hjn,jhp->hpn", weighted, x_group, preferred_element_type=jnp.float32)
    transmit = jnp.exp(cum_decay[:, -1]) * (segment[-1] == seg_before).astype(jnp.float32)
    return (block_state, transmit)


def entry_part(c_group, entering, cum_decay, segment, seg_before):
    packed = entering.astype(jnp.bfloat16)
    reach = jnp.exp(cum_decay) * (segment == seg_before).astype(jnp.float32)[None]
    product = jnp.einsum("in,hpn->ihp", c_group, packed, preferred_element_type=jnp.float32)
    return product * jnp.transpose(reach)[:, :, None]


def shifted(value, axis, steps, count):
    return lax.ppermute(value, axis, [(s, s + steps) for s in range(count - steps)])


def scan_round(transmit, state, axis, shift, count):
    far_t, far_s = shifted((transmit, state), axis, shift, count)
    return transmit * far_t, transmit[:, None, None] * far_s + state


def scan_rounds(carry, axis, stride, span, count, far):
    near, needed, rider = far
    carry, rider = lax.optimization_barrier((carry, rider))
    far[2] = rider
    transmit, state = shifted(carry, axis, stride, count)
    covered = 1
    while covered < min(span - 1, near):
        transmit, state = scan_round(transmit, state, axis, stride * covered, count)
        covered *= 2
    if covered < span - 1:

        def rest(carried):
            t, s = carried
            reach = covered
            while reach < span - 1:
                t, s = scan_round(t, s, axis, stride * reach, count)
                reach *= 2
            return t, s

        transmit, state = lax.cond(needed, rest, lambda carried: carried, (transmit, state))
    return state


def gather_round(value, axis, size):
    count = lax.axis_size(axis)
    if count & (count - 1):
        return lax.all_gather(value, axis, tiled=True) if size == 1 else value
    if size >= count:
        return value
    place = lax.axis_index(axis)
    other = lax.ppermute(value, axis, [(s, s ^ size) for s in range(count)])
    return jnp.where(
        (place & size) == 0,
        jnp.concatenate([value, other]),
        jnp.concatenate([other, value]),
    )


def gather_rounds(value, axis, first, last):
    size = 1 << first
    while size < (1 << last):
        value = gather_round(value, axis, size)
        size *= 2
    return value


def long_runs(ids, paired, tok_rows):
    count = lax.axis_size("ctx")
    longest = (count * tok_rows // 4 - 1) // tok_rows
    group = 2 if paired else 1
    near = 1
    while near * group <= longest:
        near *= 2
    window = near * group
    joined = jnp.concatenate([jnp.zeros((1,), jnp.int32), (ids[1:] == ids[:-1]).astype(jnp.int32)])
    if window > count:
        return near, jnp.zeros((), jnp.bool_)
    breaks = jnp.cumsum(1 - joined)
    ahead = jnp.concatenate([jnp.zeros((1,), jnp.int32), breaks[:-window]])
    return near, jnp.any(breaks[window - 1 :] - ahead == 0)


def blockwise(f, items):
    if jax.tree.leaves(items)[0].shape[0] == 1:
        out = f(jax.tree.map(lambda a: a[0], items))
        return jax.tree.map(lambda a: a[None], out)
    return lax.map(f, items)


def device_entry(dev_transmit, dev_state, paired, far):
    count = lax.axis_size("ctx")
    if not paired:
        return scan_rounds((dev_transmit, dev_state), "ctx", 1, count, count, far)
    heads = dev_state.shape[0]
    half = heads // 2
    core = lax.axis_index("ctx") % 2
    swap = [(s, s ^ 1) for s in range(count)]
    own_lo = core * half
    give = lax.dynamic_slice_in_dim(dev_state, half - own_lo, half, 0)
    other_t, other_s = lax.ppermute((dev_transmit, give), "ctx", swap)
    mine_s = lax.dynamic_slice_in_dim(dev_state, own_lo, half, 0)
    mine_t = lax.dynamic_slice_in_dim(dev_transmit, own_lo, half, 0)
    peer_t = lax.dynamic_slice_in_dim(other_t, own_lo, half, 0)
    first = core == 0
    chip_s = jnp.where(first, peer_t[:, None, None] * mine_s + other_s, mine_t[:, None, None] * other_s + mine_s)
    chip_t = mine_t * peer_t
    entering = scan_rounds((chip_t, chip_s), "ctx", 2, count // 2, count, far)
    lead_t = jnp.where(first, mine_t, peer_t)
    lead_s = jnp.where(first, mine_s, other_s)
    second = lead_t[:, None, None] * entering + lead_s
    back = lax.ppermute(jnp.where(first, second, entering), "ctx", swap)
    mine = jnp.where(first, entering, second)
    low = jnp.where(first, mine, back)
    high = jnp.where(first, back, mine)
    return jnp.concatenate([low, high], axis=0)


def chain_states(block_states, transmits, paired, far):

    def advance(carried, item):
        passing, state_now = carried
        transmit, block_state = item
        return (
            (passing * transmit, transmit[:, None, None] * state_now + block_state),
            (passing, state_now),
        )

    start = (jnp.ones_like(transmits[0]), jnp.zeros_like(block_states[0]))
    finals, befores = lax.scan(advance, start, (transmits, block_states))
    entering_dev = device_entry(finals[0], finals[1], paired, far)
    return befores[0][:, :, None, None] * entering_dev[None] + befores[1]


def local(
    paired,
    x_in,
    gate_z,
    bc_in,
    dt_raw,
    dt_bias,
    a_rate,
    skip_d,
    conv_x_w,
    conv_x_b,
    conv_bc_w,
    conv_bc_b,
    norm_gain,
    segment_ids,
):
    tok_rows = x_in.shape[0]
    channels = x_in.shape[1]
    head_count = dt_raw.shape[0]
    block_count = tok_rows // GROUP
    rim_rows = CONV - 1
    bc_width = bc_in.shape[1]
    rims = passed_along(
        jnp.concatenate(
            [
                x_in[tok_rows - rim_rows :],
                bc_in[tok_rows - rim_rows :],
                segment_ids[tok_rows - rim_rows :, None].astype(jnp.bfloat16),
            ],
            axis=1,
        ),
        "ctx",
        1,
    )
    rim_x = rims[:, :channels]
    rim_bc = rims[:, channels : channels + bc_width]
    rim_segment = rims[:, channels + bc_width].astype(jnp.int32)
    x_conv = conv_rows(rim_x, x_in, rim_segment, segment_ids, conv_x_w, conv_x_b)
    ids = gather_rounds(segment_ids[tok_rows - 1 :], "ctx", 0, 3)
    ids, x_conv = lax.optimization_barrier((ids, x_conv))
    bc_conv = causal_conv(rim_bc, bc_in, rim_segment, segment_ids, conv_bc_w, conv_bc_b)
    step_size = jax.nn.softplus(dt_raw + dt_bias[:, None])
    log_decay = -step_size * a_rate[:, None]
    cum_decay = jnp.transpose(
        jnp.cumsum(log_decay.reshape(head_count, block_count, GROUP), axis=2), (1, 0, 2)
    )
    step_blocks = jnp.transpose(step_size.reshape(head_count, block_count, GROUP), (1, 0, 2))
    seg_blocks = segment_ids.reshape(block_count, GROUP)
    seg_before = jnp.concatenate([rim_segment[rim_rows - 1 :], seg_blocks[:-1, -1]])
    x_blocks = x_conv.reshape(block_count, GROUP, head_count, HEAD_DIM)
    b_blocks = bc_conv[:, :STATE].reshape(block_count, GROUP, STATE)
    c_blocks = bc_conv[:, STATE:].reshape(block_count, GROUP, STATE)

    def state_of(item):
        x_group, b_group, steps_here, decay_here, segment, before = item
        return state_part(x_group, b_group, steps_here, decay_here, segment, before)

    def intra_of(item):
        x_group, b_group, c_group, steps_here, decay_here, segment = item
        return mixing_part(x_group, b_group, c_group, steps_here, decay_here, segment)

    block_states, transmits = blockwise(
        state_of, (x_blocks, b_blocks, step_blocks, cum_decay, seg_blocks, seg_before)
    )
    intra_items = (x_blocks, b_blocks, c_blocks, step_blocks, cum_decay, seg_blocks)
    ids = gather_rounds(ids, "ctx", 3, lax.axis_size("ctx").bit_length())
    ids, block_states = lax.optimization_barrier((ids, block_states))
    far = [*long_runs(ids, paired, tok_rows), intra_items]
    entering = chain_states(block_states, transmits, paired, far)
    y_intra = blockwise(intra_of, far[2])

    def enter_of(item):
        c_group, decay_here, segment, before, entering_here = item
        return entry_part(c_group, entering_here, decay_here, segment, before)

    y_state = blockwise(enter_of, (c_blocks, cum_decay, seg_blocks, seg_before, entering))
    y_blocks = y_intra + y_state
    x_heads = x_conv.reshape(tok_rows, head_count, HEAD_DIM).astype(jnp.float32)
    y_total = y_blocks.reshape(tok_rows, head_count, HEAD_DIM) + skip_d[None, :, None] * x_heads
    gated = y_total.reshape(tok_rows, channels) * jax.nn.silu(gate_z.astype(jnp.float32))
    local_sq = jnp.sum(gated * gated, axis=1)
    total_sq = lax.psum(local_sq, "tp")
    scale = lax.rsqrt(total_sq / INNER + epsilon)
    return scale_rows(gated, scale, norm_gain)


def cores_paired(mesh):
    row = mesh.devices[:, 0] if mesh.devices.ndim == 2 else mesh.devices.reshape(-1)
    if len(row) % 2:
        return False
    try:
        for lo, hi in zip(row[0::2], row[1::2]):
            if tuple(lo.coords) != tuple(hi.coords) or lo.core_on_chip == hi.core_on_chip:
                return False
    except AttributeError:
        return False
    return True


def solution(mesh):
    in_specs = (
        P("ctx", "tp"),
        P("ctx", "tp"),
        P("ctx", None),
        P("tp", "ctx"),
        P("tp"),
        P("tp"),
        P("tp"),
        P(None, "tp"),
        P("tp"),
        P(),
        P(),
        P("tp"),
        P("ctx"),
    )
    out_specs = P("ctx", "tp")
    paired = cores_paired(mesh)
    return jax.shard_map(functools.partial(local, paired), mesh=mesh, in_specs=in_specs, out_specs=out_specs, check_vma=False)
```
